512 devices in a mesh: seq: 256 (over z, y, x), head: 2 (over core).
Axes of the slice: x: 4, y: 4, z: 16, core: 2. Of those that a mesh axis runs over, the one named last changes fastest.
Arguments:
- queries: bfloat16 [131072, 1024], P('seq', 'head'), may hold values from -12 to 12
- key_states: bfloat16 [131072, 1024], P('seq', 'head'), may hold values from -5 to 5
- value_states: bfloat16 [131072, 1024], P('seq', 'head'), may hold values from -6 to 6
- out_grad: bfloat16 [131072, 1024], P('seq', 'head'), may hold values from -6 to 6
Outputs:
- normalized: bfloat16 [131072, 1024], P('seq', 'head')
- grad_queries: bfloat16 [131072, 1024], P('seq', 'head')
- grad_keys: bfloat16 [131072, 1024], P('seq', 'head')
- grad_values: bfloat16 [131072, 1024], P('seq', 'head')
The draws below stay inside these ranges and needn't reach their ends.
All inputs are finite; a program needn't handle non-finite values.
Results may differ from the reference program's by a relative error of at most 0.035.
Values may be sent and summed in bfloat16 or wider, within the bound.
No kernel may reach another device: no remote copies, remote signals or barrier semaphores. Data moves between devices by JAX's collectives and lax.ppermute only.
A program may use at most 64 MiB of HBM per device.

```python
from functools import reduce
import jax
import jax.numpy as jnp
from jax import lax

DH = 128
HEADS = 8
LEAF = 256
LEVELS = 3
TOKENS = 131072


def draw_queries(key, part):
    noise = jax.random.truncated_normal(jax.random.fold_in(key, 1), -4.0, 4.0, (TOKENS, HEADS * DH), jnp.float32)
    return noise.astype(jnp.bfloat16)


def draw_key_states(key, part):
    noise = jax.random.truncated_normal(jax.random.fold_in(key, 2), -4.0, 4.0, (TOKENS, HEADS * DH), jnp.float32)
    return noise.astype(jnp.bfloat16)


def draw_value_states(key, part):
    head_of = (jnp.arange(HEADS * DH) // DH).astype(jnp.float32) / (HEADS - 1)
    noise = jax.random.truncated_normal(jax.random.fold_in(key, 3), -4.0, 4.0, (TOKENS, HEADS * DH), jnp.float32)
    scaled = noise * (0.5 * 3.0 ** head_of)[None, :]
    return scaled.astype(jnp.bfloat16)


def levels(own_key, shape, cuts, least, largest):
    gain = 1.0
    for dim, shards_of in cuts:
        steps = jax.random.uniform(jax.random.fold_in(jax.random.fold_in(own_key, 6), dim), (shards_of,), jnp.float32, least / len(cuts), largest / len(cuts))
        gain = gain * jnp.repeat(jnp.exp(steps), shape[dim] // shards_of).reshape((-1,) + (1,) * (len(shape) - 1 - dim))
    return gain


def centred(own_key, extent, width, bound, shards=(), kind=jnp.bfloat16):
    loudness = levels(own_key, extent, shards, -0.22, 0.18) if shards else 1.0
    entries = jax.random.normal(own_key, extent, jnp.float32) * width * loudness
    return jnp.minimum(jnp.maximum(entries, -bound), bound).astype(kind)


def setup_inputs(seed: int = 0) -> dict:
    key_list = jax.random.split(jax.random.key(seed), 5)
    return {
        "queries": draw_queries(jax.random.fold_in(key_list[4], 71), 0),
        "key_states": draw_key_states(jax.random.fold_in(key_list[4], 71), 0),
        "value_states": draw_value_states(jax.random.fold_in(key_list[4], 71), 0),
        "out_grad": centred(key_list[3], (TOKENS, HEADS * DH), 1.0, 6.0, ((0, 256), (1, 2))),
    }


EPSILON = 1e-06

def halving(source):
    widened = source.astype(jnp.float32)
    paired = widened.reshape(widened.shape[:-2] + (widened.shape[-2] // 2, 2, widened.shape[-1]))
    return ((paired[..., 0, :] + paired[..., 1, :]) * 0.5).astype(jnp.bfloat16)

def query_view(tensor, level_num):
    flat_width = tensor.shape[-1]
    if level_num == 0:
        return tensor.reshape(-1, 2 * LEAF, flat_width)
    return tensor.reshape(-1, LEAF, flat_width)

def key_view(tensor, level_num):
    flat_width = tensor.shape[-1]
    if level_num == 0:
        return tensor.reshape(-1, 2 * LEAF, flat_width)
    return jnp.flip(tensor.reshape(-1, 2, LEAF, flat_width), 1).reshape(-1, LEAF, flat_width)

def key_rows(blocks, level_num):
    flat_width = blocks.shape[-1]
    if level_num == 0:
        return blocks.reshape(-1, flat_width)
    return jnp.flip(blocks.reshape(-1, 2, LEAF, flat_width), 1).reshape(-1, flat_width)

def coarse_all(tensor):
    result = [tensor]
    for level_num in range(1, LEVELS):
        result.append(halving(result[-1]))
    return result

def level_scores(coarse_query, coarse_key, level_num):
    query_blocks = query_view(coarse_query[level_num], level_num).astype(jnp.float32)
    key_blocks = key_view(coarse_key[level_num], level_num).astype(jnp.float32)
    scores = jnp.einsum('gqd,gkd->gqk', query_blocks, key_blocks) * DH ** (-0.5)
    maxima = scores.max(-1)
    exp_scores = jnp.exp(scores - maxima[..., None])
    return (query_blocks, key_blocks, maxima, exp_scores)

def head_attention(head_query, head_key, head_value):
    coarse_query = coarse_all(head_query)
    coarse_key = coarse_all(head_key)
    coarse_value = coarse_all(head_value)
    maxima_up, sums_up, weighted_up = ([], [], [])
    for level_num in range(LEVELS):
        stretch = 2 ** level_num
        query_blocks, key_blocks, maxima, exp_scores = level_scores(coarse_query, coarse_key, level_num)
        rounded = lax.optimization_barrier(exp_scores.astype(jnp.bfloat16)).astype(jnp.float32)
        value_blocks = key_view(coarse_value[level_num], level_num).astype(jnp.float32)
        weighted = jnp.einsum('gqk,gkd->gqd', rounded, value_blocks)
        maxima_up.append(jnp.repeat(maxima.reshape(-1), stretch, axis=0))
        sums_up.append(jnp.repeat(exp_scores.sum(-1).reshape(-1), stretch, axis=0))
        weighted_up.append(jnp.repeat(weighted.reshape(-1, DH), stretch, axis=0))
    highest = reduce(jnp.maximum, maxima_up)
    factors = [2.0 ** level_num * jnp.exp(maxima_up[level_num] - highest) for level_num in range(LEVELS)]
    denominator = factors[0] * sums_up[0]
    numerator = factors[0][:, None] * weighted_up[0]
    for level_num in range(1, LEVELS):
        denominator = denominator + factors[level_num] * sums_up[level_num]
        numerator = numerator + factors[level_num][:, None] * weighted_up[level_num]
    attended = (numerator / denominator[:, None]).astype(jnp.bfloat16)
    return (attended, factors, denominator)

def head_backward(head_query, head_key, head_value, head_grad):
    attended, factors, denominator = head_attention(head_query, head_key, head_value)
    coarse_query = coarse_all(head_query)
    coarse_key = coarse_all(head_key)
    coarse_value = coarse_all(head_value)
    attended_wide = attended.astype(jnp.float32)
    row_dots = lax.optimization_barrier(jnp.sum(head_grad * attended_wide, axis=-1))
    grad_total = jnp.zeros((3,) + head_query.shape, jnp.float32)
    for level_num in range(LEVELS):
        stretch = 2 ** level_num
        coarse_rows = head_query.shape[0] // stretch
        share_of = factors[level_num] / denominator
        gathered_grad = (share_of[:, None] * head_grad).reshape(coarse_rows, stretch, DH).sum(1)
        delta_rows = (share_of * row_dots).reshape(coarse_rows, stretch).sum(1)
        query_blocks, key_blocks, maxima, exp_scores = level_scores(coarse_query, coarse_key, level_num)
        rounded = lax.optimization_barrier(exp_scores.astype(jnp.bfloat16)).astype(jnp.float32)
        value_blocks = key_view(coarse_value[level_num], level_num).astype(jnp.float32)
        grad_rounded = lax.optimization_barrier(gathered_grad.astype(jnp.bfloat16)).astype(jnp.float32)
        grad_blocks = query_view(grad_rounded, level_num)
        delta_blocks = delta_rows.reshape(grad_blocks.shape[0], grad_blocks.shape[1])
        grad_scores = jnp.einsum('gqd,gkd->gqk', grad_blocks, value_blocks)
        grad_logits = (exp_scores * (grad_scores - delta_blocks[..., None])).astype(jnp.bfloat16)
        grad_logits = lax.optimization_barrier(grad_logits).astype(jnp.float32)
        grad_query = jnp.einsum('gqk,gkd->gqd', grad_logits, key_blocks) * DH ** (-0.5)
        grad_key = jnp.einsum('gqk,gqd->gkd', grad_logits, query_blocks) * DH ** (-0.5)
        grad_value = jnp.einsum('gqk,gqd->gkd', rounded, grad_blocks)
        level_grads = jnp.stack([grad_query.reshape(-1, DH), key_rows(grad_key, level_num), key_rows(grad_value, level_num)])
        grad_total = grad_total + jnp.repeat(level_grads, stretch, axis=1) * 0.5 ** level_num
    return grad_total

def reference(queries, key_states, value_states, out_grad):
    token_count, full_width = queries.shape
    head_count = full_width // DH

    def by_head(tensor):
        return tensor.reshape(token_count, head_count, DH).transpose(1, 0, 2)

    def forward_head(triple):
        return head_attention(triple[0], triple[1], triple[2])[0]
    attended = lax.map(forward_head, (by_head(queries), by_head(key_states), by_head(value_states)))
    attended = attended.transpose(1, 0, 2).reshape(token_count, full_width)
    attended_wide = attended.astype(jnp.float32)
    inverse = lax.rsqrt(lax.optimization_barrier(jnp.sum(attended_wide * attended_wide, axis=-1)) / full_width + EPSILON)
    normalized = (attended_wide * inverse[:, None]).astype(jnp.bfloat16)
    grad_wide = out_grad.astype(jnp.float32)
    dot_totals = lax.optimization_barrier(jnp.sum(grad_wide * attended_wide, axis=-1))
    grad_attended = inverse[:, None] * grad_wide - (inverse ** 3 * dot_totals / full_width)[:, None] * attended_wide

    def backward_head(quad):
        return head_backward(quad[0], quad[1], quad[2], quad[3])
    grads = lax.map(backward_head, (by_head(queries), by_head(key_states), by_head(value_states), by_head(grad_attended)))
    grads = grads.transpose(1, 2, 0, 3).reshape(3, token_count, full_width).astype(jnp.bfloat16)
    return (normalized, grads[0], grads[1], grads[2])
```

```python
import jax
import jax.numpy as jnp
from jax import lax
from jax.experimental import pallas as pl
from jax.experimental.pallas import tpu as pltpu
from jax.sharding import PartitionSpec as P

DH = 128
LEAF = 256
LEVELS = 3
EPSILON = 1e-06
SCALE = DH ** (-0.5)
F32 = jnp.float32
BF16 = jnp.bfloat16


def from_partner(value, mask):
    pairs = [(source, source ^ mask) for source in range(lax.axis_size("seq"))]
    return lax.ppermute(value, "seq", pairs)


def halving(source):
    widened = source.astype(F32)
    paired = widened.reshape(widened.shape[:-2] + (widened.shape[-2] // 2, 2, widened.shape[-1]))
    return ((paired[..., 0, :] + paired[..., 1, :]) * 0.5).astype(BF16)


def _nt(a, b):
    return lax.dot_general(a, b, (((1,), (1,)), ((), ())), preferred_element_type=F32)


def _nn(a, b):
    return lax.dot_general(a, b, (((1,), (0,)), ((), ())), preferred_element_type=F32)


def _tn(a, b):
    return lax.dot_general(a, b, (((0,), (0,)), ((), ())), preferred_element_type=F32)


def _lanes(shape):
    return lax.broadcasted_iota(jnp.int32, shape, len(shape) - 1)


def _fwd_kernel(q0, k0, v0, g0, q1, k1p, v1p, q2, k2a, v2a, k2b, v2b,
                att_ref, w_ref, sums_ref,
                a0s, m0s, s0s, a1s, m1s, s1s, a2s, m2s, s2s, atts, ws):
    h = pl.program_id(0)
    n0 = a0s.shape[0]
    n1 = a1s.shape[0]
    n2 = a2s.shape[0]

    def put(a_ref, m_ref, s_ref, a, m, s):
        a_ref[...] = a
        m_ref[...] = jnp.broadcast_to(m, a.shape)
        s_ref[...] = jnp.broadcast_to(s, a.shape)

    s = _nt(q0[...], k0[...]) * SCALE
    m = s.max(-1, keepdims=True)
    e = jnp.exp(s - m)
    put(a0s, m0s, s0s, _nn(e.astype(BF16), v0[...]), m, e.sum(-1, keepdims=True))

    s = _nt(q1[...], k1p[...]) * SCALE
    m = s.max(-1, keepdims=True)
    e = jnp.exp(s - m)
    put(a1s, m1s, s1s, _nn(e.astype(BF16), v1p[...]), m, e.sum(-1, keepdims=True))

    qv = q2[...]
    sa = _nt(qv, k2a[...]) * SCALE
    sb = _nt(qv, k2b[...]) * SCALE
    m = jnp.maximum(sa.max(-1, keepdims=True), sb.max(-1, keepdims=True))
    ea = jnp.exp(sa - m)
    eb = jnp.exp(sb - m)
    a = _nn(ea.astype(BF16), v2a[...]) + _nn(eb.astype(BF16), v2b[...])
    put(a2s, m2s, s2s, a, m, ea.sum(-1, keepdims=True) + eb.sum(-1, keepdims=True))

    lane = _lanes((n2, DH))
    for j in range(4):
        r0 = pl.ds(j, n2, stride=4)
        r1 = pl.ds(j >> 1, n2, stride=2)
        mm0 = m0s[r0, :]
        mm1 = m1s[r1, :]
        mm2 = m2s[...]
        top = jnp.maximum(jnp.maximum(mm0, mm1), mm2)
        f0 = jnp.exp(mm0 - top)
        f1 = 2.0 * jnp.exp(mm1 - top)
        f2 = 4.0 * jnp.exp(mm2 - top)
        den = f0 * s0s[r0, :] + f1 * s1s[r1, :] + f2 * s2s[...]
        num = f0 * a0s[r0, :] + f1 * a1s[r1, :] + f2 * a2s[...]
        atts[r0, :] = (num / den).astype(BF16).astype(F32)
        ws[r0, :] = jnp.where(
            lane == 0, f0 / den, jnp.where(lane == 1, f1 / den, jnp.where(lane == 2, f2 / den, 0.0))
        )
    attv = atts[...]
    att_ref[...] = attv.astype(BF16)
    w_ref[...] = ws[...]
    gf = g0[...].astype(F32)
    sq = (attv * attv).sum(-1, keepdims=True)
    dt = (gf * attv).sum(-1, keepdims=True)
    lane0 = _lanes((n0, DH))
    part = jnp.where(lane0 == 0, sq, jnp.where(lane0 == 1, dt, 0.0))

    @pl.when(h == 0)
    def _():
        sums_ref[...] = part

    @pl.when(h > 0)
    def _():
        sums_ref[...] += part


def _bwd_kernel(q0, k0, v0, g0, att, w, ic, q1, k1p, v1p, q2, k2a, v2a, k2b, v2b,
                norm_ref, gq_ref, dk0_ref, dv0_ref, g1_ref, d1_ref, g2_ref, d2_ref,
                t_s, u_s, dq0s, dq1s, dq2s, outs):
    n0 = t_s.shape[0]
    n1 = dq1s.shape[0]
    n2 = dq2s.shape[0]
    icv = ic[...]
    inv = icv[:, 0:1]
    coef = icv[:, 1:2]
    attv = att[...].astype(F32)
    norm_ref[...] = (attv * inv).astype(BF16)
    gf = g0[...].astype(F32)
    ga = inv * gf - coef * attv
    rt = (ga * attv).sum(-1, keepdims=True)
    wv = w[...]
    w0 = wv[:, 0:1]
    w1 = wv[:, 1:2]
    w2 = wv[:, 2:3]
    gl0 = (w0 * ga).astype(BF16)
    dl0 = w0 * rt

    t_s[...] = w1 * ga
    u_s[...] = jnp.broadcast_to(w1 * rt, (n0, DH))
    e_rows = pl.ds(0, n1, stride=2)
    o_rows = pl.ds(1, n1, stride=2)
    gl1 = (t_s[e_rows, :] + t_s[o_rows, :]).astype(BF16)
    dl1 = u_s[e_rows, :] + u_s[o_rows, :]

    t_s[...] = w2 * ga
    u_s[...] = jnp.broadcast_to(w2 * rt, (n0, DH))
    rows = [pl.ds(j, n2, stride=4) for j in range(4)]
    gl2 = (((t_s[rows[0], :] + t_s[rows[1], :]) + t_s[rows[2], :]) + t_s[rows[3], :]).astype(BF16)
    dl2 = ((u_s[rows[0], :] + u_s[rows[1], :]) + u_s[rows[2], :]) + u_s[rows[3], :]

    g1_ref[...] = gl1
    g2_ref[...] = gl2
    d1_ref[...] = dl1.T[0:1, :]
    d2_ref[...] = dl2.T[0:1, :]

    q0v = q0[...]
    k0v = k0[...]
    v0v = v0[...]
    s = _nt(q0v, k0v) * SCALE
    m = s.max(-1, keepdims=True)
    e = jnp.exp(s - m)
    p = e.astype(BF16)
    ds = (e * (_nt(gl0, v0v) - dl0)).astype(BF16)
    dq0s[...] = _nn(ds, k0v) * SCALE
    dk0_ref[...] = _tn(ds, q0v) * SCALE
    dv0_ref[...] = _tn(p, gl0)

    kv = k1p[...]
    s = _nt(q1[...], kv) * SCALE
    m = s.max(-1, keepdims=True)
    e = jnp.exp(s - m)
    ds = (e * (_nt(gl1, v1p[...]) - dl1[:, 0:1])).astype(BF16)
    dq1s[...] = _nn(ds, kv) * SCALE

    qv = q2[...]
    ka = k2a[...]
    kb = k2b[...]
    sa = _nt(qv, ka) * SCALE
    sb = _nt(qv, kb) * SCALE
    m = jnp.maximum(sa.max(-1, keepdims=True), sb.max(-1, keepdims=True))
    ea = jnp.exp(sa - m)
    eb = jnp.exp(sb - m)
    d2c = dl2[:, 0:1]
    dsa = (ea * (_nt(gl2, v2a[...]) - d2c)).astype(BF16)
    dsb = (eb * (_nt(gl2, v2b[...]) - d2c)).astype(BF16)
    dq2s[...] = (_nn(dsa, ka) + _nn(dsb, kb)) * SCALE

    for j in range(4):
        r1 = pl.ds(j >> 1, n2, stride=2)
        outs[rows[j], :] = dq0s[rows[j], :] + dq1s[r1, :] * 0.5 + dq2s[...] * 0.25
    gq_ref[...] = outs[...].astype(BF16)


def _own_kernel(k1o, v1o, q1p, g1p, d1p, k2o, v2o, k2s, q2a, g2a, d2a, q2b, g2b, d2b, dk0, dv0,
                gk_ref, gv_ref, dk1s, dv1s, dk2s, dv2s, outk, outv):
    n2 = dk2s.shape[0]
    qv = q1p[...]
    gv = g1p[...]
    st = _nt(k1o[...], qv) * SCALE
    m = st.max(0, keepdims=True)
    e = jnp.exp(st - m)
    p = e.astype(BF16)
    ds = (e * (_nt(v1o[...], gv) - d1p[...])).astype(BF16)
    dk1s[...] = _nn(ds, qv) * SCALE
    dv1s[...] = _nn(p, gv)

    ko = k2o[...]
    ks = k2s[...]
    vo = v2o[...]
    dks = []
    dvs = []
    for q_ref, g_ref, d_ref in ((q2a, g2a, d2a), (q2b, g2b, d2b)):
        qv = q_ref[...]
        gv = g_ref[...]
        so = _nt(ko, qv) * SCALE
        ss = _nt(ks, qv) * SCALE
        m = jnp.maximum(so.max(0, keepdims=True), ss.max(0, keepdims=True))
        e = jnp.exp(so - m)
        p = e.astype(BF16)
        ds = (e * (_nt(vo, gv) - d_ref[...])).astype(BF16)
        dks.append(_nn(ds, qv))
        dvs.append(_nn(p, gv))
    dk2s[...] = (dks[0] + dks[1]) * SCALE
    dv2s[...] = dvs[0] + dvs[1]

    for j in range(4):
        r0 = pl.ds(j, n2, stride=4)
        r1 = pl.ds(j >> 1, n2, stride=2)
        outk[r0, :] = dk0[r0, :] + dk1s[r1, :] * 0.5 + dk2s[...] * 0.25
        outv[r0, :] = dv0[r0, :] + dv1s[r1, :] * 0.5 + dv2s[...] * 0.25
    gk_ref[...] = outk[...].astype(BF16)
    gv_ref[...] = outv[...].astype(BF16)


def _cols(rows):
    return pl.BlockSpec((rows, DH), lambda h: (0, h))


def _stacked(rows, index):
    return pl.BlockSpec((None, rows, DH), lambda h: (index, 0, h))


def _per_head(rows, width):
    return pl.BlockSpec((None, rows, width), lambda h: (h, 0, 0))


def _whole(rows, width):
    return pl.BlockSpec((rows, width), lambda h: (0, 0))


def _params():
    return pltpu.CompilerParams(dimension_semantics=("arbitrary",))


def shards(queries, key_states, value_states, out_grad):
    n0, width = queries.shape
    heads = width // DH
    n1 = n0 // 2
    n2 = n0 // 4
    q0, k0, v0, g0 = queries, key_states, value_states, out_grad
    q1, k1, v1 = halving(q0), halving(k0), halving(v0)
    q2, k2, v2 = halving(q1), halving(k1), halving(v1)
    r1 = from_partner(jnp.stack([k1, v1, q1]), 1)
    send2 = jnp.stack([k2, v2, q2])
    r2a = from_partner(send2, 2)
    r2b = from_partner(send2, 3)

    att, w, sums = pl.pallas_call(
        _fwd_kernel,
        grid=(heads,),
        in_specs=[
            _cols(n0), _cols(n0), _cols(n0), _cols(n0),
            _cols(n1), _stacked(n1, 0), _stacked(n1, 1),
            _cols(n2), _stacked(n2, 0), _stacked(n2, 1), _stacked(n2, 0), _stacked(n2, 1),
        ],
        out_specs=[_cols(n0), _per_head(n0, DH), _whole(n0, DH)],
        out_shape=[
            jax.ShapeDtypeStruct((n0, width), BF16),
            jax.ShapeDtypeStruct((heads, n0, DH), F32),
            jax.ShapeDtypeStruct((n0, DH), F32),
        ],
        scratch_shapes=[pltpu.VMEM((n, DH), F32) for n in (n0, n0, n0, n1, n1, n1, n2, n2, n2, n0, n0)],
        compiler_params=_params(),
    )(q0, k0, v0, g0, q1, r1, r1, q2, r2a, r2a, r2b, r2b)

    full_width = width * lax.axis_size("head")
    totals = lax.psum(sums[:, :2], "head")
    inverse = lax.rsqrt(totals[:, 0] / full_width + EPSILON)
    coef = inverse**3 * totals[:, 1] / full_width
    ic = jnp.stack([inverse, coef], axis=1)

    norm, gq, dk0, dv0, gl1, dl1, gl2, dl2 = pl.pallas_call(
        _bwd_kernel,
        grid=(heads,),
        in_specs=[
            _cols(n0), _cols(n0), _cols(n0), _cols(n0), _cols(n0), _per_head(n0, DH), _whole(n0, 2),
            _cols(n1), _stacked(n1, 0), _stacked(n1, 1),
            _cols(n2), _stacked(n2, 0), _stacked(n2, 1), _stacked(n2, 0), _stacked(n2, 1),
        ],
        out_specs=[
            _cols(n0), _cols(n0), _cols(n0), _cols(n0),
            _cols(n1), _per_head(1, n1), _cols(n2), _per_head(1, n2),
        ],
        out_shape=[
            jax.ShapeDtypeStruct((n0, width), BF16),
            jax.ShapeDtypeStruct((n0, width), BF16),
            jax.ShapeDtypeStruct((n0, width), F32),
            jax.ShapeDtypeStruct((n0, width), F32),
            jax.ShapeDtypeStruct((n1, width), BF16),
            jax.ShapeDtypeStruct((heads, 1, n1), F32),
            jax.ShapeDtypeStruct((n2, width), BF16),
            jax.ShapeDtypeStruct((heads, 1, n2), F32),
        ],
        scratch_shapes=[pltpu.VMEM((n, DH), F32) for n in (n0, n0, n0, n1, n2, n0)],
        compiler_params=_params(),
    )(q0, k0, v0, g0, att, w, ic, q1, r1, r1, q2, r2a, r2a, r2b, r2b)

    g1p, d1p = from_partner((gl1, dl1), 1)
    g2a, d2a = from_partner((gl2, dl2), 2)
    g2b, d2b = from_partner((gl2, dl2), 3)
    k2s = halving(r1[0])

    gk, gv = pl.pallas_call(
        _own_kernel,
        grid=(heads,),
        in_specs=[
            _cols(n1), _cols(n1), _stacked(n1, 2), _cols(n1), _per_head(1, n1),
            _cols(n2), _cols(n2), _cols(n2),
            _stacked(n2, 2), _cols(n2), _per_head(1, n2),
            _stacked(n2, 2), _cols(n2), _per_head(1, n2),
            _cols(n0), _cols(n0),
        ],
        out_specs=[_cols(n0), _cols(n0)],
        out_shape=[
            jax.ShapeDtypeStruct((n0, width), BF16),
            jax.ShapeDtypeStruct((n0, width), BF16),
        ],
        scratch_shapes=[pltpu.VMEM((n, DH), F32) for n in (n1, n1, n2, n2, n0, n0)],
        compiler_params=_params(),
    )(k1, v1, r1, g1p, d1p, k2, v2, k2s, r2a, g2a, d2a, r2b, g2b, d2b, dk0, dv0)
    return (norm, gq, gk, gv)


def solution(mesh):
    return jax.shard_map(
        shards,
        mesh=mesh,
        in_specs=(P("seq", "head"), P("seq", "head"), P("seq", "head"), P("seq", "head")),
        out_specs=(P("seq", "head"), P("seq", "head"), P("seq", "head"), P("seq", "head")),
        check_vma=False,
    )
```

```python
import jax
import jax.numpy as jnp
from jax import lax
from jax.experimental import pallas as pl
from jax.experimental.pallas import tpu as pltpu
from jax.sharding import PartitionSpec as P

DH = 128
LEAF = 256
LEVELS = 3
EPSILON = 1e-06
SCALE = DH ** (-0.5)
F32 = jnp.float32
BF16 = jnp.bfloat16


def from_partner(value, mask):
    pairs = [(source, source ^ mask) for source in range(lax.axis_size("seq"))]
    return lax.ppermute(value, "seq", pairs)


def halving(source):
    widened = source.astype(F32)
    paired = widened.reshape(widened.shape[:-2] + (widened.shape[-2] // 2, 2, widened.shape[-1]))
    return ((paired[..., 0, :] + paired[..., 1, :]) * 0.5).astype(BF16)


def _nt(a, b):
    return lax.dot_general(a, b, (((1,), (1,)), ((), ())), preferred_element_type=F32)


def _nn(a, b):
    return lax.dot_general(a, b, (((1,), (0,)), ((), ())), preferred_element_type=F32)


def _tn(a, b):
    return lax.dot_general(a, b, (((0,), (0,)), ((), ())), preferred_element_type=F32)


def _lanes(shape):
    return lax.broadcasted_iota(jnp.int32, shape, len(shape) - 1)


def _halve_kernel(q0, k0, v0, s1_ref, s2_ref, wide, half):
    n1 = half.shape[0]
    n2 = n1 // 2
    for i, src in enumerate((k0, v0, q0)):
        wide[...] = src[...].astype(F32)
        h1 = ((wide[pl.ds(0, n1, stride=2), :] + wide[pl.ds(1, n1, stride=2), :]) * 0.5).astype(BF16)
        s1_ref[i] = h1
        half[...] = h1.astype(F32)
        h2 = ((half[pl.ds(0, n2, stride=2), :] + half[pl.ds(1, n2, stride=2), :]) * 0.5).astype(BF16)
        s2_ref[i] = h2


def _fwd0_kernel(q0, k0, v0, a0_ref, ms_ref):
    s = _nt(q0[...], k0[...]) * SCALE
    m = s.max(-1, keepdims=True)
    e = jnp.exp(s - m)
    a0_ref[...] = _nn(e.astype(BF16), v0[...])
    lane = _lanes(ms_ref.shape)
    ms_ref[...] = jnp.where(lane == 0, m, jnp.where(lane == 1, e.sum(-1, keepdims=True), 0.0))


def _fwd12_kernel(a0, ms0, g0, q1, k1p, v1p, q2, k2a, v2a, k2b, v2b,
                  att_ref, w_ref, sums_ref,
                  a1s, m1s, s1s, a2s, m2s, s2s, atts, ws):
    h = pl.program_id(0)
    n0 = atts.shape[0]
    n2 = a2s.shape[0]

    def put(a_ref, m_ref, s_ref, a, m, s):
        a_ref[...] = a
        m_ref[...] = jnp.broadcast_to(m, a.shape)
        s_ref[...] = jnp.broadcast_to(s, a.shape)

    s = _nt(q1[...], k1p[...]) * SCALE
    m = s.max(-1, keepdims=True)
    e = jnp.exp(s - m)
    put(a1s, m1s, s1s, _nn(e.astype(BF16), v1p[...]), m, e.sum(-1, keepdims=True))

    qv = q2[...]
    sa = _nt(qv, k2a[...]) * SCALE
    sb = _nt(qv, k2b[...]) * SCALE
    m = jnp.maximum(sa.max(-1, keepdims=True), sb.max(-1, keepdims=True))
    ea = jnp.exp(sa - m)
    eb = jnp.exp(sb - m)
    a = _nn(ea.astype(BF16), v2a[...]) + _nn(eb.astype(BF16), v2b[...])
    put(a2s, m2s, s2s, a, m, ea.sum(-1, keepdims=True) + eb.sum(-1, keepdims=True))

    lane = _lanes((n2, DH))
    for j in range(4):
        r0 = pl.ds(j, n2, stride=4)
        r1 = pl.ds(j >> 1, n2, stride=2)
        ms = ms0[r0, :]
        mm0 = ms[:, 0:1]
        mm1 = m1s[r1, :]
        mm2 = m2s[...]
        top = jnp.maximum(jnp.maximum(mm0, mm1), mm2)
        f0 = jnp.exp(mm0 - top)
        f1 = 2.0 * jnp.exp(mm1 - top)
        f2 = 4.0 * jnp.exp(mm2 - top)
        den = f0 * ms[:, 1:2] + f1 * s1s[r1, :] + f2 * s2s[...]
        num = f0 * a0[r0, :] + f1 * a1s[r1, :] + f2 * a2s[...]
        atts[r0, :] = (num / den).astype(BF16).astype(F32)
        ws[r0, :] = jnp.where(
            lane == 0, f0 / den, jnp.where(lane == 1, f1 / den, jnp.where(lane == 2, f2 / den, 0.0))
        )
    attv = atts[...]
    att_ref[...] = attv.astype(BF16)
    w_ref[...] = ws[...]
    gf = g0[...].astype(F32)
    sq = (attv * attv).sum(-1, keepdims=True)
    dt = (gf * attv).sum(-1, keepdims=True)
    lane0 = _lanes((n0, DH))
    part = jnp.where(lane0 == 0, sq, jnp.where(lane0 == 1, dt, 0.0))

    @pl.when(h == 0)
    def _():
        sums_ref[...] = part

    @pl.when(h > 0)
    def _():
        sums_ref[...] += part


def _level_grads(g0, att, w, ic, t_s, u_s):
    n0 = t_s.shape[0]
    n1 = n0 // 2
    n2 = n0 // 4
    icv = ic[...]
    inv = icv[:, 0:1]
    coef = icv[:, 1:2]
    attv = att[...].astype(F32)
    gf = g0[...].astype(F32)
    ga = inv * gf - coef * attv
    rt = (ga * attv).sum(-1, keepdims=True)
    wv = w[...]
    w0 = wv[:, 0:1]
    w1 = wv[:, 1:2]
    w2 = wv[:, 2:3]
    gl0 = (w0 * ga).astype(BF16)
    dl0 = w0 * rt
    t_s[...] = w1 * ga
    u_s[...] = jnp.broadcast_to(w1 * rt, (n0, DH))
    e_rows = pl.ds(0, n1, stride=2)
    o_rows = pl.ds(1, n1, stride=2)
    gl1 = (t_s[e_rows, :] + t_s[o_rows, :]).astype(BF16)
    dl1 = u_s[e_rows, :] + u_s[o_rows, :]
    t_s[...] = w2 * ga
    u_s[...] = jnp.broadcast_to(w2 * rt, (n0, DH))
    rows = [pl.ds(j, n2, stride=4) for j in range(4)]
    gl2 = (((t_s[rows[0], :] + t_s[rows[1], :]) + t_s[rows[2], :]) + t_s[rows[3], :]).astype(BF16)
    dl2 = ((u_s[rows[0], :] + u_s[rows[1], :]) + u_s[rows[2], :]) + u_s[rows[3], :]
    return inv, attv, gl0, dl0, gl1, dl1, gl2, dl2


def _split3(x):
    hi = x.astype(BF16).astype(F32)
    rest = x - hi
    mid = rest.astype(BF16).astype(F32)
    return hi, mid, rest - mid


def _coded(pieces):
    sub = lax.broadcasted_iota(jnp.int32, (16, DH), 0)
    out = jnp.zeros((16, DH), F32)
    for i, piece in enumerate(pieces):
        out = jnp.where(sub == i, piece, out)
    return out.astype(BF16)


def _bwd1_kernel(g0, att, w, ic, norm_ref, b1_ref, b2_ref, t_s, u_s):
    inv, attv, _, _, gl1, dl1, gl2, dl2 = _level_grads(g0, att, w, ic, t_s, u_s)
    n1 = gl1.shape[0]
    n2 = gl2.shape[0]
    norm_ref[...] = (attv * inv).astype(BF16)
    b1_ref[0:n1, :] = gl1
    b2_ref[0:n2, :] = gl2
    t1 = dl1.T
    a_parts = _split3(t1[0:1, 0:DH])
    b_parts = _split3(t1[0:1, DH:2 * DH])
    b1_ref[n1:n1 + 16, :] = _coded([a_parts[0], b_parts[0], a_parts[1], b_parts[1], a_parts[2], b_parts[2]])
    b2_ref[n2:n2 + 16, :] = _coded(list(_split3(dl2.T[0:1, :])))


def _bwd2_kernel(q0, k0, v0, g0, att, w, ic, q1, k1p, v1p, q2, k2a, v2a, k2b, v2b,
                 gq_ref, dk0_ref, dv0_ref,
                 t_s, u_s, dq0s, dq1s, dq2s, outs):
    n2 = dq2s.shape[0]
    _, _, gl0, dl0, gl1, dl1, gl2, dl2 = _level_grads(g0, att, w, ic, t_s, u_s)
    q0v = q0[...]
    k0v = k0[...]
    v0v = v0[...]
    s = _nt(q0v, k0v) * SCALE
    m = s.max(-1, keepdims=True)
    e = jnp.exp(s - m)
    p = e.astype(BF16)
    ds = (e * (_nt(gl0, v0v) - dl0)).astype(BF16)
    dq0s[...] = _nn(ds, k0v) * SCALE
    dk0_ref[...] = _tn(ds, q0v) * SCALE
    dv0_ref[...] = _tn(p, gl0)

    kv = k1p[...]
    s = _nt(q1[...], kv) * SCALE
    m = s.max(-1, keepdims=True)
    e = jnp.exp(s - m)
    ds = (e * (_nt(gl1, v1p[...]) - dl1[:, 0:1])).astype(BF16)
    dq1s[...] = _nn(ds, kv) * SCALE

    qv = q2[...]
    ka = k2a[...]
    kb = k2b[...]
    sa = _nt(qv, ka) * SCALE
    sb = _nt(qv, kb) * SCALE
    m = jnp.maximum(sa.max(-1, keepdims=True), sb.max(-1, keepdims=True))
    ea = jnp.exp(sa - m)
    eb = jnp.exp(sb - m)
    d2c = dl2[:, 0:1]
    dsa = (ea * (_nt(gl2, v2a[...]) - d2c)).astype(BF16)
    dsb = (eb * (_nt(gl2, v2b[...]) - d2c)).astype(BF16)
    dq2s[...] = (_nn(dsa, ka) + _nn(dsb, kb)) * SCALE

    for j in range(4):
        r0 = pl.ds(j, n2, stride=4)
        r1 = pl.ds(j >> 1, n2, stride=2)
        outs[r0, :] = dq0s[r0, :] + dq1s[r1, :] * 0.5 + dq2s[...] * 0.25
    gq_ref[...] = outs[...].astype(BF16)


def _own_kernel(k1o, v1o, q1p, k1p, b1p, k2o, v2o, q2a, b2a, q2b, b2b, dk0, dv0,
                gk_ref, gv_ref, wide, dk1s, dv1s, dk2s, dv2s, outk, outv):
    n1 = dk1s.shape[0]
    n2 = dk2s.shape[0]
    qv = q1p[...]
    gv = b1p[0:n1, :]
    x = b1p[n1:n1 + 16, :].astype(F32)
    d_row = jnp.concatenate([(x[0:1] + x[2:3]) + x[4:5], (x[1:2] + x[3:4]) + x[5:6]], axis=1)
    st = _nt(k1o[...], qv) * SCALE
    m = st.max(0, keepdims=True)
    e = jnp.exp(st - m)
    p = e.astype(BF16)
    ds = (e * (_nt(v1o[...], gv) - d_row)).astype(BF16)
    dk1s[...] = _nn(ds, qv) * SCALE
    dv1s[...] = _nn(p, gv)

    wide[...] = k1p[...].astype(F32)
    ks = ((wide[pl.ds(0, n2, stride=2), :] + wide[pl.ds(1, n2, stride=2), :]) * 0.5).astype(BF16)
    ko = k2o[...]
    vo = v2o[...]
    dks = []
    dvs = []
    for q_ref, b_ref in ((q2a, b2a), (q2b, b2b)):
        qv = q_ref[...]
        gv = b_ref[0:n2, :]
        x = b_ref[n2:n2 + 16, :].astype(F32)
        d_row = (x[0:1] + x[1:2]) + x[2:3]
        so = _nt(ko, qv) * SCALE
        ss = _nt(ks, qv) * SCALE
        m = jnp.maximum(so.max(0, keepdims=True), ss.max(0, keepdims=True))
        e = jnp.exp(so - m)
        p = e.astype(BF16)
        ds = (e * (_nt(vo, gv) - d_row)).astype(BF16)
        dks.append(_nn(ds, qv))
        dvs.append(_nn(p, gv))
    dk2s[...] = (dks[0] + dks[1]) * SCALE
    dv2s[...] = dvs[0] + dvs[1]

    for j in range(4):
        r0 = pl.ds(j, n2, stride=4)
        r1 = pl.ds(j >> 1, n2, stride=2)
        outk[r0, :] = dk0[r0, :] + dk1s[r1, :] * 0.5 + dk2s[...] * 0.25
        outv[r0, :] = dv0[r0, :] + dv1s[r1, :] * 0.5 + dv2s[...] * 0.25
    gk_ref[...] = outk[...].astype(BF16)
    gv_ref[...] = outv[...].astype(BF16)


def _cols(rows):
    return pl.BlockSpec((rows, DH), lambda h: (0, h))


def _stacked(rows, index):
    return pl.BlockSpec((None, rows, DH), lambda h: (index, 0, h))


def _per_head(rows, width):
    return pl.BlockSpec((None, rows, width), lambda h: (h, 0, 0))


def _whole(rows, width):
    return pl.BlockSpec((rows, width), lambda h: (0, 0))


def _params():
    return pltpu.CompilerParams(dimension_semantics=("arbitrary",))


def _three(rows):
    return pl.BlockSpec((3, rows, DH), lambda h: (0, 0, h))


def shards(queries, key_states, value_states, out_grad):
    n0, width = queries.shape
    heads = width // DH
    n1 = n0 // 2
    n2 = n0 // 4
    q0, k0, v0, g0 = queries, key_states, value_states, out_grad
    s1, s2 = pl.pallas_call(
        _halve_kernel,
        grid=(heads,),
        in_specs=[_cols(n0), _cols(n0), _cols(n0)],
        out_specs=[_three(n1), _three(n2)],
        out_shape=[
            jax.ShapeDtypeStruct((3, n1, width), BF16),
            jax.ShapeDtypeStruct((3, n2, width), BF16),
        ],
        scratch_shapes=[pltpu.VMEM((n0, DH), F32), pltpu.VMEM((n1, DH), F32)],
        compiler_params=_params(),
    )(q0, k0, v0)
    r1 = from_partner(s1, 1)
    r2a = from_partner(s2, 2)
    r2b = from_partner(s2, 3)

    a0, ms0 = pl.pallas_call(
        _fwd0_kernel,
        grid=(heads,),
        in_specs=[_cols(n0), _cols(n0), _cols(n0)],
        out_specs=[_cols(n0), _per_head(n0, DH)],
        out_shape=[
            jax.ShapeDtypeStruct((n0, width), F32),
            jax.ShapeDtypeStruct((heads, n0, DH), F32),
        ],
        compiler_params=_params(),
    )(q0, k0, v0)

    att, w, sums = pl.pallas_call(
        _fwd12_kernel,
        grid=(heads,),
        in_specs=[
            _cols(n0), _per_head(n0, DH), _cols(n0),
            _stacked(n1, 2), _stacked(n1, 0), _stacked(n1, 1),
            _stacked(n2, 2), _stacked(n2, 0), _stacked(n2, 1), _stacked(n2, 0), _stacked(n2, 1),
        ],
        out_specs=[_cols(n0), _per_head(n0, DH), _whole(n0, DH)],
        out_shape=[
            jax.ShapeDtypeStruct((n0, width), BF16),
            jax.ShapeDtypeStruct((heads, n0, DH), F32),
            jax.ShapeDtypeStruct((n0, DH), F32),
        ],
        scratch_shapes=[pltpu.VMEM((n, DH), F32) for n in (n1, n1, n1, n2, n2, n2, n0, n0)],
        compiler_params=_params(),
    )(a0, ms0, g0, s1, r1, r1, s2, r2a, r2a, r2b, r2b)

    full_width = width * lax.axis_size("head")
    totals = lax.psum(sums[:, :2], "head")
    inverse = lax.rsqrt(totals[:, 0] / full_width + EPSILON)
    coef = inverse**3 * totals[:, 1] / full_width
    ic = jnp.stack([inverse, coef], axis=1)

    norm, b1, b2 = pl.pallas_call(
        _bwd1_kernel,
        grid=(heads,),
        in_specs=[_cols(n0), _cols(n0), _per_head(n0, DH), _whole(n0, 2)],
        out_specs=[_cols(n0), _cols(n1 + 16), _cols(n2 + 16)],
        out_shape=[
            jax.ShapeDtypeStruct((n0, width), BF16),
            jax.ShapeDtypeStruct((n1 + 16, width), BF16),
            jax.ShapeDtypeStruct((n2 + 16, width), BF16),
        ],
        scratch_shapes=[pltpu.VMEM((n0, DH), F32), pltpu.VMEM((n0, DH), F32)],
        compiler_params=_params(),
    )(g0, att, w, ic)
    b1p = from_partner(b1, 1)
    b2a = from_partner(b2, 2)
    b2b = from_partner(b2, 3)

    gq, dk0, dv0 = pl.pallas_call(
        _bwd2_kernel,
        grid=(heads,),
        in_specs=[
            _cols(n0), _cols(n0), _cols(n0), _cols(n0), _cols(n0), _per_head(n0, DH), _whole(n0, 2),
            _stacked(n1, 2), _stacked(n1, 0), _stacked(n1, 1),
            _stacked(n2, 2), _stacked(n2, 0), _stacked(n2, 1), _stacked(n2, 0), _stacked(n2, 1),
        ],
        out_specs=[_cols(n0), _cols(n0), _cols(n0)],
        out_shape=[
            jax.ShapeDtypeStruct((n0, width), BF16),
            jax.ShapeDtypeStruct((n0, width), F32),
            jax.ShapeDtypeStruct((n0, width), F32),
        ],
        scratch_shapes=[pltpu.VMEM((n, DH), F32) for n in (n0, n0, n0, n1, n2, n0)],
        compiler_params=_params(),
    )(q0, k0, v0, g0, att, w, ic, s1, r1, r1, s2, r2a, r2a, r2b, r2b)

    gk, gv = pl.pallas_call(
        _own_kernel,
        grid=(heads,),
        in_specs=[
            _stacked(n1, 0), _stacked(n1, 1), _stacked(n1, 2), _stacked(n1, 0), _cols(n1 + 16),
            _stacked(n2, 0), _stacked(n2, 1),
            _stacked(n2, 2), _cols(n2 + 16),
            _stacked(n2, 2), _cols(n2 + 16),
            _cols(n0), _cols(n0),
        ],
        out_specs=[_cols(n0), _cols(n0)],
        out_shape=[
            jax.ShapeDtypeStruct((n0, width), BF16),
            jax.ShapeDtypeStruct((n0, width), BF16),
        ],
        scratch_shapes=[pltpu.VMEM((n, DH), F32) for n in (n1, n1, n1, n2, n2, n0, n0)],
        compiler_params=_params(),
    )(s1, s1, r1, r1, b1p, s2, s2, r2a, b2a, r2b, b2b, dk0, dv0)
    return (norm, gq, gk, gv)


def solution(mesh):
    return jax.shard_map(
        shards,
        mesh=mesh,
        in_specs=(P("seq", "head"), P("seq", "head"), P("seq", "head"), P("seq", "head")),
        out_specs=(P("seq", "head"), P("seq", "head"), P("seq", "head"), P("seq", "head")),
        check_vma=False,
    )
```

```python
import jax
import jax.numpy as jnp
from jax import lax
from jax.experimental import pallas as pl
from jax.experimental.pallas import tpu as pltpu
from jax.sharding import PartitionSpec as P

DH = 128
LEAF = 256
LEVELS = 3
EPSILON = 1e-06
SCALE = DH ** (-0.5)
F32 = jnp.float32
BF16 = jnp.bfloat16


def from_partner(value, mask):
    pairs = [(source, source ^ mask) for source in range(lax.axis_size("seq"))]
    return lax.ppermute(value, "seq", pairs)


def halving(source):
    widened = source.astype(F32)
    paired = widened.reshape(widened.shape[:-2] + (widened.shape[-2] // 2, 2, widened.shape[-1]))
    return ((paired[..., 0, :] + paired[..., 1, :]) * 0.5).astype(BF16)


def _nt(a, b):
    return lax.dot_general(a, b, (((1,), (1,)), ((), ())), preferred_element_type=F32)


def _nn(a, b):
    return lax.dot_general(a, b, (((1,), (0,)), ((), ())), preferred_element_type=F32)


def _tn(a, b):
    return lax.dot_general(a, b, (((0,), (0,)), ((), ())), preferred_element_type=F32)


def _lanes(shape):
    return lax.broadcasted_iota(jnp.int32, shape, len(shape) - 1)


def _halve_kernel(q0, k0, v0, s1_ref, q1_ref, s2_ref, q2_ref, wide, half):
    n1 = half.shape[0]
    n2 = n1 // 2
    for i, src in enumerate((k0, v0, q0)):
        wide[...] = src[...].astype(F32)
        h1 = ((wide[pl.ds(0, n1, stride=2), :] + wide[pl.ds(1, n1, stride=2), :]) * 0.5).astype(BF16)
        half[...] = h1.astype(F32)
        h2 = ((half[pl.ds(0, n2, stride=2), :] + half[pl.ds(1, n2, stride=2), :]) * 0.5).astype(BF16)
        if i < 2:
            s1_ref[i] = h1
            s2_ref[i] = h2
        else:
            q1_ref[...] = h1
            q2_ref[...] = h2


def _fwd0_kernel(q0, k0, v0, a0_ref, ms_ref):
    s = _nt(q0[...], k0[...]) * SCALE
    m = s.max(-1, keepdims=True)
    e = jnp.exp(s - m)
    a0_ref[...] = _nn(e.astype(BF16), v0[...])
    lane = _lanes(ms_ref.shape)
    ms_ref[...] = jnp.where(lane == 0, m, jnp.where(lane == 1, e.sum(-1, keepdims=True), 0.0))


def _fwd12_kernel(a0, ms0, g0, q1, k1p, v1p, q2, k2a, v2a, k2b, v2b,
                  att_ref, w_ref, sums_ref,
                  a1s, m1s, s1s, a2s, m2s, s2s, atts, ws):
    h = pl.program_id(0)
    n0 = atts.shape[0]
    n2 = a2s.shape[0]

    def put(a_ref, m_ref, s_ref, a, m, s):
        a_ref[...] = a
        m_ref[...] = jnp.broadcast_to(m, a.shape)
        s_ref[...] = jnp.broadcast_to(s, a.shape)

    s = _nt(q1[...], k1p[...]) * SCALE
    m = s.max(-1, keepdims=True)
    e = jnp.exp(s - m)
    put(a1s, m1s, s1s, _nn(e.astype(BF16), v1p[...]), m, e.sum(-1, keepdims=True))

    qv = q2[...]
    sa = _nt(qv, k2a[...]) * SCALE
    sb = _nt(qv, k2b[...]) * SCALE
    m = jnp.maximum(sa.max(-1, keepdims=True), sb.max(-1, keepdims=True))
    ea = jnp.exp(sa - m)
    eb = jnp.exp(sb - m)
    a = _nn(ea.astype(BF16), v2a[...]) + _nn(eb.astype(BF16), v2b[...])
    put(a2s, m2s, s2s, a, m, ea.sum(-1, keepdims=True) + eb.sum(-1, keepdims=True))

    lane = _lanes((n2, DH))
    for j in range(4):
        r0 = pl.ds(j, n2, stride=4)
        r1 = pl.ds(j >> 1, n2, stride=2)
        ms = ms0[r0, :]
        mm0 = ms[:, 0:1]
        mm1 = m1s[r1, :]
        mm2 = m2s[...]
        top = jnp.maximum(jnp.maximum(mm0, mm1), mm2)
        f0 = jnp.exp(mm0 - top)
        f1 = 2.0 * jnp.exp(mm1 - top)
        f2 = 4.0 * jnp.exp(mm2 - top)
        den = f0 * ms[:, 1:2] + f1 * s1s[r1, :] + f2 * s2s[...]
        num = f0 * a0[r0, :] + f1 * a1s[r1, :] + f2 * a2s[...]
        atts[r0, :] = (num / den).astype(BF16).astype(F32)
        ws[r0, :] = jnp.where(
            lane == 0, f0 / den, jnp.where(lane == 1, f1 / den, jnp.where(lane == 2, f2 / den, 0.0))
        )
    attv = atts[...]
    att_ref[...] = attv.astype(BF16)
    w_ref[...] = ws[...]
    gf = g0[...].astype(F32)
    sq = (attv * attv).sum(-1, keepdims=True)
    dt = (gf * attv).sum(-1, keepdims=True)
    lane0 = _lanes((n0, DH))
    part = jnp.where(lane0 == 0, sq, jnp.where(lane0 == 1, dt, 0.0))

    @pl.when(h == 0)
    def _():
        sums_ref[...] = part

    @pl.when(h > 0)
    def _():
        sums_ref[...] += part


def _level_grads(g0, att, w, ic, t_s, u_s):
    n0 = t_s.shape[0]
    n1 = n0 // 2
    n2 = n0 // 4
    icv = ic[...]
    inv = icv[:, 0:1]
    coef = icv[:, 1:2]
    attv = att[...].astype(F32)
    gf = g0[...].astype(F32)
    ga = inv * gf - coef * attv
    rt = (ga * attv).sum(-1, keepdims=True)
    wv = w[...]
    w0 = wv[:, 0:1]
    w1 = wv[:, 1:2]
    w2 = wv[:, 2:3]
    gl0 = (w0 * ga).astype(BF16)
    dl0 = w0 * rt
    t_s[...] = w1 * ga
    u_s[...] = jnp.broadcast_to(w1 * rt, (n0, DH))
    e_rows = pl.ds(0, n1, stride=2)
    o_rows = pl.ds(1, n1, stride=2)
    gl1 = (t_s[e_rows, :] + t_s[o_rows, :]).astype(BF16)
    dl1 = u_s[e_rows, :] + u_s[o_rows, :]
    t_s[...] = w2 * ga
    u_s[...] = jnp.broadcast_to(w2 * rt, (n0, DH))
    rows = [pl.ds(j, n2, stride=4) for j in range(4)]
    gl2 = (((t_s[rows[0], :] + t_s[rows[1], :]) + t_s[rows[2], :]) + t_s[rows[3], :]).astype(BF16)
    dl2 = ((u_s[rows[0], :] + u_s[rows[1], :]) + u_s[rows[2], :]) + u_s[rows[3], :]
    return inv, attv, gl0, dl0, gl1, dl1, gl2, dl2


def _split3(x):
    hi = x.astype(BF16).astype(F32)
    rest = x - hi
    mid = rest.astype(BF16).astype(F32)
    return hi, mid, rest - mid


def _coded(pieces):
    sub = lax.broadcasted_iota(jnp.int32, (16, DH), 0)
    out = jnp.zeros((16, DH), F32)
    for i, piece in enumerate(pieces):
        out = jnp.where(sub == i, piece, out)
    return out.astype(BF16)


def _bwd1_kernel(g0, att, w, ic, q1, q2, norm_ref, b1_ref, b2_ref, t_s, u_s):
    inv, attv, _, _, gl1, dl1, gl2, dl2 = _level_grads(g0, att, w, ic, t_s, u_s)
    n1 = gl1.shape[0]
    n2 = gl2.shape[0]
    norm_ref[...] = (attv * inv).astype(BF16)
    b1_ref[0:n1, :] = gl1
    b2_ref[0:n2, :] = gl2
    t1 = dl1.T
    a_parts = _split3(t1[0:1, 0:DH])
    b_parts = _split3(t1[0:1, DH:2 * DH])
    b1_ref[n1:n1 + 16, :] = _coded([a_parts[0], b_parts[0], a_parts[1], b_parts[1], a_parts[2], b_parts[2]])
    b2_ref[n2:n2 + 16, :] = _coded(list(_split3(dl2.T[0:1, :])))
    b1_ref[n1 + 16:, :] = q1[...]
    b2_ref[n2 + 16:, :] = q2[...]


def _bwd2_kernel(q0, k0, v0, g0, att, w, ic, q1, k1p, v1p, q2, k2a, v2a, k2b, v2b,
                 gq_ref, dk0_ref, dv0_ref,
                 t_s, u_s, dq0s, dq1s, dq2s, outs):
    n2 = dq2s.shape[0]
    _, _, gl0, dl0, gl1, dl1, gl2, dl2 = _level_grads(g0, att, w, ic, t_s, u_s)
    q0v = q0[...]
    k0v = k0[...]
    v0v = v0[...]
    s = _nt(q0v, k0v) * SCALE
    m = s.max(-1, keepdims=True)
    e = jnp.exp(s - m)
    p = e.astype(BF16)
    ds = (e * (_nt(gl0, v0v) - dl0)).astype(BF16)
    dq0s[...] = _nn(ds, k0v) * SCALE
    dk0_ref[...] = _tn(ds, q0v) * SCALE
    dv0_ref[...] = _tn(p, gl0)

    kv = k1p[...]
    s = _nt(q1[...], kv) * SCALE
    m = s.max(-1, keepdims=True)
    e = jnp.exp(s - m)
    ds = (e * (_nt(gl1, v1p[...]) - dl1[:, 0:1])).astype(BF16)
    dq1s[...] = _nn(ds, kv) * SCALE

    qv = q2[...]
    ka = k2a[...]
    kb = k2b[...]
    sa = _nt(qv, ka) * SCALE
    sb = _nt(qv, kb) * SCALE
    m = jnp.maximum(sa.max(-1, keepdims=True), sb.max(-1, keepdims=True))
    ea = jnp.exp(sa - m)
    eb = jnp.exp(sb - m)
    d2c = dl2[:, 0:1]
    dsa = (ea * (_nt(gl2, v2a[...]) - d2c)).astype(BF16)
    dsb = (eb * (_nt(gl2, v2b[...]) - d2c)).astype(BF16)
    dq2s[...] = (_nn(dsa, ka) + _nn(dsb, kb)) * SCALE

    for j in range(4):
        r0 = pl.ds(j, n2, stride=4)
        r1 = pl.ds(j >> 1, n2, stride=2)
        outs[r0, :] = dq0s[r0, :] + dq1s[r1, :] * 0.5 + dq2s[...] * 0.25
    gq_ref[...] = outs[...].astype(BF16)


def _own_kernel(k1o, v1o, k1p, b1p, k2o, v2o, b2a, b2b, dk0, dv0,
                gk_ref, gv_ref, wide, dk1s, dv1s, dk2s, dv2s, outk, outv):
    n1 = dk1s.shape[0]
    n2 = dk2s.shape[0]
    qv = b1p[n1 + 16:, :]
    gv = b1p[0:n1, :]
    x = b1p[n1:n1 + 16, :].astype(F32)
    d_row = jnp.concatenate([(x[0:1] + x[2:3]) + x[4:5], (x[1:2] + x[3:4]) + x[5:6]], axis=1)
    st = _nt(k1o[...], qv) * SCALE
    m = st.max(0, keepdims=True)
    e = jnp.exp(st - m)
    p = e.astype(BF16)
    ds = (e * (_nt(v1o[...], gv) - d_row)).astype(BF16)
    dk1s[...] = _nn(ds, qv) * SCALE
    dv1s[...] = _nn(p, gv)

    wide[...] = k1p[...].astype(F32)
    ks = ((wide[pl.ds(0, n2, stride=2), :] + wide[pl.ds(1, n2, stride=2), :]) * 0.5).astype(BF16)
    ko = k2o[...]
    vo = v2o[...]
    dks = []
    dvs = []
    for b_ref in (b2a, b2b):
        qv = b_ref[n2 + 16:, :]
        gv = b_ref[0:n2, :]
        x = b_ref[n2:n2 + 16, :].astype(F32)
        d_row = (x[0:1] + x[1:2]) + x[2:3]
        so = _nt(ko, qv) * SCALE
        ss = _nt(ks, qv) * SCALE
        m = jnp.maximum(so.max(0, keepdims=True), ss.max(0, keepdims=True))
        e = jnp.exp(so - m)
        p = e.astype(BF16)
        ds = (e * (_nt(vo, gv) - d_row)).astype(BF16)
        dks.append(_nn(ds, qv))
        dvs.append(_nn(p, gv))
    dk2s[...] = (dks[0] + dks[1]) * SCALE
    dv2s[...] = dvs[0] + dvs[1]

    for j in range(4):
        r0 = pl.ds(j, n2, stride=4)
        r1 = pl.ds(j >> 1, n2, stride=2)
        outk[r0, :] = dk0[r0, :] + dk1s[r1, :] * 0.5 + dk2s[...] * 0.25
        outv[r0, :] = dv0[r0, :] + dv1s[r1, :] * 0.5 + dv2s[...] * 0.25
    gk_ref[...] = outk[...].astype(BF16)
    gv_ref[...] = outv[...].astype(BF16)


def _cols(rows):
    return pl.BlockSpec((rows, DH), lambda h: (0, h))


def _stacked(rows, index):
    return pl.BlockSpec((None, rows, DH), lambda h: (index, 0, h))


def _per_head(rows, width):
    return pl.BlockSpec((None, rows, width), lambda h: (h, 0, 0))


def _whole(rows, width):
    return pl.BlockSpec((rows, width), lambda h: (0, 0))


def _params():
    return pltpu.CompilerParams(dimension_semantics=("arbitrary",))


def _two(rows):
    return pl.BlockSpec((2, rows, DH), lambda h: (0, 0, h))


def shards(queries, key_states, value_states, out_grad):
    n0, width = queries.shape
    heads = width // DH
    n1 = n0 // 2
    n2 = n0 // 4
    q0, k0, v0, g0 = queries, key_states, value_states, out_grad
    s1, q1, s2, q2 = pl.pallas_call(
        _halve_kernel,
        grid=(heads,),
        in_specs=[_cols(n0), _cols(n0), _cols(n0)],
        out_specs=[_two(n1), _cols(n1), _two(n2), _cols(n2)],
        out_shape=[
            jax.ShapeDtypeStruct((2, n1, width), BF16),
            jax.ShapeDtypeStruct((n1, width), BF16),
            jax.ShapeDtypeStruct((2, n2, width), BF16),
            jax.ShapeDtypeStruct((n2, width), BF16),
        ],
        scratch_shapes=[pltpu.VMEM((n0, DH), F32), pltpu.VMEM((n1, DH), F32)],
        compiler_params=_params(),
    )(q0, k0, v0)
    r1 = from_partner(s1, 1)
    r2a = from_partner(s2, 2)
    r2b = from_partner(s2, 3)

    a0, ms0 = pl.pallas_call(
        _fwd0_kernel,
        grid=(heads,),
        in_specs=[_cols(n0), _cols(n0), _cols(n0)],
        out_specs=[_cols(n0), _per_head(n0, DH)],
        out_shape=[
            jax.ShapeDtypeStruct((n0, width), F32),
            jax.ShapeDtypeStruct((heads, n0, DH), F32),
        ],
        compiler_params=_params(),
    )(q0, k0, v0)

    att, w, sums = pl.pallas_call(
        _fwd12_kernel,
        grid=(heads,),
        in_specs=[
            _cols(n0), _per_head(n0, DH), _cols(n0),
            _cols(n1), _stacked(n1, 0), _stacked(n1, 1),
            _cols(n2), _stacked(n2, 0), _stacked(n2, 1), _stacked(n2, 0), _stacked(n2, 1),
        ],
        out_specs=[_cols(n0), _per_head(n0, DH), _whole(n0, DH)],
        out_shape=[
            jax.ShapeDtypeStruct((n0, width), BF16),
            jax.ShapeDtypeStruct((heads, n0, DH), F32),
            jax.ShapeDtypeStruct((n0, DH), F32),
        ],
        scratch_shapes=[pltpu.VMEM((n, DH), F32) for n in (n1, n1, n1, n2, n2, n2, n0, n0)],
        compiler_params=_params(),
    )(a0, ms0, g0, q1, r1, r1, q2, r2a, r2a, r2b, r2b)

    full_width = width * lax.axis_size("head")
    totals = lax.psum(sums[:, :2], "head")
    inverse = lax.rsqrt(totals[:, 0] / full_width + EPSILON)
    coef = inverse**3 * totals[:, 1] / full_width
    ic = jnp.stack([inverse, coef], axis=1)

    norm, b1, b2 = pl.pallas_call(
        _bwd1_kernel,
        grid=(heads,),
        in_specs=[_cols(n0), _cols(n0), _per_head(n0, DH), _whole(n0, 2), _cols(n1), _cols(n2)],
        out_specs=[_cols(n0), _cols(2 * n1 + 16), _cols(2 * n2 + 16)],
        out_shape=[
            jax.ShapeDtypeStruct((n0, width), BF16),
            jax.ShapeDtypeStruct((2 * n1 + 16, width), BF16),
            jax.ShapeDtypeStruct((2 * n2 + 16, width), BF16),
        ],
        scratch_shapes=[pltpu.VMEM((n0, DH), F32), pltpu.VMEM((n0, DH), F32)],
        compiler_params=_params(),
    )(g0, att, w, ic, q1, q2)
    b1p = from_partner(b1, 1)
    b2a = from_partner(b2, 2)
    b2b = from_partner(b2, 3)

    gq, dk0, dv0 = pl.pallas_call(
        _bwd2_kernel,
        grid=(heads,),
        in_specs=[
            _cols(n0), _cols(n0), _cols(n0), _cols(n0), _cols(n0), _per_head(n0, DH), _whole(n0, 2),
            _cols(n1), _stacked(n1, 0), _stacked(n1, 1),
            _cols(n2), _stacked(n2, 0), _stacked(n2, 1), _stacked(n2, 0), _stacked(n2, 1),
        ],
        out_specs=[_cols(n0), _cols(n0), _cols(n0)],
        out_shape=[
            jax.ShapeDtypeStruct((n0, width), BF16),
            jax.ShapeDtypeStruct((n0, width), F32),
            jax.ShapeDtypeStruct((n0, width), F32),
        ],
        scratch_shapes=[pltpu.VMEM((n, DH), F32) for n in (n0, n0, n0, n1, n2, n0)],
        compiler_params=_params(),
    )(q0, k0, v0, g0, att, w, ic, q1, r1, r1, q2, r2a, r2a, r2b, r2b)

    gk, gv = pl.pallas_call(
        _own_kernel,
        grid=(heads,),
        in_specs=[
            _stacked(n1, 0), _stacked(n1, 1), _stacked(n1, 0), _cols(2 * n1 + 16),
            _stacked(n2, 0), _stacked(n2, 1), _cols(2 * n2 + 16), _cols(2 * n2 + 16),
            _cols(n0), _cols(n0),
        ],
        out_specs=[_cols(n0), _cols(n0)],
        out_shape=[
            jax.ShapeDtypeStruct((n0, width), BF16),
            jax.ShapeDtypeStruct((n0, width), BF16),
        ],
        scratch_shapes=[pltpu.VMEM((n, DH), F32) for n in (n1, n1, n1, n2, n2, n0, n0)],
        compiler_params=_params(),
    )(s1, s1, r1, b1p, s2, s2, b2a, b2b, dk0, dv0)
    return (norm, gq, gk, gv)


def solution(mesh):
    return jax.shard_map(
        shards,
        mesh=mesh,
        in_specs=(P("seq", "head"), P("seq", "head"), P("seq", "head"), P("seq", "head")),
        out_specs=(P("seq", "head"), P("seq", "head"), P("seq", "head"), P("seq", "head")),
        check_vma=False,
    )
```

```python
import jax
import jax.numpy as jnp
from jax import lax
from jax.experimental import pallas as pl
from jax.experimental.pallas import tpu as pltpu
from jax.sharding import PartitionSpec as P

DH = 128
LEAF = 256
LEVELS = 3
EPSILON = 1e-06
SCALE = DH ** (-0.5)
F32 = jnp.float32
BF16 = jnp.bfloat16


def from_partner(value, mask):
    pairs = [(source, source ^ mask) for source in range(lax.axis_size("seq"))]
    return lax.ppermute(value, "seq", pairs)


def halving(source):
    widened = source.astype(F32)
    paired = widened.reshape(widened.shape[:-2] + (widened.shape[-2] // 2, 2, widened.shape[-1]))
    return ((paired[..., 0, :] + paired[..., 1, :]) * 0.5).astype(BF16)


def _nt(a, b):
    return lax.dot_general(a, b, (((1,), (1,)), ((), ())), preferred_element_type=F32)


def _nn(a, b):
    return lax.dot_general(a, b, (((1,), (0,)), ((), ())), preferred_element_type=F32)


def _tn(a, b):
    return lax.dot_general(a, b, (((0,), (0,)), ((), ())), preferred_element_type=F32)


def _lanes(shape):
    return lax.broadcasted_iota(jnp.int32, shape, len(shape) - 1)


def _halve_kernel(q0, k0, v0, s1_ref, q1_ref, s2_ref, q2_ref, wide, half):
    n1 = half.shape[0]
    n2 = n1 // 2
    for i, src in enumerate((k0, v0, q0)):
        wide[...] = src[...].astype(F32)
        h1 = ((wide[pl.ds(0, n1, stride=2), :] + wide[pl.ds(1, n1, stride=2), :]) * 0.5).astype(BF16)
        half[...] = h1.astype(F32)
        h2 = ((half[pl.ds(0, n2, stride=2), :] + half[pl.ds(1, n2, stride=2), :]) * 0.5).astype(BF16)
        if i < 2:
            s1_ref[i] = h1
            s2_ref[i] = h2
        else:
            q1_ref[...] = h1
            q2_ref[...] = h2


def _fwd0_kernel(q0, k0, v0, a0_ref, ms_ref):
    s = _nt(q0[...], k0[...]) * SCALE
    m = s.max(-1, keepdims=True)
    e = jnp.exp(s - m)
    a0_ref[...] = _nn(e.astype(BF16), v0[...])
    lane = _lanes(ms_ref.shape)
    ms_ref[...] = jnp.where(lane == 0, m, jnp.where(lane == 1, e.sum(-1, keepdims=True), 0.0))


def _fwd12_kernel(a0, ms0, g0, q1, k1p, v1p, q2, k2a, v2a, k2b, v2b,
                  att_ref, w_ref, sums_ref,
                  a1s, m1s, s1s, a2s, m2s, s2s, atts, ws):
    h = pl.program_id(0)
    n0 = atts.shape[0]
    n2 = a2s.shape[0]

    def put(a_ref, m_ref, s_ref, a, m, s):
        a_ref[...] = a
        m_ref[...] = jnp.broadcast_to(m, a.shape)
        s_ref[...] = jnp.broadcast_to(s, a.shape)

    s = _nt(q1[...], k1p[...]) * SCALE
    m = s.max(-1, keepdims=True)
    e = jnp.exp(s - m)
    put(a1s, m1s, s1s, _nn(e.astype(BF16), v1p[...]), m, e.sum(-1, keepdims=True))

    qv = q2[...]
    sa = _nt(qv, k2a[...]) * SCALE
    sb = _nt(qv, k2b[...]) * SCALE
    m = jnp.maximum(sa.max(-1, keepdims=True), sb.max(-1, keepdims=True))
    ea = jnp.exp(sa - m)
    eb = jnp.exp(sb - m)
    a = _nn(ea.astype(BF16), v2a[...]) + _nn(eb.astype(BF16), v2b[...])
    put(a2s, m2s, s2s, a, m, ea.sum(-1, keepdims=True) + eb.sum(-1, keepdims=True))

    lane = _lanes((n2, DH))
    for j in range(4):
        r0 = pl.ds(j, n2, stride=4)
        r1 = pl.ds(j >> 1, n2, stride=2)
        ms = ms0[r0, :]
        mm0 = ms[:, 0:1]
        mm1 = m1s[r1, :]
        mm2 = m2s[...]
        top = jnp.maximum(jnp.maximum(mm0, mm1), mm2)
        f0 = jnp.exp(mm0 - top)
        f1 = 2.0 * jnp.exp(mm1 - top)
        f2 = 4.0 * jnp.exp(mm2 - top)
        den = f0 * ms[:, 1:2] + f1 * s1s[r1, :] + f2 * s2s[...]
        num = f0 * a0[r0, :] + f1 * a1s[r1, :] + f2 * a2s[...]
        atts[r0, :] = (num / den).astype(BF16).astype(F32)
        ws[r0, :] = jnp.where(
            lane == 0, f0 / den, jnp.where(lane == 1, f1 / den, jnp.where(lane == 2, f2 / den, 0.0))
        )
    attv = atts[...]
    att_ref[...] = attv.astype(BF16)
    w_ref[...] = ws[...]
    gf = g0[...].astype(F32)
    sq = (attv * attv).sum(-1, keepdims=True)
    dt = (gf * attv).sum(-1, keepdims=True)
    lane0 = _lanes((n0, DH))
    part = jnp.where(lane0 == 0, sq, jnp.where(lane0 == 1, dt, 0.0))

    @pl.when(h == 0)
    def _():
        sums_ref[...] = part

    @pl.when(h > 0)
    def _():
        sums_ref[...] += part


def _level_grads(g0, att, w, mine, theirs, t_s, u_s):
    n0 = t_s.shape[0]
    n1 = n0 // 2
    n2 = n0 // 4
    full_width = 2 * 4 * DH
    totals = mine[:, 0:2] + theirs[:, 0:2]
    inv = lax.rsqrt(totals[:, 0:1] / full_width + EPSILON)
    coef = inv * inv * inv * totals[:, 1:2] / full_width
    attv = att[...].astype(F32)
    gf = g0[...].astype(F32)
    ga = inv * gf - coef * attv
    rt = (ga * attv).sum(-1, keepdims=True)
    wv = w[...]
    w0 = wv[:, 0:1]
    w1 = wv[:, 1:2]
    w2 = wv[:, 2:3]
    gl0 = (w0 * ga).astype(BF16)
    dl0 = w0 * rt
    t_s[...] = w1 * ga
    u_s[...] = jnp.broadcast_to(w1 * rt, (n0, DH))
    e_rows = pl.ds(0, n1, stride=2)
    o_rows = pl.ds(1, n1, stride=2)
    gl1 = (t_s[e_rows, :] + t_s[o_rows, :]).astype(BF16)
    dl1 = u_s[e_rows, :] + u_s[o_rows, :]
    t_s[...] = w2 * ga
    u_s[...] = jnp.broadcast_to(w2 * rt, (n0, DH))
    rows = [pl.ds(j, n2, stride=4) for j in range(4)]
    gl2 = (((t_s[rows[0], :] + t_s[rows[1], :]) + t_s[rows[2], :]) + t_s[rows[3], :]).astype(BF16)
    dl2 = ((u_s[rows[0], :] + u_s[rows[1], :]) + u_s[rows[2], :]) + u_s[rows[3], :]
    return inv, attv, gl0, dl0, gl1, dl1, gl2, dl2


def _split3(x):
    hi = x.astype(BF16).astype(F32)
    rest = x - hi
    mid = rest.astype(BF16).astype(F32)
    return hi, mid, rest - mid


def _coded(pieces):
    sub = lax.broadcasted_iota(jnp.int32, (16, DH), 0)
    out = jnp.zeros((16, DH), F32)
    for i, piece in enumerate(pieces):
        out = jnp.where(sub == i, piece, out)
    return out.astype(BF16)


def _bwd1_kernel(g0, att, w, mine, theirs, q1, q2, norm_ref, b1_ref, b2_ref, t_s, u_s):
    inv, attv, _, _, gl1, dl1, gl2, dl2 = _level_grads(g0, att, w, mine, theirs, t_s, u_s)
    n1 = gl1.shape[0]
    n2 = gl2.shape[0]
    norm_ref[...] = (attv * inv).astype(BF16)
    b1_ref[0:n1, :] = gl1
    b2_ref[0:n2, :] = gl2
    t1 = dl1.T
    a_parts = _split3(t1[0:1, 0:DH])
    b_parts = _split3(t1[0:1, DH:2 * DH])
    b1_ref[n1:n1 + 16, :] = _coded([a_parts[0], b_parts[0], a_parts[1], b_parts[1], a_parts[2], b_parts[2]])
    b2_ref[n2:n2 + 16, :] = _coded(list(_split3(dl2.T[0:1, :])))
    b1_ref[n1 + 16:, :] = q1[...]
    b2_ref[n2 + 16:, :] = q2[...]


def _bwd2_kernel(q0, k0, v0, g0, att, w, mine, theirs, q1, k1p, v1p, q2, k2a, v2a, k2b, v2b,
                 gq_ref, dk0_ref, dv0_ref,
                 t_s, u_s, dq0s, dq1s, dq2s, outs):
    n2 = dq2s.shape[0]
    _, _, gl0, dl0, gl1, dl1, gl2, dl2 = _level_grads(g0, att, w, mine, theirs, t_s, u_s)
    q0v = q0[...]
    k0v = k0[...]
    v0v = v0[...]
    s = _nt(q0v, k0v) * SCALE
    m = s.max(-1, keepdims=True)
    e = jnp.exp(s - m)
    p = e.astype(BF16)
    ds = (e * (_nt(gl0, v0v) - dl0)).astype(BF16)
    dq0s[...] = _nn(ds, k0v) * SCALE
    dk0_ref[...] = _tn(ds, q0v) * SCALE
    dv0_ref[...] = _tn(p, gl0)

    kv = k1p[...]
    s = _nt(q1[...], kv) * SCALE
    m = s.max(-1, keepdims=True)
    e = jnp.exp(s - m)
    ds = (e * (_nt(gl1, v1p[...]) - dl1[:, 0:1])).astype(BF16)
    dq1s[...] = _nn(ds, kv) * SCALE

    qv = q2[...]
    ka = k2a[...]
    kb = k2b[...]
    sa = _nt(qv, ka) * SCALE
    sb = _nt(qv, kb) * SCALE
    m = jnp.maximum(sa.max(-1, keepdims=True), sb.max(-1, keepdims=True))
    ea = jnp.exp(sa - m)
    eb = jnp.exp(sb - m)
    d2c = dl2[:, 0:1]
    dsa = (ea * (_nt(gl2, v2a[...]) - d2c)).astype(BF16)
    dsb = (eb * (_nt(gl2, v2b[...]) - d2c)).astype(BF16)
    dq2s[...] = (_nn(dsa, ka) + _nn(dsb, kb)) * SCALE

    for j in range(4):
        r0 = pl.ds(j, n2, stride=4)
        r1 = pl.ds(j >> 1, n2, stride=2)
        outs[r0, :] = dq0s[r0, :] + dq1s[r1, :] * 0.5 + dq2s[...] * 0.25
    gq_ref[...] = outs[...].astype(BF16)


def _own_kernel(k1o, v1o, k1p, b1p, k2o, v2o, b2a, b2b, dk0, dv0,
                gk_ref, gv_ref, wide, dk1s, dv1s, dk2s, dv2s, outk, outv):
    n1 = dk1s.shape[0]
    n2 = dk2s.shape[0]
    qv = b1p[n1 + 16:, :]
    gv = b1p[0:n1, :]
    x = b1p[n1:n1 + 16, :].astype(F32)
    d_row = jnp.concatenate([(x[0:1] + x[2:3]) + x[4:5], (x[1:2] + x[3:4]) + x[5:6]], axis=1)
    st = _nt(k1o[...], qv) * SCALE
    m = st.max(0, keepdims=True)
    e = jnp.exp(st - m)
    p = e.astype(BF16)
    ds = (e * (_nt(v1o[...], gv) - d_row)).astype(BF16)
    dk1s[...] = _nn(ds, qv) * SCALE
    dv1s[...] = _nn(p, gv)

    wide[...] = k1p[...].astype(F32)
    ks = ((wide[pl.ds(0, n2, stride=2), :] + wide[pl.ds(1, n2, stride=2), :]) * 0.5).astype(BF16)
    ko = k2o[...]
    vo = v2o[...]
    dks = []
    dvs = []
    for b_ref in (b2a, b2b):
        qv = b_ref[n2 + 16:, :]
        gv = b_ref[0:n2, :]
        x = b_ref[n2:n2 + 16, :].astype(F32)
        d_row = (x[0:1] + x[1:2]) + x[2:3]
        so = _nt(ko, qv) * SCALE
        ss = _nt(ks, qv) * SCALE
        m = jnp.maximum(so.max(0, keepdims=True), ss.max(0, keepdims=True))
        e = jnp.exp(so - m)
        p = e.astype(BF16)
        ds = (e * (_nt(vo, gv) - d_row)).astype(BF16)
        dks.append(_nn(ds, qv))
        dvs.append(_nn(p, gv))
    dk2s[...] = (dks[0] + dks[1]) * SCALE
    dv2s[...] = dvs[0] + dvs[1]

    for j in range(4):
        r0 = pl.ds(j, n2, stride=4)
        r1 = pl.ds(j >> 1, n2, stride=2)
        outk[r0, :] = dk0[r0, :] + dk1s[r1, :] * 0.5 + dk2s[...] * 0.25
        outv[r0, :] = dv0[r0, :] + dv1s[r1, :] * 0.5 + dv2s[...] * 0.25
    gk_ref[...] = outk[...].astype(BF16)
    gv_ref[...] = outv[...].astype(BF16)


def _cols(rows):
    return pl.BlockSpec((rows, DH), lambda h: (0, h))


def _stacked(rows, index):
    return pl.BlockSpec((None, rows, DH), lambda h: (index, 0, h))


def _per_head(rows, width):
    return pl.BlockSpec((None, rows, width), lambda h: (h, 0, 0))


def _whole(rows, width):
    return pl.BlockSpec((rows, width), lambda h: (0, 0))


def _params():
    return pltpu.CompilerParams(dimension_semantics=("arbitrary",))


def _two(rows):
    return pl.BlockSpec((2, rows, DH), lambda h: (0, 0, h))


def shards(queries, key_states, value_states, out_grad):
    n0, width = queries.shape
    heads = width // DH
    n1 = n0 // 2
    n2 = n0 // 4
    q0, k0, v0, g0 = queries, key_states, value_states, out_grad
    s1, q1, s2, q2 = pl.pallas_call(
        _halve_kernel,
        grid=(heads,),
        in_specs=[_cols(n0), _cols(n0), _cols(n0)],
        out_specs=[_two(n1), _cols(n1), _two(n2), _cols(n2)],
        out_shape=[
            jax.ShapeDtypeStruct((2, n1, width), BF16),
            jax.ShapeDtypeStruct((n1, width), BF16),
            jax.ShapeDtypeStruct((2, n2, width), BF16),
            jax.ShapeDtypeStruct((n2, width), BF16),
        ],
        scratch_shapes=[pltpu.VMEM((n0, DH), F32), pltpu.VMEM((n1, DH), F32)],
        compiler_params=_params(),
    )(q0, k0, v0)
    r1 = from_partner(s1, 1)
    r2a = from_partner(s2, 2)
    r2b = from_partner(s2, 3)

    a0, ms0 = pl.pallas_call(
        _fwd0_kernel,
        grid=(heads,),
        in_specs=[_cols(n0), _cols(n0), _cols(n0)],
        out_specs=[_cols(n0), _per_head(n0, DH)],
        out_shape=[
            jax.ShapeDtypeStruct((n0, width), F32),
            jax.ShapeDtypeStruct((heads, n0, DH), F32),
        ],
        compiler_params=_params(),
    )(q0, k0, v0)

    att, w, sums = pl.pallas_call(
        _fwd12_kernel,
        grid=(heads,),
        in_specs=[
            _cols(n0), _per_head(n0, DH), _cols(n0),
            _cols(n1), _stacked(n1, 0), _stacked(n1, 1),
            _cols(n2), _stacked(n2, 0), _stacked(n2, 1), _stacked(n2, 0), _stacked(n2, 1),
        ],
        out_specs=[_cols(n0), _per_head(n0, DH), _whole(n0, DH)],
        out_shape=[
            jax.ShapeDtypeStruct((n0, width), BF16),
            jax.ShapeDtypeStruct((heads, n0, DH), F32),
            jax.ShapeDtypeStruct((n0, DH), F32),
        ],
        scratch_shapes=[pltpu.VMEM((n, DH), F32) for n in (n1, n1, n1, n2, n2, n2, n0, n0)],
        compiler_params=_params(),
    )(a0, ms0, g0, q1, r1, r1, q2, r2a, r2a, r2b, r2b)

    assert width * lax.axis_size("head") == 2 * 4 * DH
    other = lax.ppermute(sums, "head", [(0, 1), (1, 0)])

    norm, b1, b2 = pl.pallas_call(
        _bwd1_kernel,
        grid=(heads,),
        in_specs=[_cols(n0), _cols(n0), _per_head(n0, DH), _whole(n0, DH), _whole(n0, DH), _cols(n1), _cols(n2)],
        out_specs=[_cols(n0), _cols(2 * n1 + 16), _cols(2 * n2 + 16)],
        out_shape=[
            jax.ShapeDtypeStruct((n0, width), BF16),
            jax.ShapeDtypeStruct((2 * n1 + 16, width), BF16),
            jax.ShapeDtypeStruct((2 * n2 + 16, width), BF16),
        ],
        scratch_shapes=[pltpu.VMEM((n0, DH), F32), pltpu.VMEM((n0, DH), F32)],
        compiler_params=_params(),
    )(g0, att, w, sums, other, q1, q2)
    b1p = from_partner(b1, 1)
    b2a = from_partner(b2, 2)
    b2b = from_partner(b2, 3)

    gq, dk0, dv0 = pl.pallas_call(
        _bwd2_kernel,
        grid=(heads,),
        in_specs=[
            _cols(n0), _cols(n0), _cols(n0), _cols(n0), _cols(n0), _per_head(n0, DH),
            _whole(n0, DH), _whole(n0, DH),
            _cols(n1), _stacked(n1, 0), _stacked(n1, 1),
            _cols(n2), _stacked(n2, 0), _stacked(n2, 1), _stacked(n2, 0), _stacked(n2, 1),
        ],
        out_specs=[_cols(n0), _cols(n0), _cols(n0)],
        out_shape=[
            jax.ShapeDtypeStruct((n0, width), BF16),
            jax.ShapeDtypeStruct((n0, width), F32),
            jax.ShapeDtypeStruct((n0, width), F32),
        ],
        scratch_shapes=[pltpu.VMEM((n, DH), F32) for n in (n0, n0, n0, n1, n2, n0)],
        compiler_params=_params(),
    )(q0, k0, v0, g0, att, w, sums, other, q1, r1, r1, q2, r2a, r2a, r2b, r2b)

    gk, gv = pl.pallas_call(
        _own_kernel,
        grid=(heads,),
        in_specs=[
            _stacked(n1, 0), _stacked(n1, 1), _stacked(n1, 0), _cols(2 * n1 + 16),
            _stacked(n2, 0), _stacked(n2, 1), _cols(2 * n2 + 16), _cols(2 * n2 + 16),
            _cols(n0), _cols(n0),
        ],
        out_specs=[_cols(n0), _cols(n0)],
        out_shape=[
            jax.ShapeDtypeStruct((n0, width), BF16),
            jax.ShapeDtypeStruct((n0, width), BF16),
        ],
        scratch_shapes=[pltpu.VMEM((n, DH), F32) for n in (n1, n1, n1, n2, n2, n0, n0)],
        compiler_params=_params(),
    )(s1, s1, r1, b1p, s2, s2, b2a, b2b, dk0, dv0)
    return (norm, gq, gk, gv)


def solution(mesh):
    return jax.shard_map(
        shards,
        mesh=mesh,
        in_specs=(P("seq", "head"), P("seq", "head"), P("seq", "head"), P("seq", "head")),
        out_specs=(P("seq", "head"), P("seq", "head"), P("seq", "head"), P("seq", "head")),
        check_vma=False,
    )
```

```python
import jax
import jax.numpy as jnp
from jax import lax
from jax.experimental import pallas as pl
from jax.experimental.pallas import tpu as pltpu
from jax.sharding import PartitionSpec as P


DH = 128
EPSILON = 1e-06
SCALE = DH ** (-0.5)
F32 = jnp.float32
BF16 = jnp.bfloat16


def from_partner(value, mask):
    pairs = [(source, source ^ mask) for source in range(lax.axis_size("seq"))]
    return lax.ppermute(value, "seq", pairs)


def _nt(a, b):
    return lax.dot_general(a, b, (((1,), (1,)), ((), ())), preferred_element_type=F32)


def _nn(a, b):
    return lax.dot_general(a, b, (((1,), (0,)), ((), ())), preferred_element_type=F32)


def _tn(a, b):
    return lax.dot_general(a, b, (((0,), (0,)), ((), ())), preferred_element_type=F32)


def _lanes(shape):
    return lax.broadcasted_iota(jnp.int32, shape, len(shape) - 1)


def _halve_kernel(q0, k0, v0, s1_ref, q1_ref, s2_ref, q2_ref, wide, half):
    n1 = half.shape[0]
    n2 = n1 // 2
    for i, src in enumerate((k0, v0, q0)):
        wide[...] = src[...].astype(F32)
        h1 = ((wide[pl.ds(0, n1, stride=2), :] + wide[pl.ds(1, n1, stride=2), :]) * 0.5).astype(BF16)
        half[...] = h1.astype(F32)
        h2 = ((half[pl.ds(0, n2, stride=2), :] + half[pl.ds(1, n2, stride=2), :]) * 0.5).astype(BF16)
        if i < 2:
            s1_ref[i] = h1
            s2_ref[i] = h2
        else:
            q1_ref[...] = h1
            q2_ref[...] = h2


def _fwd0_kernel(q0, k0, v0, a0_ref, ms_ref):
    s = _nt(q0[...], k0[...]) * SCALE
    m = s.max(-1, keepdims=True)
    e = jnp.exp(s - m)
    a0_ref[...] = _nn(e.astype(BF16), v0[...])
    lane = _lanes(ms_ref.shape)
    ms_ref[...] = jnp.where(lane == 0, m, jnp.where(lane == 1, e.sum(-1, keepdims=True), 0.0))


def _fwd12_kernel(a0, ms0, g0, q1, k1p, v1p, q2, k2a, v2a, k2b, v2b,
                  att_ref, w_ref, sums_ref,
                  a1s, m1s, s1s, a2s, m2s, s2s, atts, ws):
    h = pl.program_id(0)
    n0 = atts.shape[0]
    n2 = a2s.shape[0]

    def put(a_ref, m_ref, s_ref, a, m, s):
        a_ref[...] = a
        m_ref[...] = jnp.broadcast_to(m, a.shape)
        s_ref[...] = jnp.broadcast_to(s, a.shape)

    s = _nt(q1[...], k1p[...]) * SCALE
    m = s.max(-1, keepdims=True)
    e = jnp.exp(s - m)
    put(a1s, m1s, s1s, _nn(e.astype(BF16), v1p[...]), m, e.sum(-1, keepdims=True))

    qv = q2[...]
    sa = _nt(qv, k2a[...]) * SCALE
    sb = _nt(qv, k2b[...]) * SCALE
    m = jnp.maximum(sa.max(-1, keepdims=True), sb.max(-1, keepdims=True))
    ea = jnp.exp(sa - m)
    eb = jnp.exp(sb - m)
    a = _nn(ea.astype(BF16), v2a[...]) + _nn(eb.astype(BF16), v2b[...])
    put(a2s, m2s, s2s, a, m, ea.sum(-1, keepdims=True) + eb.sum(-1, keepdims=True))

    lane = _lanes((n2, DH))
    for j in range(4):
        r0 = pl.ds(j, n2, stride=4)
        r1 = pl.ds(j >> 1, n2, stride=2)
        ms = ms0[r0, :]
        mm0 = ms[:, 0:1]
        mm1 = m1s[r1, :]
        mm2 = m2s[...]
        top = jnp.maximum(jnp.maximum(mm0, mm1), mm2)
        f0 = jnp.exp(mm0 - top)
        f1 = 2.0 * jnp.exp(mm1 - top)
        f2 = 4.0 * jnp.exp(mm2 - top)
        den = f0 * ms[:, 1:2] + f1 * s1s[r1, :] + f2 * s2s[...]
        num = f0 * a0[r0, :] + f1 * a1s[r1, :] + f2 * a2s[...]
        atts[r0, :] = (num / den).astype(BF16).astype(F32)
        ws[r0, :] = jnp.where(
            lane == 0, f0 / den, jnp.where(lane == 1, f1 / den, jnp.where(lane == 2, f2 / den, 0.0))
        )
    attv = atts[...]
    att_ref[...] = attv.astype(BF16)
    w_ref[...] = ws[...]
    gf = g0[...].astype(F32)
    sq = (attv * attv).sum(-1, keepdims=True)
    dt = (gf * attv).sum(-1, keepdims=True)
    lane0 = _lanes((n0, DH))
    part = jnp.where(lane0 == 0, sq, jnp.where(lane0 == 1, dt, 0.0))

    @pl.when(h == 0)
    def _():
        sums_ref[...] = part

    @pl.when(h > 0)
    def _():
        sums_ref[...] += part


def _level_grads(g0, att, w, mine, theirs, t_s, u_s):
    n0 = t_s.shape[0]
    n1 = n0 // 2
    n2 = n0 // 4
    full_width = 2 * 4 * DH
    totals = mine[:, 0:2] + theirs[:, 0:2]
    inv = lax.rsqrt(totals[:, 0:1] / full_width + EPSILON)
    coef = inv * inv * inv * totals[:, 1:2] / full_width
    attv = att[...].astype(F32)
    gf = g0[...].astype(F32)
    ga = inv * gf - coef * attv
    rt = (ga * attv).sum(-1, keepdims=True)
    wv = w[...]
    w0 = wv[:, 0:1]
    w1 = wv[:, 1:2]
    w2 = wv[:, 2:3]
    gl0 = (w0 * ga).astype(BF16)
    dl0 = w0 * rt
    t_s[...] = w1 * ga
    u_s[...] = jnp.broadcast_to(w1 * rt, (n0, DH))
    e_rows = pl.ds(0, n1, stride=2)
    o_rows = pl.ds(1, n1, stride=2)
    gl1 = (t_s[e_rows, :] + t_s[o_rows, :]).astype(BF16)
    dl1 = u_s[e_rows, :] + u_s[o_rows, :]
    t_s[...] = w2 * ga
    u_s[...] = jnp.broadcast_to(w2 * rt, (n0, DH))
    rows = [pl.ds(j, n2, stride=4) for j in range(4)]
    gl2 = (((t_s[rows[0], :] + t_s[rows[1], :]) + t_s[rows[2], :]) + t_s[rows[3], :]).astype(BF16)
    dl2 = ((u_s[rows[0], :] + u_s[rows[1], :]) + u_s[rows[2], :]) + u_s[rows[3], :]
    return inv, attv, gl0, dl0, gl1, dl1, gl2, dl2


def _split3(x):
    hi = x.astype(BF16).astype(F32)
    rest = x - hi
    mid = rest.astype(BF16).astype(F32)
    return hi, mid, rest - mid


def _coded(pieces):
    sub = lax.broadcasted_iota(jnp.int32, (16, DH), 0)
    out = jnp.zeros((16, DH), F32)
    for i, piece in enumerate(pieces):
        out = jnp.where(sub == i, piece, out)
    return out.astype(BF16)


def _bwd1_kernel(g0, att, w, mine, theirs, q1, q2, norm_ref, b1_ref, b2_ref, t_s, u_s):
    inv, attv, _, _, gl1, dl1, gl2, dl2 = _level_grads(g0, att, w, mine, theirs, t_s, u_s)
    n1 = gl1.shape[0]
    n2 = gl2.shape[0]
    norm_ref[...] = (attv * inv).astype(BF16)
    b1_ref[0:n1, :] = gl1
    b2_ref[0:n2, :] = gl2
    t1 = dl1.T
    a_parts = _split3(t1[0:1, 0:DH])
    b_parts = _split3(t1[0:1, DH:2 * DH])
    b1_ref[n1:n1 + 16, :] = _coded([a_parts[0], b_parts[0], a_parts[1], b_parts[1], a_parts[2], b_parts[2]])
    b2_ref[n2:n2 + 16, :] = _coded(list(_split3(dl2.T[0:1, :])))
    b2_ref[n2 + 16:, :] = q2[...]


def _bwd2_kernel(q0, k0, v0, g0, att, w, mine, theirs, q1, k1p, v1p, q2, k2a, v2a, k2b, v2b,
                 gq_ref, dk0_ref, dv0_ref,
                 t_s, u_s, dq0s, dq1s, dq2s, outs):
    n2 = dq2s.shape[0]
    _, _, gl0, dl0, gl1, dl1, gl2, dl2 = _level_grads(g0, att, w, mine, theirs, t_s, u_s)
    q0v = q0[...]
    k0v = k0[...]
    v0v = v0[...]
    s = _nt(q0v, k0v) * SCALE
    m = s.max(-1, keepdims=True)
    e = jnp.exp(s - m)
    p = e.astype(BF16)
    ds = (e * (_nt(gl0, v0v) - dl0)).astype(BF16)
    dq0s[...] = _nn(ds, k0v) * SCALE
    dk0_ref[...] = _tn(ds, q0v) * SCALE
    dv0_ref[...] = _tn(p, gl0)

    kv = k1p[...]
    s = _nt(q1[...], kv) * SCALE
    m = s.max(-1, keepdims=True)
    e = jnp.exp(s - m)
    ds = (e * (_nt(gl1, v1p[...]) - dl1[:, 0:1])).astype(BF16)
    dq1s[...] = _nn(ds, kv) * SCALE

    qv = q2[...]
    ka = k2a[...]
    kb = k2b[...]
    sa = _nt(qv, ka) * SCALE
    sb = _nt(qv, kb) * SCALE
    m = jnp.maximum(sa.max(-1, keepdims=True), sb.max(-1, keepdims=True))
    ea = jnp.exp(sa - m)
    eb = jnp.exp(sb - m)
    d2c = dl2[:, 0:1]
    dsa = (ea * (_nt(gl2, v2a[...]) - d2c)).astype(BF16)
    dsb = (eb * (_nt(gl2, v2b[...]) - d2c)).astype(BF16)
    dq2s[...] = (_nn(dsa, ka) + _nn(dsb, kb)) * SCALE

    for j in range(4):
        r0 = pl.ds(j, n2, stride=4)
        r1 = pl.ds(j >> 1, n2, stride=2)
        outs[r0, :] = dq0s[r0, :] + dq1s[r1, :] * 0.5 + dq2s[...] * 0.25
    gq_ref[...] = outs[...].astype(BF16)


def _own_kernel(k1o, v1o, k1p, q1p, b1p, k2o, v2o, b2a, b2b, dk0, dv0,
                gk_ref, gv_ref, wide, dk1s, dv1s, dk2s, dv2s, outk, outv):
    n1 = dk1s.shape[0]
    n2 = dk2s.shape[0]
    qv = q1p[...]
    gv = b1p[0:n1, :]
    x = b1p[n1:n1 + 16, :].astype(F32)
    d_row = jnp.concatenate([(x[0:1] + x[2:3]) + x[4:5], (x[1:2] + x[3:4]) + x[5:6]], axis=1)
    st = _nt(k1o[...], qv) * SCALE
    m = st.max(0, keepdims=True)
    e = jnp.exp(st - m)
    p = e.astype(BF16)
    ds = (e * (_nt(v1o[...], gv) - d_row)).astype(BF16)
    dk1s[...] = _nn(ds, qv) * SCALE
    dv1s[...] = _nn(p, gv)

    wide[...] = k1p[...].astype(F32)
    ks = ((wide[pl.ds(0, n2, stride=2), :] + wide[pl.ds(1, n2, stride=2), :]) * 0.5).astype(BF16)
    ko = k2o[...]
    vo = v2o[...]
    dks = []
    dvs = []
    for b_ref in (b2a, b2b):
        qv = b_ref[n2 + 16:, :]
        gv = b_ref[0:n2, :]
        x = b_ref[n2:n2 + 16, :].astype(F32)
        d_row = (x[0:1] + x[1:2]) + x[2:3]
        so = _nt(ko, qv) * SCALE
        ss = _nt(ks, qv) * SCALE
        m = jnp.maximum(so.max(0, keepdims=True), ss.max(0, keepdims=True))
        e = jnp.exp(so - m)
        p = e.astype(BF16)
        ds = (e * (_nt(vo, gv) - d_row)).astype(BF16)
        dks.append(_nn(ds, qv))
        dvs.append(_nn(p, gv))
    dk2s[...] = (dks[0] + dks[1]) * SCALE
    dv2s[...] = dvs[0] + dvs[1]

    for j in range(4):
        r0 = pl.ds(j, n2, stride=4)
        r1 = pl.ds(j >> 1, n2, stride=2)
        outk[r0, :] = dk0[r0, :] + dk1s[r1, :] * 0.5 + dk2s[...] * 0.25
        outv[r0, :] = dv0[r0, :] + dv1s[r1, :] * 0.5 + dv2s[...] * 0.25
    gk_ref[...] = outk[...].astype(BF16)
    gv_ref[...] = outv[...].astype(BF16)


def _cols(rows):
    return pl.BlockSpec((rows, DH), lambda h: (0, h))


def _stacked(rows, index):
    return pl.BlockSpec((None, rows, DH), lambda h: (index, 0, h))


def _per_head(rows, width):
    return pl.BlockSpec((None, rows, width), lambda h: (h, 0, 0))


def _whole(rows, width):
    return pl.BlockSpec((rows, width), lambda h: (0, 0))


def _params():
    return pltpu.CompilerParams(dimension_semantics=("arbitrary",))


def _fwd12_call(heads, n0, n1, n2, width, a0, ms0, g0, q1, r1, q2, r2a, r2b):
    return pl.pallas_call(
        _fwd12_kernel,
        grid=(heads,),
        in_specs=[
            _cols(n0), _per_head(n0, DH), _cols(n0),
            _cols(n1), _stacked(n1, 0), _stacked(n1, 1),
            _cols(n2), _stacked(n2, 0), _stacked(n2, 1), _stacked(n2, 0), _stacked(n2, 1),
        ],
        out_specs=[_cols(n0), _per_head(n0, DH), _whole(n0, DH)],
        out_shape=[
            jax.ShapeDtypeStruct((n0, width), BF16),
            jax.ShapeDtypeStruct((heads, n0, DH), F32),
            jax.ShapeDtypeStruct((n0, DH), F32),
        ],
        scratch_shapes=[pltpu.VMEM((n, DH), F32) for n in (n1, n1, n1, n2, n2, n2, n0, n0)],
        compiler_params=_params(),
    )(a0, ms0, g0, q1, r1, r1, q2, r2a, r2a, r2b, r2b)


def _two(rows):
    return pl.BlockSpec((2, rows, DH), lambda h: (0, 0, h))


def shards(queries, key_states, value_states, out_grad):
    n0, width = queries.shape
    heads = width // DH
    n1 = n0 // 2
    n2 = n0 // 4
    q0, k0, v0, g0 = queries, key_states, value_states, out_grad
    s1, q1, s2, q2 = pl.pallas_call(
        _halve_kernel,
        grid=(heads,),
        in_specs=[_cols(n0), _cols(n0), _cols(n0)],
        out_specs=[_two(n1), _cols(n1), _two(n2), _cols(n2)],
        out_shape=[
            jax.ShapeDtypeStruct((2, n1, width), BF16),
            jax.ShapeDtypeStruct((n1, width), BF16),
            jax.ShapeDtypeStruct((2, n2, width), BF16),
            jax.ShapeDtypeStruct((n2, width), BF16),
        ],
        scratch_shapes=[pltpu.VMEM((n0, DH), F32), pltpu.VMEM((n1, DH), F32)],
        compiler_params=_params(),
    )(q0, k0, v0)
    r1 = from_partner(s1, 1)
    r2a = from_partner(s2, 2)
    r2b = from_partner(s2, 3)

    a0, ms0 = pl.pallas_call(
        _fwd0_kernel,
        grid=(heads,),
        in_specs=[_cols(n0), _cols(n0), _cols(n0)],
        out_specs=[_cols(n0), _per_head(n0, DH)],
        out_shape=[
            jax.ShapeDtypeStruct((n0, width), F32),
            jax.ShapeDtypeStruct((heads, n0, DH), F32),
        ],
        compiler_params=_params(),
    )(q0, k0, v0)

    att, w, sums = _fwd12_call(heads, n0, n1, n2, width, a0, ms0, g0, q1, r1, q2, r2a, r2b)


    assert width * lax.axis_size("head") == 2 * 4 * DH
    other = lax.ppermute(sums, "head", [(0, 1), (1, 0)])
    gated = lax.optimization_barrier((q1, r1, r2a, r2b))[0]
    q1p = from_partner(gated, 1)

    norm, b1, b2 = pl.pallas_call(
        _bwd1_kernel,
        grid=(heads,),
        in_specs=[_cols(n0), _cols(n0), _per_head(n0, DH), _whole(n0, DH), _whole(n0, DH), _cols(n1), _cols(n2)],
        out_specs=[_cols(n0), _cols(n1 + 16), _cols(2 * n2 + 16)],
        out_shape=[
            jax.ShapeDtypeStruct((n0, width), BF16),
            jax.ShapeDtypeStruct((n1 + 16, width), BF16),
            jax.ShapeDtypeStruct((2 * n2 + 16, width), BF16),
        ],
        scratch_shapes=[pltpu.VMEM((n0, DH), F32), pltpu.VMEM((n0, DH), F32)],
        compiler_params=_params(),
    )(g0, att, w, sums, other, q1, q2)
    b1p = from_partner(b1, 1)
    b2a = from_partner(b2, 2)
    b2b = from_partner(b2, 3)

    gq, dk0, dv0 = pl.pallas_call(
        _bwd2_kernel,
        grid=(heads,),
        in_specs=[
            _cols(n0), _cols(n0), _cols(n0), _cols(n0), _cols(n0), _per_head(n0, DH),
            _whole(n0, DH), _whole(n0, DH),
            _cols(n1), _stacked(n1, 0), _stacked(n1, 1),
            _cols(n2), _stacked(n2, 0), _stacked(n2, 1), _stacked(n2, 0), _stacked(n2, 1),
        ],
        out_specs=[_cols(n0), _cols(n0), _cols(n0)],
        out_shape=[
            jax.ShapeDtypeStruct((n0, width), BF16),
            jax.ShapeDtypeStruct((n0, width), F32),
            jax.ShapeDtypeStruct((n0, width), F32),
        ],
        scratch_shapes=[pltpu.VMEM((n, DH), F32) for n in (n0, n0, n0, n1, n2, n0)],
        compiler_params=_params(),
    )(q0, k0, v0, g0, att, w, sums, other, q1, r1, r1, q2, r2a, r2a, r2b, r2b)

    gk, gv = pl.pallas_call(
        _own_kernel,
        grid=(heads,),
        in_specs=[
            _stacked(n1, 0), _stacked(n1, 1), _stacked(n1, 0), _cols(n1), _cols(n1 + 16),
            _stacked(n2, 0), _stacked(n2, 1), _cols(2 * n2 + 16), _cols(2 * n2 + 16),
            _cols(n0), _cols(n0),
        ],
        out_specs=[_cols(n0), _cols(n0)],
        out_shape=[
            jax.ShapeDtypeStruct((n0, width), BF16),
            jax.ShapeDtypeStruct((n0, width), BF16),
        ],
        scratch_shapes=[pltpu.VMEM((n, DH), F32) for n in (n1, n1, n1, n2, n2, n0, n0)],
        compiler_params=_params(),
    )(s1, s1, r1, q1p, b1p, s2, s2, b2a, b2b, dk0, dv0)
    return (norm, gq, gk, gv)


def solution(mesh):
    return jax.shard_map(
        shards,
        mesh=mesh,
        in_specs=(P("seq", "head"), P("seq", "head"), P("seq", "head"), P("seq", "head")),
        out_specs=(P("seq", "head"), P("seq", "head"), P("seq", "head"), P("seq", "head")),
        check_vma=False,
    )
```

```python
import jax
import jax.numpy as jnp
from jax import lax
from jax.experimental import pallas as pl
from jax.experimental.pallas import tpu as pltpu
from jax.sharding import PartitionSpec as P

DH = 128
LEAF = 256
LEVELS = 3
EPSILON = 1e-06
SCALE = DH ** (-0.5)
F32 = jnp.float32
BF16 = jnp.bfloat16


def from_partner(value, mask):
    pairs = [(source, source ^ mask) for source in range(lax.axis_size("seq"))]
    return lax.ppermute(value, "seq", pairs)


def halving(source):
    widened = source.astype(F32)
    paired = widened.reshape(widened.shape[:-2] + (widened.shape[-2] // 2, 2, widened.shape[-1]))
    return ((paired[..., 0, :] + paired[..., 1, :]) * 0.5).astype(BF16)


def _nt(a, b):
    return lax.dot_general(a, b, (((1,), (1,)), ((), ())), preferred_element_type=F32)


def _nn(a, b):
    return lax.dot_general(a, b, (((1,), (0,)), ((), ())), preferred_element_type=F32)


def _tn(a, b):
    return lax.dot_general(a, b, (((0,), (0,)), ((), ())), preferred_element_type=F32)


def _lanes(shape):
    return lax.broadcasted_iota(jnp.int32, shape, len(shape) - 1)


def _halve_kernel(q0, k0, v0, s1_ref, q1_ref, s2_ref, q2_ref, wide, half):
    n1 = half.shape[0]
    n2 = n1 // 2
    for h in range(q0.shape[1] // DH):
        cols = slice(h * DH, (h + 1) * DH)
        for i, src in enumerate((k0, v0, q0)):
            wide[...] = src[:, cols].astype(F32)
            h1 = ((wide[pl.ds(0, n1, stride=2), :] + wide[pl.ds(1, n1, stride=2), :]) * 0.5).astype(BF16)
            half[...] = h1.astype(F32)
            h2 = ((half[pl.ds(0, n2, stride=2), :] + half[pl.ds(1, n2, stride=2), :]) * 0.5).astype(BF16)
            if i < 2:
                s1_ref[i, :, cols] = h1
                s2_ref[i, :, cols] = h2
            else:
                q1_ref[:, cols] = h1
                q2_ref[:, cols] = h2


def _fwd0_kernel(q0, k0, v0, a0_ref, ms_ref):
    s = _nt(q0[...], k0[...]) * SCALE
    m = s.max(-1, keepdims=True)
    e = jnp.exp(s - m)
    a0_ref[...] = _nn(e.astype(BF16), v0[...])
    lane = _lanes(ms_ref.shape)
    ms_ref[...] = jnp.where(lane == 0, m, jnp.where(lane == 1, e.sum(-1, keepdims=True), 0.0))


def _fwd12_kernel(a0, ms0, g0, q1, k1p, v1p, q2, k2a, v2a, k2b, v2b,
                  att_ref, w_ref, sums_ref,
                  a1s, m1s, s1s, a2s, m2s, s2s, atts, ws):
    h = pl.program_id(0)
    n0 = atts.shape[0]
    n2 = a2s.shape[0]

    def put(a_ref, m_ref, s_ref, a, m, s):
        a_ref[...] = a
        m_ref[...] = jnp.broadcast_to(m, a.shape)
        s_ref[...] = jnp.broadcast_to(s, a.shape)

    s = _nt(q1[...], k1p[...]) * SCALE
    m = s.max(-1, keepdims=True)
    e = jnp.exp(s - m)
    put(a1s, m1s, s1s, _nn(e.astype(BF16), v1p[...]), m, e.sum(-1, keepdims=True))

    qv = q2[...]
    sa = _nt(qv, k2a[...]) * SCALE
    sb = _nt(qv, k2b[...]) * SCALE
    m = jnp.maximum(sa.max(-1, keepdims=True), sb.max(-1, keepdims=True))
    ea = jnp.exp(sa - m)
    eb = jnp.exp(sb - m)
    a = _nn(ea.astype(BF16), v2a[...]) + _nn(eb.astype(BF16), v2b[...])
    put(a2s, m2s, s2s, a, m, ea.sum(-1, keepdims=True) + eb.sum(-1, keepdims=True))

    lane = _lanes((n2, DH))
    for j in range(4):
        r0 = pl.ds(j, n2, stride=4)
        r1 = pl.ds(j >> 1, n2, stride=2)
        ms = ms0[r0, :]
        mm0 = ms[:, 0:1]
        mm1 = m1s[r1, :]
        mm2 = m2s[...]
        top = jnp.maximum(jnp.maximum(mm0, mm1), mm2)
        f0 = jnp.exp(mm0 - top)
        f1 = 2.0 * jnp.exp(mm1 - top)
        f2 = 4.0 * jnp.exp(mm2 - top)
        den = f0 * ms[:, 1:2] + f1 * s1s[r1, :] + f2 * s2s[...]
        num = f0 * a0[r0, :] + f1 * a1s[r1, :] + f2 * a2s[...]
        atts[r0, :] = (num / den).astype(BF16).astype(F32)
        ws[r0, :] = jnp.where(
            lane == 0, f0 / den, jnp.where(lane == 1, f1 / den, jnp.where(lane == 2, f2 / den, 0.0))
        )
    attv = atts[...]
    att_ref[...] = attv.astype(BF16)
    w_ref[...] = ws[...]
    gf = g0[...].astype(F32)
    sq = (attv * attv).sum(-1, keepdims=True)
    dt = (gf * attv).sum(-1, keepdims=True)
    lane0 = _lanes((n0, DH))
    part = jnp.where(lane0 == 0, sq, jnp.where(lane0 == 1, dt, 0.0))

    @pl.when(h == 0)
    def _():
        sums_ref[...] = part

    @pl.when(h > 0)
    def _():
        sums_ref[...] += part


def _level_grads(g0, att, w, mine, theirs, t_s, u_s):
    n0 = t_s.shape[0]
    n1 = n0 // 2
    n2 = n0 // 4
    full_width = 2 * 4 * DH
    totals = mine[:, 0:2] + theirs[:, 0:2]
    inv = lax.rsqrt(totals[:, 0:1] / full_width + EPSILON)
    coef = inv * inv * inv * totals[:, 1:2] / full_width
    attv = att[...].astype(F32)
    gf = g0[...].astype(F32)
    ga = inv * gf - coef * attv
    rt = (ga * attv).sum(-1, keepdims=True)
    wv = w[...]
    w0 = wv[:, 0:1]
    w1 = wv[:, 1:2]
    w2 = wv[:, 2:3]
    gl0 = (w0 * ga).astype(BF16)
    dl0 = w0 * rt
    t_s[...] = w1 * ga
    u_s[...] = jnp.broadcast_to(w1 * rt, (n0, DH))
    e_rows = pl.ds(0, n1, stride=2)
    o_rows = pl.ds(1, n1, stride=2)
    gl1 = (t_s[e_rows, :] + t_s[o_rows, :]).astype(BF16)
    dl1 = u_s[e_rows, :] + u_s[o_rows, :]
    t_s[...] = w2 * ga
    u_s[...] = jnp.broadcast_to(w2 * rt, (n0, DH))
    rows = [pl.ds(j, n2, stride=4) for j in range(4)]
    gl2 = (((t_s[rows[0], :] + t_s[rows[1], :]) + t_s[rows[2], :]) + t_s[rows[3], :]).astype(BF16)
    dl2 = ((u_s[rows[0], :] + u_s[rows[1], :]) + u_s[rows[2], :]) + u_s[rows[3], :]
    return inv, attv, gl0, dl0, gl1, dl1, gl2, dl2


def _split3(x):
    hi = x.astype(BF16).astype(F32)
    rest = x - hi
    mid = rest.astype(BF16).astype(F32)
    return hi, mid, rest - mid


def _coded(pieces):
    sub = lax.broadcasted_iota(jnp.int32, (16, DH), 0)
    out = jnp.zeros((16, DH), F32)
    for i, piece in enumerate(pieces):
        out = jnp.where(sub == i, piece, out)
    return out.astype(BF16)


def _bwd1_kernel(g0, att, w, mine, theirs, q1, q2, norm_ref, b1_ref, b2_ref, t_s, u_s):
    inv, attv, _, _, gl1, dl1, gl2, dl2 = _level_grads(g0, att, w, mine, theirs, t_s, u_s)
    n1 = gl1.shape[0]
    n2 = gl2.shape[0]
    norm_ref[...] = (attv * inv).astype(BF16)
    b1_ref[0:n1, :] = gl1
    b2_ref[0:n2, :] = gl2
    t1 = dl1.T
    a_parts = _split3(t1[0:1, 0:DH])
    b_parts = _split3(t1[0:1, DH:2 * DH])
    b1_ref[n1:n1 + 16, :] = _coded([a_parts[0], b_parts[0], a_parts[1], b_parts[1], a_parts[2], b_parts[2]])
    b2_ref[n2:n2 + 16, :] = _coded(list(_split3(dl2.T[0:1, :])))
    b1_ref[n1 + 16:, :] = q1[...]
    b2_ref[n2 + 16:, :] = q2[...]


def _bwd2_kernel(q0, k0, v0, g0, att, w, mine, theirs, q1, k1p, v1p, q2, k2a, v2a, k2b, v2b,
                 gq_ref, dk0_ref, dv0_ref,
                 t_s, u_s, dq0s, dq1s, dq2s, outs):
    n2 = dq2s.shape[0]
    _, _, gl0, dl0, gl1, dl1, gl2, dl2 = _level_grads(g0, att, w, mine, theirs, t_s, u_s)
    q0v = q0[...]
    k0v = k0[...]
    v0v = v0[...]
    s = _nt(q0v, k0v) * SCALE
    m = s.max(-1, keepdims=True)
    e = jnp.exp(s - m)
    p = e.astype(BF16)
    ds = (e * (_nt(gl0, v0v) - dl0)).astype(BF16)
    dq0s[...] = _nn(ds, k0v) * SCALE
    dk0_ref[...] = _tn(ds, q0v) * SCALE
    dv0_ref[...] = _tn(p, gl0)

    kv = k1p[...]
    s = _nt(q1[...], kv) * SCALE
    m = s.max(-1, keepdims=True)
    e = jnp.exp(s - m)
    ds = (e * (_nt(gl1, v1p[...]) - dl1[:, 0:1])).astype(BF16)
    dq1s[...] = _nn(ds, kv) * SCALE

    qv = q2[...]
    ka = k2a[...]
    kb = k2b[...]
    sa = _nt(qv, ka) * SCALE
    sb = _nt(qv, kb) * SCALE
    m = jnp.maximum(sa.max(-1, keepdims=True), sb.max(-1, keepdims=True))
    ea = jnp.exp(sa - m)
    eb = jnp.exp(sb - m)
    d2c = dl2[:, 0:1]
    dsa = (ea * (_nt(gl2, v2a[...]) - d2c)).astype(BF16)
    dsb = (eb * (_nt(gl2, v2b[...]) - d2c)).astype(BF16)
    dq2s[...] = (_nn(dsa, ka) + _nn(dsb, kb)) * SCALE

    for j in range(4):
        r0 = pl.ds(j, n2, stride=4)
        r1 = pl.ds(j >> 1, n2, stride=2)
        outs[r0, :] = dq0s[r0, :] + dq1s[r1, :] * 0.5 + dq2s[...] * 0.25
    gq_ref[...] = outs[...].astype(BF16)


def _own_kernel(k1o, v1o, k1p, b1p, k2o, v2o, b2a, b2b, dk0, dv0,
                gk_ref, gv_ref, wide, dk1s, dv1s, dk2s, dv2s, outk, outv):
    n1 = dk1s.shape[0]
    n2 = dk2s.shape[0]
    qv = b1p[n1 + 16:, :]
    gv = b1p[0:n1, :]
    x = b1p[n1:n1 + 16, :].astype(F32)
    d_row = jnp.concatenate([(x[0:1] + x[2:3]) + x[4:5], (x[1:2] + x[3:4]) + x[5:6]], axis=1)
    st = _nt(k1o[...], qv) * SCALE
    m = st.max(0, keepdims=True)
    e = jnp.exp(st - m)
    p = e.astype(BF16)
    ds = (e * (_nt(v1o[...], gv) - d_row)).astype(BF16)
    dk1s[...] = _nn(ds, qv) * SCALE
    dv1s[...] = _nn(p, gv)

    wide[...] = k1p[...].astype(F32)
    ks = ((wide[pl.ds(0, n2, stride=2), :] + wide[pl.ds(1, n2, stride=2), :]) * 0.5).astype(BF16)
    ko = k2o[...]
    vo = v2o[...]
    dks = []
    dvs = []
    for b_ref in (b2a, b2b):
        qv = b_ref[n2 + 16:, :]
        gv = b_ref[0:n2, :]
        x = b_ref[n2:n2 + 16, :].astype(F32)
        d_row = (x[0:1] + x[1:2]) + x[2:3]
        so = _nt(ko, qv) * SCALE
        ss = _nt(ks, qv) * SCALE
        m = jnp.maximum(so.max(0, keepdims=True), ss.max(0, keepdims=True))
        e = jnp.exp(so - m)
        p = e.astype(BF16)
        ds = (e * (_nt(vo, gv) - d_row)).astype(BF16)
        dks.append(_nn(ds, qv))
        dvs.append(_nn(p, gv))
    dk2s[...] = (dks[0] + dks[1]) * SCALE
    dv2s[...] = dvs[0] + dvs[1]

    for j in range(4):
        r0 = pl.ds(j, n2, stride=4)
        r1 = pl.ds(j >> 1, n2, stride=2)
        outk[r0, :] = dk0[r0, :] + dk1s[r1, :] * 0.5 + dk2s[...] * 0.25
        outv[r0, :] = dv0[r0, :] + dv1s[r1, :] * 0.5 + dv2s[...] * 0.25
    gk_ref[...] = outk[...].astype(BF16)
    gv_ref[...] = outv[...].astype(BF16)


def _cols(rows):
    return pl.BlockSpec((rows, DH), lambda h: (0, h))


def _stacked(rows, index):
    return pl.BlockSpec((None, rows, DH), lambda h: (index, 0, h))


def _per_head(rows, width):
    return pl.BlockSpec((None, rows, width), lambda h: (h, 0, 0))


def _whole(rows, width):
    return pl.BlockSpec((rows, width), lambda h: (0, 0))


def _params():
    return pltpu.CompilerParams(dimension_semantics=("arbitrary",))


def _full3(rows, width):
    return pl.BlockSpec((2, rows, width), lambda h: (0, 0, 0))


def _two(rows):
    return pl.BlockSpec((2, rows, DH), lambda h: (0, 0, h))


def shards(queries, key_states, value_states, out_grad):
    n0, width = queries.shape
    heads = width // DH
    n1 = n0 // 2
    n2 = n0 // 4
    q0, k0, v0, g0 = queries, key_states, value_states, out_grad
    s1, q1, s2, q2 = pl.pallas_call(
        _halve_kernel,
        grid=(1,),
        in_specs=[_whole(n0, width), _whole(n0, width), _whole(n0, width)],
        out_specs=[_full3(n1, width), _whole(n1, width), _full3(n2, width), _whole(n2, width)],
        out_shape=[
            jax.ShapeDtypeStruct((2, n1, width), BF16),
            jax.ShapeDtypeStruct((n1, width), BF16),
            jax.ShapeDtypeStruct((2, n2, width), BF16),
            jax.ShapeDtypeStruct((n2, width), BF16),
        ],
        scratch_shapes=[pltpu.VMEM((n0, DH), F32), pltpu.VMEM((n1, DH), F32)],
        compiler_params=_params(),
    )(q0, k0, v0)
    r1 = from_partner(s1, 1)
    r2a = from_partner(s2, 2)
    r2b = from_partner(s2, 3)

    a0, ms0 = pl.pallas_call(
        _fwd0_kernel,
        grid=(heads,),
        in_specs=[_cols(n0), _cols(n0), _cols(n0)],
        out_specs=[_cols(n0), _per_head(n0, DH)],
        out_shape=[
            jax.ShapeDtypeStruct((n0, width), F32),
            jax.ShapeDtypeStruct((heads, n0, DH), F32),
        ],
        compiler_params=_params(),
    )(q0, k0, v0)

    att, w, sums = pl.pallas_call(
        _fwd12_kernel,
        grid=(heads,),
        in_specs=[
            _cols(n0), _per_head(n0, DH), _cols(n0),
            _cols(n1), _stacked(n1, 0), _stacked(n1, 1),
            _cols(n2), _stacked(n2, 0), _stacked(n2, 1), _stacked(n2, 0), _stacked(n2, 1),
        ],
        out_specs=[_cols(n0), _per_head(n0, DH), _whole(n0, DH)],
        out_shape=[
            jax.ShapeDtypeStruct((n0, width), BF16),
            jax.ShapeDtypeStruct((heads, n0, DH), F32),
            jax.ShapeDtypeStruct((n0, DH), F32),
        ],
        scratch_shapes=[pltpu.VMEM((n, DH), F32) for n in (n1, n1, n1, n2, n2, n2, n0, n0)],
        compiler_params=_params(),
    )(a0, ms0, g0, q1, r1, r1, q2, r2a, r2a, r2b, r2b)

    assert width * lax.axis_size("head") == 2 * 4 * DH
    other = lax.ppermute(sums, "head", [(0, 1), (1, 0)])

    norm, b1, b2 = pl.pallas_call(
        _bwd1_kernel,
        grid=(heads,),
        in_specs=[_cols(n0), _cols(n0), _per_head(n0, DH), _whole(n0, DH), _whole(n0, DH), _cols(n1), _cols(n2)],
        out_specs=[_cols(n0), _cols(2 * n1 + 16), _cols(2 * n2 + 16)],
        out_shape=[
            jax.ShapeDtypeStruct((n0, width), BF16),
            jax.ShapeDtypeStruct((2 * n1 + 16, width), BF16),
            jax.ShapeDtypeStruct((2 * n2 + 16, width), BF16),
        ],
        scratch_shapes=[pltpu.VMEM((n0, DH), F32), pltpu.VMEM((n0, DH), F32)],
        compiler_params=_params(),
    )(g0, att, w, sums, other, q1, q2)
    b1p = from_partner(b1, 1)
    b2a = from_partner(b2, 2)
    b2b = from_partner(b2, 3)

    gq, dk0, dv0 = pl.pallas_call(
        _bwd2_kernel,
        grid=(heads,),
        in_specs=[
            _cols(n0), _cols(n0), _cols(n0), _cols(n0), _cols(n0), _per_head(n0, DH),
            _whole(n0, DH), _whole(n0, DH),
            _cols(n1), _stacked(n1, 0), _stacked(n1, 1),
            _cols(n2), _stacked(n2, 0), _stacked(n2, 1), _stacked(n2, 0), _stacked(n2, 1),
        ],
        out_specs=[_cols(n0), _cols(n0), _cols(n0)],
        out_shape=[
            jax.ShapeDtypeStruct((n0, width), BF16),
            jax.ShapeDtypeStruct((n0, width), F32),
            jax.ShapeDtypeStruct((n0, width), F32),
        ],
        scratch_shapes=[pltpu.VMEM((n, DH), F32) for n in (n0, n0, n0, n1, n2, n0)],
        compiler_params=_params(),
    )(q0, k0, v0, g0, att, w, sums, other, q1, r1, r1, q2, r2a, r2a, r2b, r2b)

    gk, gv = pl.pallas_call(
        _own_kernel,
        grid=(heads,),
        in_specs=[
            _stacked(n1, 0), _stacked(n1, 1), _stacked(n1, 0), _cols(2 * n1 + 16),
            _stacked(n2, 0), _stacked(n2, 1), _cols(2 * n2 + 16), _cols(2 * n2 + 16),
            _cols(n0), _cols(n0),
        ],
        out_specs=[_cols(n0), _cols(n0)],
        out_shape=[
            jax.ShapeDtypeStruct((n0, width), BF16),
            jax.ShapeDtypeStruct((n0, width), BF16),
        ],
        scratch_shapes=[pltpu.VMEM((n, DH), F32) for n in (n1, n1, n1, n2, n2, n0, n0)],
        compiler_params=_params(),
    )(s1, s1, r1, b1p, s2, s2, b2a, b2b, dk0, dv0)
    return (norm, gq, gk, gv)


def solution(mesh):
    return jax.shard_map(
        shards,
        mesh=mesh,
        in_specs=(P("seq", "head"), P("seq", "head"), P("seq", "head"), P("seq", "head")),
        out_specs=(P("seq", "head"), P("seq", "head"), P("seq", "head"), P("seq", "head")),
        check_vma=False,
    )
```

```python
import jax
import jax.numpy as jnp
from jax import lax
from jax.experimental import pallas as pl
from jax.experimental.pallas import tpu as pltpu
from jax.sharding import PartitionSpec as P

DH = 128
LEAF = 256
LEVELS = 3
EPSILON = 1e-06
SCALE = DH ** (-0.5)
F32 = jnp.float32
BF16 = jnp.bfloat16


def from_partner(value, mask):
    pairs = [(source, source ^ mask) for source in range(lax.axis_size("seq"))]
    return lax.ppermute(value, "seq", pairs)


def halving(source):
    widened = source.astype(F32)
    paired = widened.reshape(widened.shape[:-2] + (widened.shape[-2] // 2, 2, widened.shape[-1]))
    return ((paired[..., 0, :] + paired[..., 1, :]) * 0.5).astype(BF16)


def _nt(a, b):
    return lax.dot_general(a, b, (((1,), (1,)), ((), ())), preferred_element_type=F32)


def _nn(a, b):
    return lax.dot_general(a, b, (((1,), (0,)), ((), ())), preferred_element_type=F32)


def _tn(a, b):
    return lax.dot_general(a, b, (((0,), (0,)), ((), ())), preferred_element_type=F32)


def _lanes(shape):
    return lax.broadcasted_iota(jnp.int32, shape, len(shape) - 1)


def _halve_kernel(q0, k0, v0, s1_ref, q1_ref, s2_ref, q2_ref, wide, half):
    n1 = half.shape[0]
    n2 = n1 // 2
    for h in range(q0.shape[1] // DH):
        cols = slice(h * DH, (h + 1) * DH)
        for i, src in enumerate((k0, v0, q0)):
            wide[...] = src[:, cols].astype(F32)
            h1 = ((wide[pl.ds(0, n1, stride=2), :] + wide[pl.ds(1, n1, stride=2), :]) * 0.5).astype(BF16)
            half[...] = h1.astype(F32)
            h2 = ((half[pl.ds(0, n2, stride=2), :] + half[pl.ds(1, n2, stride=2), :]) * 0.5).astype(BF16)
            if i < 2:
                s1_ref[i, :, cols] = h1
                s2_ref[i, :, cols] = h2
            else:
                q1_ref[:, cols] = h1
                q2_ref[:, cols] = h2


def _fwd0_kernel(q0, k0, v0, a0_ref, ms_ref):
    s = _nt(q0[...], k0[...]) * SCALE
    m = s.max(-1, keepdims=True)
    e = jnp.exp(s - m)
    a0_ref[...] = _nn(e.astype(BF16), v0[...])
    lane = _lanes(ms_ref.shape)
    ms_ref[...] = jnp.where(lane == 0, m, jnp.where(lane == 1, e.sum(-1, keepdims=True), 0.0))


def _fwd12_kernel(a0, ms0, g0, q1, k1p, v1p, q2, k2a, v2a, k2b, v2b,
                  att_ref, w_ref, sums_ref,
                  a1s, m1s, s1s, a2s, m2s, s2s, atts, ws):
    h = pl.program_id(0)
    n0 = atts.shape[0]
    n2 = a2s.shape[0]

    def put(a_ref, m_ref, s_ref, a, m, s):
        a_ref[...] = a
        m_ref[...] = jnp.broadcast_to(m, a.shape)
        s_ref[...] = jnp.broadcast_to(s, a.shape)

    s = _nt(q1[...], k1p[...]) * SCALE
    m = s.max(-1, keepdims=True)
    e = jnp.exp(s - m)
    put(a1s, m1s, s1s, _nn(e.astype(BF16), v1p[...]), m, e.sum(-1, keepdims=True))

    qv = q2[...]
    sa = _nt(qv, k2a[...]) * SCALE
    sb = _nt(qv, k2b[...]) * SCALE
    m = jnp.maximum(sa.max(-1, keepdims=True), sb.max(-1, keepdims=True))
    ea = jnp.exp(sa - m)
    eb = jnp.exp(sb - m)
    a = _nn(ea.astype(BF16), v2a[...]) + _nn(eb.astype(BF16), v2b[...])
    put(a2s, m2s, s2s, a, m, ea.sum(-1, keepdims=True) + eb.sum(-1, keepdims=True))

    lane = _lanes((n2, DH))
    for j in range(4):
        r0 = pl.ds(j, n2, stride=4)
        r1 = pl.ds(j >> 1, n2, stride=2)
        ms = ms0[r0, :]
        mm0 = ms[:, 0:1]
        mm1 = m1s[r1, :]
        mm2 = m2s[...]
        top = jnp.maximum(jnp.maximum(mm0, mm1), mm2)
        f0 = jnp.exp(mm0 - top)
        f1 = 2.0 * jnp.exp(mm1 - top)
        f2 = 4.0 * jnp.exp(mm2 - top)
        den = f0 * ms[:, 1:2] + f1 * s1s[r1, :] + f2 * s2s[...]
        num = f0 * a0[r0, :] + f1 * a1s[r1, :] + f2 * a2s[...]
        atts[r0, :] = (num / den).astype(BF16).astype(F32)
        ws[r0, :] = jnp.where(
            lane == 0, f0 / den, jnp.where(lane == 1, f1 / den, jnp.where(lane == 2, f2 / den, 0.0))
        )
    attv = atts[...]
    att_ref[...] = attv.astype(BF16)
    w_ref[...] = ws[...]
    gf = g0[...].astype(F32)
    sq = (attv * attv).sum(-1, keepdims=True)
    dt = (gf * attv).sum(-1, keepdims=True)
    part = jnp.where(_lanes((n0, 2)) == 0, sq, dt)

    @pl.when(h == 0)
    def _():
        sums_ref[...] = part

    @pl.when(h > 0)
    def _():
        sums_ref[...] += part


def _level_grads(g0, att, w, mine, theirs, t_s, u_s):
    n0 = t_s.shape[0]
    n1 = n0 // 2
    n2 = n0 // 4
    full_width = 2 * 4 * DH
    totals = mine[...] + theirs[...]
    inv = lax.rsqrt(totals[:, 0:1] / full_width + EPSILON)
    coef = inv * inv * inv * totals[:, 1:2] / full_width
    attv = att[...].astype(F32)
    gf = g0[...].astype(F32)
    ga = inv * gf - coef * attv
    rt = (ga * attv).sum(-1, keepdims=True)
    wv = w[...]
    w0 = wv[:, 0:1]
    w1 = wv[:, 1:2]
    w2 = wv[:, 2:3]
    gl0 = (w0 * ga).astype(BF16)
    dl0 = w0 * rt
    t_s[...] = w1 * ga
    u_s[...] = jnp.broadcast_to(w1 * rt, (n0, DH))
    e_rows = pl.ds(0, n1, stride=2)
    o_rows = pl.ds(1, n1, stride=2)
    gl1 = (t_s[e_rows, :] + t_s[o_rows, :]).astype(BF16)
    dl1 = u_s[e_rows, :] + u_s[o_rows, :]
    t_s[...] = w2 * ga
    u_s[...] = jnp.broadcast_to(w2 * rt, (n0, DH))
    rows = [pl.ds(j, n2, stride=4) for j in range(4)]
    gl2 = (((t_s[rows[0], :] + t_s[rows[1], :]) + t_s[rows[2], :]) + t_s[rows[3], :]).astype(BF16)
    dl2 = ((u_s[rows[0], :] + u_s[rows[1], :]) + u_s[rows[2], :]) + u_s[rows[3], :]
    return inv, attv, gl0, dl0, gl1, dl1, gl2, dl2


def _split3(x):
    hi = x.astype(BF16).astype(F32)
    rest = x - hi
    mid = rest.astype(BF16).astype(F32)
    return hi, mid, rest - mid


def _coded(pieces):
    sub = lax.broadcasted_iota(jnp.int32, (16, DH), 0)
    out = jnp.zeros((16, DH), F32)
    for i, piece in enumerate(pieces):
        out = jnp.where(sub == i, piece, out)
    return out.astype(BF16)


def _bwd1_kernel(g0, att, w, mine, theirs, q1, q2, b1_ref, b2_ref, t_s, u_s):
    _, _, _, _, gl1, dl1, gl2, dl2 = _level_grads(g0, att, w, mine, theirs, t_s, u_s)
    n1 = gl1.shape[0]
    n2 = gl2.shape[0]
    b1_ref[0:n1, :] = gl1
    b2_ref[0:n2, :] = gl2
    t1 = dl1.T
    a_parts = _split3(t1[0:1, 0:DH])
    b_parts = _split3(t1[0:1, DH:2 * DH])
    b1_ref[n1:n1 + 16, :] = _coded([a_parts[0], b_parts[0], a_parts[1], b_parts[1], a_parts[2], b_parts[2]])
    b2_ref[n2:n2 + 16, :] = _coded(list(_split3(dl2.T[0:1, :])))
    b1_ref[n1 + 16:, :] = q1[...]
    b2_ref[n2 + 16:, :] = q2[...]


def _bwd2_kernel(q0, k0, v0, g0, att, w, mine, theirs, q1, k1p, v1p, q2, k2a, v2a, k2b, v2b,
                 norm_ref, gq_ref, dk0_ref, dv0_ref,
                 t_s, u_s, dq0s, dq1s, dq2s, outs):
    n2 = dq2s.shape[0]
    inv, attv, gl0, dl0, gl1, dl1, gl2, dl2 = _level_grads(g0, att, w, mine, theirs, t_s, u_s)
    norm_ref[...] = (attv * inv).astype(BF16)
    q0v = q0[...]
    k0v = k0[...]
    v0v = v0[...]
    s = _nt(q0v, k0v) * SCALE
    m = s.max(-1, keepdims=True)
    e = jnp.exp(s - m)
    p = e.astype(BF16)
    ds = (e * (_nt(gl0, v0v) - dl0)).astype(BF16)
    dq0s[...] = _nn(ds, k0v) * SCALE
    dk0_ref[...] = _tn(ds, q0v) * SCALE
    dv0_ref[...] = _tn(p, gl0)

    kv = k1p[...]
    s = _nt(q1[...], kv) * SCALE
    m = s.max(-1, keepdims=True)
    e = jnp.exp(s - m)
    ds = (e * (_nt(gl1, v1p[...]) - dl1[:, 0:1])).astype(BF16)
    dq1s[...] = _nn(ds, kv) * SCALE

    qv = q2[...]
    ka = k2a[...]
    kb = k2b[...]
    sa = _nt(qv, ka) * SCALE
    sb = _nt(qv, kb) * SCALE
    m = jnp.maximum(sa.max(-1, keepdims=True), sb.max(-1, keepdims=True))
    ea = jnp.exp(sa - m)
    eb = jnp.exp(sb - m)
    d2c = dl2[:, 0:1]
    dsa = (ea * (_nt(gl2, v2a[...]) - d2c)).astype(BF16)
    dsb = (eb * (_nt(gl2, v2b[...]) - d2c)).astype(BF16)
    dq2s[...] = (_nn(dsa, ka) + _nn(dsb, kb)) * SCALE

    for j in range(4):
        r0 = pl.ds(j, n2, stride=4)
        r1 = pl.ds(j >> 1, n2, stride=2)
        outs[r0, :] = dq0s[r0, :] + dq1s[r1, :] * 0.5 + dq2s[...] * 0.25
    gq_ref[...] = outs[...].astype(BF16)


def _own_kernel(k1o, v1o, k1p, b1p, k2o, v2o, b2a, b2b, dk0, dv0,
                gk_ref, gv_ref, wide, dk1s, dv1s, dk2s, dv2s, outk, outv):
    n1 = dk1s.shape[0]
    n2 = dk2s.shape[0]
    qv = b1p[n1 + 16:, :]
    gv = b1p[0:n1, :]
    x = b1p[n1:n1 + 16, :].astype(F32)
    d_row = jnp.concatenate([(x[0:1] + x[2:3]) + x[4:5], (x[1:2] + x[3:4]) + x[5:6]], axis=1)
    st = _nt(k1o[...], qv) * SCALE
    m = st.max(0, keepdims=True)
    e = jnp.exp(st - m)
    p = e.astype(BF16)
    ds = (e * (_nt(v1o[...], gv) - d_row)).astype(BF16)
    dk1s[...] = _nn(ds, qv) * SCALE
    dv1s[...] = _nn(p, gv)

    wide[...] = k1p[...].astype(F32)
    ks = ((wide[pl.ds(0, n2, stride=2), :] + wide[pl.ds(1, n2, stride=2), :]) * 0.5).astype(BF16)
    ko = k2o[...]
    vo = v2o[...]
    dks = []
    dvs = []
    for b_ref in (b2a, b2b):
        qv = b_ref[n2 + 16:, :]
        gv = b_ref[0:n2, :]
        x = b_ref[n2:n2 + 16, :].astype(F32)
        d_row = (x[0:1] + x[1:2]) + x[2:3]
        so = _nt(ko, qv) * SCALE
        ss = _nt(ks, qv) * SCALE
        m = jnp.maximum(so.max(0, keepdims=True), ss.max(0, keepdims=True))
        e = jnp.exp(so - m)
        p = e.astype(BF16)
        ds = (e * (_nt(vo, gv) - d_row)).astype(BF16)
        dks.append(_nn(ds, qv))
        dvs.append(_nn(p, gv))
    dk2s[...] = (dks[0] + dks[1]) * SCALE
    dv2s[...] = dvs[0] + dvs[1]

    for j in range(4):
        r0 = pl.ds(j, n2, stride=4)
        r1 = pl.ds(j >> 1, n2, stride=2)
        outk[r0, :] = dk0[r0, :] + dk1s[r1, :] * 0.5 + dk2s[...] * 0.25
        outv[r0, :] = dv0[r0, :] + dv1s[r1, :] * 0.5 + dv2s[...] * 0.25
    gk_ref[...] = outk[...].astype(BF16)
    gv_ref[...] = outv[...].astype(BF16)


def _cols(rows):
    return pl.BlockSpec((rows, DH), lambda h: (0, h))


def _stacked(rows, index):
    return pl.BlockSpec((None, rows, DH), lambda h: (index, 0, h))


def _per_head(rows, width):
    return pl.BlockSpec((None, rows, width), lambda h: (h, 0, 0))


def _whole(rows, width):
    return pl.BlockSpec((rows, width), lambda h: (0, 0))


def _params():
    return pltpu.CompilerParams(dimension_semantics=("arbitrary",))


def _full3(rows, width):
    return pl.BlockSpec((2, rows, width), lambda h: (0, 0, 0))


def _two(rows):
    return pl.BlockSpec((2, rows, DH), lambda h: (0, 0, h))


def shards(queries, key_states, value_states, out_grad):
    n0, width = queries.shape
    heads = width // DH
    n1 = n0 // 2
    n2 = n0 // 4
    q0, k0, v0, g0 = queries, key_states, value_states, out_grad
    s1, q1, s2, q2 = pl.pallas_call(
        _halve_kernel,
        grid=(1,),
        in_specs=[_whole(n0, width), _whole(n0, width), _whole(n0, width)],
        out_specs=[_full3(n1, width), _whole(n1, width), _full3(n2, width), _whole(n2, width)],
        out_shape=[
            jax.ShapeDtypeStruct((2, n1, width), BF16),
            jax.ShapeDtypeStruct((n1, width), BF16),
            jax.ShapeDtypeStruct((2, n2, width), BF16),
            jax.ShapeDtypeStruct((n2, width), BF16),
        ],
        scratch_shapes=[pltpu.VMEM((n0, DH), F32), pltpu.VMEM((n1, DH), F32)],
        compiler_params=_params(),
    )(q0, k0, v0)
    r1 = from_partner(s1, 1)
    r2a = from_partner(s2, 2)
    r2b = from_partner(s2, 3)

    a0, ms0 = pl.pallas_call(
        _fwd0_kernel,
        grid=(heads,),
        in_specs=[_cols(n0), _cols(n0), _cols(n0)],
        out_specs=[_cols(n0), _per_head(n0, DH)],
        out_shape=[
            jax.ShapeDtypeStruct((n0, width), F32),
            jax.ShapeDtypeStruct((heads, n0, DH), F32),
        ],
        compiler_params=_params(),
    )(q0, k0, v0)

    att, w, sums = pl.pallas_call(
        _fwd12_kernel,
        grid=(heads,),
        in_specs=[
            _cols(n0), _per_head(n0, DH), _cols(n0),
            _cols(n1), _stacked(n1, 0), _stacked(n1, 1),
            _cols(n2), _stacked(n2, 0), _stacked(n2, 1), _stacked(n2, 0), _stacked(n2, 1),
        ],
        out_specs=[_cols(n0), _per_head(n0, DH), _whole(n0, 2)],
        out_shape=[
            jax.ShapeDtypeStruct((n0, width), BF16),
            jax.ShapeDtypeStruct((heads, n0, DH), F32),
            jax.ShapeDtypeStruct((n0, 2), F32),
        ],
        scratch_shapes=[pltpu.VMEM((n, DH), F32) for n in (n1, n1, n1, n2, n2, n2, n0, n0)],
        compiler_params=_params(),
    )(a0, ms0, g0, q1, r1, r1, q2, r2a, r2a, r2b, r2b)

    assert width * lax.axis_size("head") == 2 * 4 * DH
    other = lax.ppermute(sums, "head", [(0, 1), (1, 0)])

    b1, b2 = pl.pallas_call(
        _bwd1_kernel,
        grid=(heads,),
        in_specs=[_cols(n0), _cols(n0), _per_head(n0, DH), _whole(n0, 2), _whole(n0, 2), _cols(n1), _cols(n2)],
        out_specs=[_cols(2 * n1 + 16), _cols(2 * n2 + 16)],
        out_shape=[
            jax.ShapeDtypeStruct((2 * n1 + 16, width), BF16),
            jax.ShapeDtypeStruct((2 * n2 + 16, width), BF16),
        ],
        scratch_shapes=[pltpu.VMEM((n0, DH), F32), pltpu.VMEM((n0, DH), F32)],
        compiler_params=_params(),
    )(g0, att, w, sums, other, q1, q2)
    b1p = from_partner(b1, 1)
    b2a = from_partner(b2, 2)
    b2b = from_partner(b2, 3)

    norm, gq, dk0, dv0 = pl.pallas_call(
        _bwd2_kernel,
        grid=(heads,),
        in_specs=[
            _cols(n0), _cols(n0), _cols(n0), _cols(n0), _cols(n0), _per_head(n0, DH),
            _whole(n0, 2), _whole(n0, 2),
            _cols(n1), _stacked(n1, 0), _stacked(n1, 1),
            _cols(n2), _stacked(n2, 0), _stacked(n2, 1), _stacked(n2, 0), _stacked(n2, 1),
        ],
        out_specs=[_cols(n0), _cols(n0), _cols(n0), _cols(n0)],
        out_shape=[
            jax.ShapeDtypeStruct((n0, width), BF16),
            jax.ShapeDtypeStruct((n0, width), BF16),
            jax.ShapeDtypeStruct((n0, width), F32),
            jax.ShapeDtypeStruct((n0, width), F32),
        ],
        scratch_shapes=[pltpu.VMEM((n, DH), F32) for n in (n0, n0, n0, n1, n2, n0)],
        compiler_params=_params(),
    )(q0, k0, v0, g0, att, w, sums, other, q1, r1, r1, q2, r2a, r2a, r2b, r2b)

    gk, gv = pl.pallas_call(
        _own_kernel,
        grid=(heads,),
        in_specs=[
            _stacked(n1, 0), _stacked(n1, 1), _stacked(n1, 0), _cols(2 * n1 + 16),
            _stacked(n2, 0), _stacked(n2, 1), _cols(2 * n2 + 16), _cols(2 * n2 + 16),
            _cols(n0), _cols(n0),
        ],
        out_specs=[_cols(n0), _cols(n0)],
        out_shape=[
            jax.ShapeDtypeStruct((n0, width), BF16),
            jax.ShapeDtypeStruct((n0, width), BF16),
        ],
        scratch_shapes=[pltpu.VMEM((n, DH), F32) for n in (n1, n1, n1, n2, n2, n0, n0)],
        compiler_params=_params(),
    )(s1, s1, r1, b1p, s2, s2, b2a, b2b, dk0, dv0)
    return (norm, gq, gk, gv)


def solution(mesh):
    return jax.shard_map(
        shards,
        mesh=mesh,
        in_specs=(P("seq", "head"), P("seq", "head"), P("seq", "head"), P("seq", "head")),
        out_specs=(P("seq", "head"), P("seq", "head"), P("seq", "head"), P("seq", "head")),
        check_vma=False,
    )
```

```python
import jax
import jax.numpy as jnp
from jax import lax
from jax.experimental import pallas as pl
from jax.experimental.pallas import tpu as pltpu
from jax.sharding import PartitionSpec as P

DH = 128
LEAF = 256
LEVELS = 3
EPSILON = 1e-06
SCALE = DH ** (-0.5)
F32 = jnp.float32
BF16 = jnp.bfloat16


def from_partner(value, mask):
    pairs = [(source, source ^ mask) for source in range(lax.axis_size("seq"))]
    return lax.ppermute(value, "seq", pairs)


def halving(source):
    widened = source.astype(F32)
    paired = widened.reshape(widened.shape[:-2] + (widened.shape[-2] // 2, 2, widened.shape[-1]))
    return ((paired[..., 0, :] + paired[..., 1, :]) * 0.5).astype(BF16)


def _nt(a, b):
    return lax.dot_general(a, b, (((1,), (1,)), ((), ())), preferred_element_type=F32)


def _nn(a, b):
    return lax.dot_general(a, b, (((1,), (0,)), ((), ())), preferred_element_type=F32)


def _tn(a, b):
    return lax.dot_general(a, b, (((0,), (0,)), ((), ())), preferred_element_type=F32)


def _lanes(shape):
    return lax.broadcasted_iota(jnp.int32, shape, len(shape) - 1)


def _halve_kernel(q0, k0, v0, s1_ref, q1_ref, s2_ref, q2_ref, wide, half):
    n1 = half.shape[0]
    n2 = n1 // 2
    for h in range(q0.shape[1] // DH):
        cols = slice(h * DH, (h + 1) * DH)
        for i, src in enumerate((k0, v0, q0)):
            wide[...] = src[:, cols].astype(F32)
            h1 = ((wide[pl.ds(0, n1, stride=2), :] + wide[pl.ds(1, n1, stride=2), :]) * 0.5).astype(BF16)
            half[...] = h1.astype(F32)
            h2 = ((half[pl.ds(0, n2, stride=2), :] + half[pl.ds(1, n2, stride=2), :]) * 0.5).astype(BF16)
            if i < 2:
                s1_ref[i, :, cols] = h1
                s2_ref[i, :, cols] = h2
            else:
                q1_ref[:, cols] = h1
                q2_ref[:, cols] = h2


def _fwd0_kernel(q0, k0, v0, a0_ref, ms_ref):
    s = _nt(q0[...], k0[...]) * SCALE
    m = s.max(-1, keepdims=True)
    e = jnp.exp(s - m)
    a0_ref[...] = _nn(e.astype(BF16), v0[...])
    lane = _lanes(ms_ref.shape)
    ms_ref[...] = jnp.where(lane == 0, m, jnp.where(lane == 1, e.sum(-1, keepdims=True), 0.0))


def _fwd12_kernel(a0, ms0, g0, q1, k1p, v1p, q2, k2a, v2a, k2b, v2b,
                  att_ref, w_ref, sums_ref,
                  a1s, m1s, s1s, a2s, m2s, s2s, atts, ws):
    h = pl.program_id(0)
    n0 = atts.shape[0]
    n2 = a2s.shape[0]

    def put(a_ref, m_ref, s_ref, a, m, s):
        a_ref[...] = a
        m_ref[...] = jnp.broadcast_to(m, a.shape)
        s_ref[...] = jnp.broadcast_to(s, a.shape)

    s = _nt(q1[...], k1p[...]) * SCALE
    m = s.max(-1, keepdims=True)
    e = jnp.exp(s - m)
    put(a1s, m1s, s1s, _nn(e.astype(BF16), v1p[...]), m, e.sum(-1, keepdims=True))

    qv = q2[...]
    sa = _nt(qv, k2a[...]) * SCALE
    sb = _nt(qv, k2b[...]) * SCALE
    m = jnp.maximum(sa.max(-1, keepdims=True), sb.max(-1, keepdims=True))
    ea = jnp.exp(sa - m)
    eb = jnp.exp(sb - m)
    a = _nn(ea.astype(BF16), v2a[...]) + _nn(eb.astype(BF16), v2b[...])
    put(a2s, m2s, s2s, a, m, ea.sum(-1, keepdims=True) + eb.sum(-1, keepdims=True))

    lane = _lanes((n2, DH))
    for j in range(4):
        r0 = pl.ds(j, n2, stride=4)
        r1 = pl.ds(j >> 1, n2, stride=2)
        ms = ms0[r0, :]
        mm0 = ms[:, 0:1]
        mm1 = m1s[r1, :]
        mm2 = m2s[...]
        top = jnp.maximum(jnp.maximum(mm0, mm1), mm2)
        f0 = jnp.exp(mm0 - top)
        f1 = 2.0 * jnp.exp(mm1 - top)
        f2 = 4.0 * jnp.exp(mm2 - top)
        den = f0 * ms[:, 1:2] + f1 * s1s[r1, :] + f2 * s2s[...]
        num = f0 * a0[r0, :] + f1 * a1s[r1, :] + f2 * a2s[...]
        atts[r0, :] = (num / den).astype(BF16).astype(F32)
        ws[r0, :] = jnp.where(
            lane == 0, f0 / den, jnp.where(lane == 1, f1 / den, jnp.where(lane == 2, f2 / den, 0.0))
        )
    attv = atts[...]
    att_ref[...] = attv.astype(BF16)
    w_ref[...] = ws[...]
    gf = g0[...].astype(F32)
    sq = (attv * attv).sum(-1, keepdims=True)
    dt = (gf * attv).sum(-1, keepdims=True)
    lane0 = _lanes((n0, DH))
    part = jnp.where(lane0 == 0, sq, jnp.where(lane0 == 1, dt, 0.0))

    @pl.when(h == 0)
    def _():
        sums_ref[...] = part

    @pl.when(h > 0)
    def _():
        sums_ref[...] += part


def _level_grads(g0, att, w, mine, theirs, t_s, u_s):
    n0 = t_s.shape[0]
    n1 = n0 // 2
    n2 = n0 // 4
    full_width = 2 * 4 * DH
    totals = mine[:, 0:2] + theirs[:, 0:2]
    inv = lax.rsqrt(totals[:, 0:1] / full_width + EPSILON)
    coef = inv * inv * inv * totals[:, 1:2] / full_width
    attv = att[...].astype(F32)
    gf = g0[...].astype(F32)
    ga = inv * gf - coef * attv
    rt = (ga * attv).sum(-1, keepdims=True)
    wv = w[...]
    w0 = wv[:, 0:1]
    w1 = wv[:, 1:2]
    w2 = wv[:, 2:3]
    gl0 = (w0 * ga).astype(BF16)
    dl0 = w0 * rt
    t_s[...] = w1 * ga
    u_s[...] = jnp.broadcast_to(w1 * rt, (n0, DH))
    e_rows = pl.ds(0, n1, stride=2)
    o_rows = pl.ds(1, n1, stride=2)
    gl1 = (t_s[e_rows, :] + t_s[o_rows, :]).astype(BF16)
    dl1 = u_s[e_rows, :] + u_s[o_rows, :]
    t_s[...] = w2 * ga
    u_s[...] = jnp.broadcast_to(w2 * rt, (n0, DH))
    rows = [pl.ds(j, n2, stride=4) for j in range(4)]
    gl2 = (((t_s[rows[0], :] + t_s[rows[1], :]) + t_s[rows[2], :]) + t_s[rows[3], :]).astype(BF16)
    dl2 = ((u_s[rows[0], :] + u_s[rows[1], :]) + u_s[rows[2], :]) + u_s[rows[3], :]
    return inv, attv, gl0, dl0, gl1, dl1, gl2, dl2


def _split3(x):
    hi = x.astype(BF16).astype(F32)
    rest = x - hi
    mid = rest.astype(BF16).astype(F32)
    return hi, mid, rest - mid


def _coded(pieces):
    sub = lax.broadcasted_iota(jnp.int32, (16, DH), 0)
    out = jnp.zeros((16, DH), F32)
    for i, piece in enumerate(pieces):
        out = jnp.where(sub == i, piece, out)
    return out.astype(BF16)


def _bwd1_kernel(g0, att, w, mine, theirs, q1, q2, norm_ref, b1_ref, b2_ref, t_s, u_s):
    for h in range(g0.shape[1] // DH):
        cols = slice(h * DH, (h + 1) * DH)
        _bwd1_head(g0.at[:, cols], att.at[:, cols], w.at[h], mine, theirs, q1.at[:, cols], q2.at[:, cols],
                   norm_ref.at[:, cols], b1_ref.at[:, cols], b2_ref.at[:, cols], t_s, u_s)


def _bwd1_head(g0, att, w, mine, theirs, q1, q2, norm_ref, b1_ref, b2_ref, t_s, u_s):
    inv, attv, _, _, gl1, dl1, gl2, dl2 = _level_grads(g0, att, w, mine, theirs, t_s, u_s)
    n1 = gl1.shape[0]
    n2 = gl2.shape[0]
    norm_ref[...] = (attv * inv).astype(BF16)
    b1_ref[0:n1, :] = gl1
    b2_ref[0:n2, :] = gl2
    t1 = dl1.T
    a_parts = _split3(t1[0:1, 0:DH])
    b_parts = _split3(t1[0:1, DH:2 * DH])
    b1_ref[n1:n1 + 16, :] = _coded([a_parts[0], b_parts[0], a_parts[1], b_parts[1], a_parts[2], b_parts[2]])
    b2_ref[n2:n2 + 16, :] = _coded(list(_split3(dl2.T[0:1, :])))
    b1_ref[n1 + 16:, :] = q1[...]
    b2_ref[n2 + 16:, :] = q2[...]


def _bwd2_kernel(q0, k0, v0, g0, att, w, mine, theirs, q1, k1p, v1p, q2, k2a, v2a, k2b, v2b,
                 gq_ref, dk0_ref, dv0_ref,
                 t_s, u_s, dq0s, dq1s, dq2s, outs):
    n2 = dq2s.shape[0]
    _, _, gl0, dl0, gl1, dl1, gl2, dl2 = _level_grads(g0, att, w, mine, theirs, t_s, u_s)
    q0v = q0[...]
    k0v = k0[...]
    v0v = v0[...]
    s = _nt(q0v, k0v) * SCALE
    m = s.max(-1, keepdims=True)
    e = jnp.exp(s - m)
    p = e.astype(BF16)
    ds = (e * (_nt(gl0, v0v) - dl0)).astype(BF16)
    dq0s[...] = _nn(ds, k0v) * SCALE
    dk0_ref[...] = _tn(ds, q0v) * SCALE
    dv0_ref[...] = _tn(p, gl0)

    kv = k1p[...]
    s = _nt(q1[...], kv) * SCALE
    m = s.max(-1, keepdims=True)
    e = jnp.exp(s - m)
    ds = (e * (_nt(gl1, v1p[...]) - dl1[:, 0:1])).astype(BF16)
    dq1s[...] = _nn(ds, kv) * SCALE

    qv = q2[...]
    ka = k2a[...]
    kb = k2b[...]
    sa = _nt(qv, ka) * SCALE
    sb = _nt(qv, kb) * SCALE
    m = jnp.maximum(sa.max(-1, keepdims=True), sb.max(-1, keepdims=True))
    ea = jnp.exp(sa - m)
    eb = jnp.exp(sb - m)
    d2c = dl2[:, 0:1]
    dsa = (ea * (_nt(gl2, v2a[...]) - d2c)).astype(BF16)
    dsb = (eb * (_nt(gl2, v2b[...]) - d2c)).astype(BF16)
    dq2s[...] = (_nn(dsa, ka) + _nn(dsb, kb)) * SCALE

    for j in range(4):
        r0 = pl.ds(j, n2, stride=4)
        r1 = pl.ds(j >> 1, n2, stride=2)
        outs[r0, :] = dq0s[r0, :] + dq1s[r1, :] * 0.5 + dq2s[...] * 0.25
    gq_ref[...] = outs[...].astype(BF16)


def _own_kernel(k1o, v1o, k1p, b1p, k2o, v2o, b2a, b2b, dk0, dv0,
                gk_ref, gv_ref, wide, dk1s, dv1s, dk2s, dv2s, outk, outv):
    n1 = dk1s.shape[0]
    n2 = dk2s.shape[0]
    qv = b1p[n1 + 16:, :]
    gv = b1p[0:n1, :]
    x = b1p[n1:n1 + 16, :].astype(F32)
    d_row = jnp.concatenate([(x[0:1] + x[2:3]) + x[4:5], (x[1:2] + x[3:4]) + x[5:6]], axis=1)
    st = _nt(k1o[...], qv) * SCALE
    m = st.max(0, keepdims=True)
    e = jnp.exp(st - m)
    p = e.astype(BF16)
    ds = (e * (_nt(v1o[...], gv) - d_row)).astype(BF16)
    dk1s[...] = _nn(ds, qv) * SCALE
    dv1s[...] = _nn(p, gv)

    wide[...] = k1p[...].astype(F32)
    ks = ((wide[pl.ds(0, n2, stride=2), :] + wide[pl.ds(1, n2, stride=2), :]) * 0.5).astype(BF16)
    ko = k2o[...]
    vo = v2o[...]
    dks = []
    dvs = []
    for b_ref in (b2a, b2b):
        qv = b_ref[n2 + 16:, :]
        gv = b_ref[0:n2, :]
        x = b_ref[n2:n2 + 16, :].astype(F32)
        d_row = (x[0:1] + x[1:2]) + x[2:3]
        so = _nt(ko, qv) * SCALE
        ss = _nt(ks, qv) * SCALE
        m = jnp.maximum(so.max(0, keepdims=True), ss.max(0, keepdims=True))
        e = jnp.exp(so - m)
        p = e.astype(BF16)
        ds = (e * (_nt(vo, gv) - d_row)).astype(BF16)
        dks.append(_nn(ds, qv))
        dvs.append(_nn(p, gv))
    dk2s[...] = (dks[0] + dks[1]) * SCALE
    dv2s[...] = dvs[0] + dvs[1]

    for j in range(4):
        r0 = pl.ds(j, n2, stride=4)
        r1 = pl.ds(j >> 1, n2, stride=2)
        outk[r0, :] = dk0[r0, :] + dk1s[r1, :] * 0.5 + dk2s[...] * 0.25
        outv[r0, :] = dv0[r0, :] + dv1s[r1, :] * 0.5 + dv2s[...] * 0.25
    gk_ref[...] = outk[...].astype(BF16)
    gv_ref[...] = outv[...].astype(BF16)


def _cols(rows):
    return pl.BlockSpec((rows, DH), lambda h: (0, h))


def _stacked(rows, index):
    return pl.BlockSpec((None, rows, DH), lambda h: (index, 0, h))


def _per_head(rows, width):
    return pl.BlockSpec((None, rows, width), lambda h: (h, 0, 0))


def _whole(rows, width):
    return pl.BlockSpec((rows, width), lambda h: (0, 0))


def _params():
    return pltpu.CompilerParams(dimension_semantics=("arbitrary",))


def _full3(rows, width):
    return pl.BlockSpec((2, rows, width), lambda h: (0, 0, 0))


def _two(rows):
    return pl.BlockSpec((2, rows, DH), lambda h: (0, 0, h))


def shards(queries, key_states, value_states, out_grad):
    n0, width = queries.shape
    heads = width // DH
    n1 = n0 // 2
    n2 = n0 // 4
    q0, k0, v0, g0 = queries, key_states, value_states, out_grad
    s1, q1, s2, q2 = pl.pallas_call(
        _halve_kernel,
        grid=(1,),
        in_specs=[_whole(n0, width), _whole(n0, width), _whole(n0, width)],
        out_specs=[_full3(n1, width), _whole(n1, width), _full3(n2, width), _whole(n2, width)],
        out_shape=[
            jax.ShapeDtypeStruct((2, n1, width), BF16),
            jax.ShapeDtypeStruct((n1, width), BF16),
            jax.ShapeDtypeStruct((2, n2, width), BF16),
            jax.ShapeDtypeStruct((n2, width), BF16),
        ],
        scratch_shapes=[pltpu.VMEM((n0, DH), F32), pltpu.VMEM((n1, DH), F32)],
        compiler_params=_params(),
    )(q0, k0, v0)
    r1 = from_partner(s1, 1)
    r2a = from_partner(s2, 2)
    r2b = from_partner(s2, 3)

    a0, ms0 = pl.pallas_call(
        _fwd0_kernel,
        grid=(heads,),
        in_specs=[_cols(n0), _cols(n0), _cols(n0)],
        out_specs=[_cols(n0), _per_head(n0, DH)],
        out_shape=[
            jax.ShapeDtypeStruct((n0, width), F32),
            jax.ShapeDtypeStruct((heads, n0, DH), F32),
        ],
        compiler_params=_params(),
    )(q0, k0, v0)

    att, w, sums = pl.pallas_call(
        _fwd12_kernel,
        grid=(heads,),
        in_specs=[
            _cols(n0), _per_head(n0, DH), _cols(n0),
            _cols(n1), _stacked(n1, 0), _stacked(n1, 1),
            _cols(n2), _stacked(n2, 0), _stacked(n2, 1), _stacked(n2, 0), _stacked(n2, 1),
        ],
        out_specs=[_cols(n0), _per_head(n0, DH), _whole(n0, DH)],
        out_shape=[
            jax.ShapeDtypeStruct((n0, width), BF16),
            jax.ShapeDtypeStruct((heads, n0, DH), F32),
            jax.ShapeDtypeStruct((n0, DH), F32),
        ],
        scratch_shapes=[pltpu.VMEM((n, DH), F32) for n in (n1, n1, n1, n2, n2, n2, n0, n0)],
        compiler_params=_params(),
    )(a0, ms0, g0, q1, r1, r1, q2, r2a, r2a, r2b, r2b)

    assert width * lax.axis_size("head") == 2 * 4 * DH
    other = lax.ppermute(sums, "head", [(0, 1), (1, 0)])

    norm, b1, b2 = pl.pallas_call(
        _bwd1_kernel,
        grid=(1,),
        in_specs=[
            _whole(n0, width), _whole(n0, width), pl.BlockSpec((heads, n0, DH), lambda h: (0, 0, 0)),
            _whole(n0, DH), _whole(n0, DH), _whole(n1, width), _whole(n2, width),
        ],
        out_specs=[_whole(n0, width), _whole(2 * n1 + 16, width), _whole(2 * n2 + 16, width)],
        out_shape=[
            jax.ShapeDtypeStruct((n0, width), BF16),
            jax.ShapeDtypeStruct((2 * n1 + 16, width), BF16),
            jax.ShapeDtypeStruct((2 * n2 + 16, width), BF16),
        ],
        scratch_shapes=[pltpu.VMEM((n0, DH), F32), pltpu.VMEM((n0, DH), F32)],
        compiler_params=_params(),
    )(g0, att, w, sums, other, q1, q2)
    b1p = from_partner(b1, 1)
    b2a = from_partner(b2, 2)
    b2b = from_partner(b2, 3)

    gq, dk0, dv0 = pl.pallas_call(
        _bwd2_kernel,
        grid=(heads,),
        in_specs=[
            _cols(n0), _cols(n0), _cols(n0), _cols(n0), _cols(n0), _per_head(n0, DH),
            _whole(n0, DH), _whole(n0, DH),
            _cols(n1), _stacked(n1, 0), _stacked(n1, 1),
            _cols(n2), _stacked(n2, 0), _stacked(n2, 1), _stacked(n2, 0), _stacked(n2, 1),
        ],
        out_specs=[_cols(n0), _cols(n0), _cols(n0)],
        out_shape=[
            jax.ShapeDtypeStruct((n0, width), BF16),
            jax.ShapeDtypeStruct((n0, width), F32),
            jax.ShapeDtypeStruct((n0, width), F32),
        ],
        scratch_shapes=[pltpu.VMEM((n, DH), F32) for n in (n0, n0, n0, n1, n2, n0)],
        compiler_params=_params(),
    )(q0, k0, v0, g0, att, w, sums, other, q1, r1, r1, q2, r2a, r2a, r2b, r2b)

    gk, gv = pl.pallas_call(
        _own_kernel,
        grid=(heads,),
        in_specs=[
            _stacked(n1, 0), _stacked(n1, 1), _stacked(n1, 0), _cols(2 * n1 + 16),
            _stacked(n2, 0), _stacked(n2, 1), _cols(2 * n2 + 16), _cols(2 * n2 + 16),
            _cols(n0), _cols(n0),
        ],
        out_specs=[_cols(n0), _cols(n0)],
        out_shape=[
            jax.ShapeDtypeStruct((n0, width), BF16),
            jax.ShapeDtypeStruct((n0, width), BF16),
        ],
        scratch_shapes=[pltpu.VMEM((n, DH), F32) for n in (n1, n1, n1, n2, n2, n0, n0)],
        compiler_params=_params(),
    )(s1, s1, r1, b1p, s2, s2, b2a, b2b, dk0, dv0)
    return (norm, gq, gk, gv)


def solution(mesh):
    return jax.shard_map(
        shards,
        mesh=mesh,
        in_specs=(P("seq", "head"), P("seq", "head"), P("seq", "head"), P("seq", "head")),
        out_specs=(P("seq", "head"), P("seq", "head"), P("seq", "head"), P("seq", "head")),
        check_vma=False,
    )
```

```python
import jax
import jax.numpy as jnp
from jax import lax
from jax.experimental import pallas as pl
from jax.experimental.pallas import tpu as pltpu
from jax.sharding import PartitionSpec as P


DH = 128
EPSILON = 1e-06
SCALE = DH ** (-0.5)
F32 = jnp.float32
BF16 = jnp.bfloat16


def from_partner(value, mask):
    pairs = [(source, source ^ mask) for source in range(lax.axis_size("seq"))]
    return lax.ppermute(value, "seq", pairs)


def _nt(a, b):
    return lax.dot_general(a, b, (((1,), (1,)), ((), ())), preferred_element_type=F32)


def _nn(a, b):
    return lax.dot_general(a, b, (((1,), (0,)), ((), ())), preferred_element_type=F32)


def _tn(a, b):
    return lax.dot_general(a, b, (((0,), (0,)), ((), ())), preferred_element_type=F32)


def _lanes(shape):
    return lax.broadcasted_iota(jnp.int32, shape, len(shape) - 1)


def _halve_kernel(q0, k0, v0, s1_ref, q1_ref, s2_ref, q2_ref, wide, half):
    n1 = half.shape[0]
    n2 = n1 // 2
    for h in range(q0.shape[1] // DH):
        cols = slice(h * DH, (h + 1) * DH)
        for i, src in enumerate((k0, v0, q0)):
            wide[...] = src[:, cols].astype(F32)
            h1 = ((wide[pl.ds(0, n1, stride=2), :] + wide[pl.ds(1, n1, stride=2), :]) * 0.5).astype(BF16)
            half[...] = h1.astype(F32)
            h2 = ((half[pl.ds(0, n2, stride=2), :] + half[pl.ds(1, n2, stride=2), :]) * 0.5).astype(BF16)
            if i < 2:
                s1_ref[i, :, cols] = h1
                s2_ref[i, :, cols] = h2
            else:
                q1_ref[:, cols] = h1
                q2_ref[:, cols] = h2


def _fwd0_kernel(q0, k0, v0, a0_ref, ms_ref):
    s = _nt(q0[...], k0[...]) * SCALE
    m = s.max(-1, keepdims=True)
    e = jnp.exp(s - m)
    a0_ref[...] = _nn(e.astype(BF16), v0[...])
    lane = _lanes(ms_ref.shape)
    ms_ref[...] = jnp.where(lane == 0, m, jnp.where(lane == 1, e.sum(-1, keepdims=True), 0.0))


def _fwd12_kernel(a0, ms0, g0, q1, k1p, v1p, q2, k2a, v2a, k2b, v2b,
                  att_ref, w_ref, sums_ref,
                  a1s, m1s, s1s, a2s, m2s, s2s, atts, ws):
    h = pl.program_id(0)
    n0 = atts.shape[0]
    n2 = a2s.shape[0]

    def put(a_ref, m_ref, s_ref, a, m, s):
        a_ref[...] = a
        m_ref[...] = jnp.broadcast_to(m, a.shape)
        s_ref[...] = jnp.broadcast_to(s, a.shape)

    s = _nt(q1[...], k1p[...]) * SCALE
    m = s.max(-1, keepdims=True)
    e = jnp.exp(s - m)
    put(a1s, m1s, s1s, _nn(e.astype(BF16), v1p[...]), m, e.sum(-1, keepdims=True))

    qv = q2[...]
    sa = _nt(qv, k2a[...]) * SCALE
    sb = _nt(qv, k2b[...]) * SCALE
    m = jnp.maximum(sa.max(-1, keepdims=True), sb.max(-1, keepdims=True))
    ea = jnp.exp(sa - m)
    eb = jnp.exp(sb - m)
    a = _nn(ea.astype(BF16), v2a[...]) + _nn(eb.astype(BF16), v2b[...])
    put(a2s, m2s, s2s, a, m, ea.sum(-1, keepdims=True) + eb.sum(-1, keepdims=True))

    lane = _lanes((n2, DH))
    for j in range(4):
        r0 = pl.ds(j, n2, stride=4)
        r1 = pl.ds(j >> 1, n2, stride=2)
        ms = ms0[r0, :]
        mm0 = ms[:, 0:1]
        mm1 = m1s[r1, :]
        mm2 = m2s[...]
        top = jnp.maximum(jnp.maximum(mm0, mm1), mm2)
        f0 = jnp.exp(mm0 - top)
        f1 = 2.0 * jnp.exp(mm1 - top)
        f2 = 4.0 * jnp.exp(mm2 - top)
        den = f0 * ms[:, 1:2] + f1 * s1s[r1, :] + f2 * s2s[...]
        num = f0 * a0[r0, :] + f1 * a1s[r1, :] + f2 * a2s[...]
        atts[r0, :] = (num / den).astype(BF16).astype(F32)
        ws[r0, :] = jnp.where(
            lane == 0, f0 / den, jnp.where(lane == 1, f1 / den, jnp.where(lane == 2, f2 / den, 0.0))
        )
    attv = atts[...]
    att_ref[...] = attv.astype(BF16)
    w_ref[...] = ws[...]
    gf = g0[...].astype(F32)
    sq = (attv * attv).sum(-1, keepdims=True)
    dt = (gf * attv).sum(-1, keepdims=True)
    lane0 = _lanes((n0, DH))
    part = jnp.where(lane0 == 0, sq, jnp.where(lane0 == 1, dt, 0.0))

    @pl.when(h == 0)
    def _():
        sums_ref[...] = part

    @pl.when(h > 0)
    def _():
        sums_ref[...] += part


def _level_grads(g0, att, w, mine, theirs, t_s, u_s):
    n0 = t_s.shape[0]
    n1 = n0 // 2
    n2 = n0 // 4
    full_width = 2 * 4 * DH
    totals = mine[:, 0:2] + theirs[:, 0:2]
    inv = lax.rsqrt(totals[:, 0:1] / full_width + EPSILON)
    coef = inv * inv * inv * totals[:, 1:2] / full_width
    attv = att[...].astype(F32)
    gf = g0[...].astype(F32)
    ga = inv * gf - coef * attv
    rt = (ga * attv).sum(-1, keepdims=True)
    wv = w[...]
    w0 = wv[:, 0:1]
    w1 = wv[:, 1:2]
    w2 = wv[:, 2:3]
    gl0 = (w0 * ga).astype(BF16)
    dl0 = w0 * rt
    t_s[...] = w1 * ga
    u_s[...] = jnp.broadcast_to(w1 * rt, (n0, DH))
    e_rows = pl.ds(0, n1, stride=2)
    o_rows = pl.ds(1, n1, stride=2)
    gl1 = (t_s[e_rows, :] + t_s[o_rows, :]).astype(BF16)
    dl1 = u_s[e_rows, :] + u_s[o_rows, :]
    t_s[...] = w2 * ga
    u_s[...] = jnp.broadcast_to(w2 * rt, (n0, DH))
    rows = [pl.ds(j, n2, stride=4) for j in range(4)]
    gl2 = (((t_s[rows[0], :] + t_s[rows[1], :]) + t_s[rows[2], :]) + t_s[rows[3], :]).astype(BF16)
    dl2 = ((u_s[rows[0], :] + u_s[rows[1], :]) + u_s[rows[2], :]) + u_s[rows[3], :]
    return inv, attv, gl0, dl0, gl1, dl1, gl2, dl2


def _split3(x):
    hi = x.astype(BF16).astype(F32)
    rest = x - hi
    mid = rest.astype(BF16).astype(F32)
    return hi, mid, rest - mid


def _coded(pieces):
    sub = lax.broadcasted_iota(jnp.int32, (16, DH), 0)
    out = jnp.zeros((16, DH), F32)
    for i, piece in enumerate(pieces):
        out = jnp.where(sub == i, piece, out)
    return out.astype(BF16)


def _bwd1_kernel(g0, att, w, mine, theirs, q1, q2, norm_ref, b1_ref, b2_ref, t_s, u_s):
    inv, attv, _, _, gl1, dl1, gl2, dl2 = _level_grads(g0, att, w, mine, theirs, t_s, u_s)
    n1 = gl1.shape[0]
    n2 = gl2.shape[0]
    norm_ref[...] = (attv * inv).astype(BF16)
    b1_ref[0:n1, :] = gl1
    b2_ref[0:n2, :] = gl2
    t1 = dl1.T
    a_parts = _split3(t1[0:1, 0:DH])
    b_parts = _split3(t1[0:1, DH:2 * DH])
    b1_ref[n1:n1 + 16, :] = _coded([a_parts[0], b_parts[0], a_parts[1], b_parts[1], a_parts[2], b_parts[2]])
    b2_ref[n2:n2 + 16, :] = _coded(list(_split3(dl2.T[0:1, :])))
    b1_ref[n1 + 16:, :] = q1[...]
    b2_ref[n2 + 16:, :] = q2[...]


def _bwd2_kernel(q0, k0, v0, g0, att, w, mine, theirs, q1, k1p, v1p, q2, k2a, v2a, k2b, v2b,
                 gq_ref, dk0_ref, dv0_ref,
                 t_s, u_s, dq0s, dq1s, dq2s, outs):
    n2 = dq2s.shape[0]
    _, _, gl0, dl0, gl1, dl1, gl2, dl2 = _level_grads(g0, att, w, mine, theirs, t_s, u_s)
    q0v = q0[...]
    k0v = k0[...]
    v0v = v0[...]
    s = _nt(q0v, k0v) * SCALE
    m = s.max(-1, keepdims=True)
    e = jnp.exp(s - m)
    p = e.astype(BF16)
    ds = (e * (_nt(gl0, v0v) - dl0)).astype(BF16)
    dq0s[...] = _nn(ds, k0v) * SCALE
    dk0_ref[...] = _tn(ds, q0v) * SCALE
    dv0_ref[...] = _tn(p, gl0)

    kv = k1p[...]
    s = _nt(q1[...], kv) * SCALE
    m = s.max(-1, keepdims=True)
    e = jnp.exp(s - m)
    ds = (e * (_nt(gl1, v1p[...]) - dl1[:, 0:1])).astype(BF16)
    dq1s[...] = _nn(ds, kv) * SCALE

    qv = q2[...]
    ka = k2a[...]
    kb = k2b[...]
    sa = _nt(qv, ka) * SCALE
    sb = _nt(qv, kb) * SCALE
    m = jnp.maximum(sa.max(-1, keepdims=True), sb.max(-1, keepdims=True))
    ea = jnp.exp(sa - m)
    eb = jnp.exp(sb - m)
    d2c = dl2[:, 0:1]
    dsa = (ea * (_nt(gl2, v2a[...]) - d2c)).astype(BF16)
    dsb = (eb * (_nt(gl2, v2b[...]) - d2c)).astype(BF16)
    dq2s[...] = (_nn(dsa, ka) + _nn(dsb, kb)) * SCALE

    for j in range(4):
        r0 = pl.ds(j, n2, stride=4)
        r1 = pl.ds(j >> 1, n2, stride=2)
        outs[r0, :] = dq0s[r0, :] + dq1s[r1, :] * 0.5 + dq2s[...] * 0.25
    gq_ref[...] = outs[...].astype(BF16)


def _own_kernel(k1o, v1o, k1p, b1p, k2o, v2o, b2a, b2b, dk0, dv0,
                gk_ref, gv_ref, wide, dk1s, dv1s, dk2s, dv2s, outk, outv):
    n1 = dk1s.shape[0]
    n2 = dk2s.shape[0]
    qv = b1p[n1 + 16:, :]
    gv = b1p[0:n1, :]
    x = b1p[n1:n1 + 16, :].astype(F32)
    d_row = jnp.concatenate([(x[0:1] + x[2:3]) + x[4:5], (x[1:2] + x[3:4]) + x[5:6]], axis=1)
    st = _nt(k1o[...], qv) * SCALE
    m = st.max(0, keepdims=True)
    e = jnp.exp(st - m)
    p = e.astype(BF16)
    ds = (e * (_nt(v1o[...], gv) - d_row)).astype(BF16)
    dk1s[...] = _nn(ds, qv) * SCALE
    dv1s[...] = _nn(p, gv)

    wide[...] = k1p[...].astype(F32)
    ks = ((wide[pl.ds(0, n2, stride=2), :] + wide[pl.ds(1, n2, stride=2), :]) * 0.5).astype(BF16)
    ko = k2o[...]
    vo = v2o[...]
    dks = []
    dvs = []
    for b_ref in (b2a, b2b):
        qv = b_ref[n2 + 16:, :]
        gv = b_ref[0:n2, :]
        x = b_ref[n2:n2 + 16, :].astype(F32)
        d_row = (x[0:1] + x[1:2]) + x[2:3]
        so = _nt(ko, qv) * SCALE
        ss = _nt(ks, qv) * SCALE
        m = jnp.maximum(so.max(0, keepdims=True), ss.max(0, keepdims=True))
        e = jnp.exp(so - m)
        p = e.astype(BF16)
        ds = (e * (_nt(vo, gv) - d_row)).astype(BF16)
        dks.append(_nn(ds, qv))
        dvs.append(_nn(p, gv))
    dk2s[...] = (dks[0] + dks[1]) * SCALE
    dv2s[...] = dvs[0] + dvs[1]

    for j in range(4):
        r0 = pl.ds(j, n2, stride=4)
        r1 = pl.ds(j >> 1, n2, stride=2)
        outk[r0, :] = dk0[r0, :] + dk1s[r1, :] * 0.5 + dk2s[...] * 0.25
        outv[r0, :] = dv0[r0, :] + dv1s[r1, :] * 0.5 + dv2s[...] * 0.25
    gk_ref[...] = outk[...].astype(BF16)
    gv_ref[...] = outv[...].astype(BF16)


def _cols(rows):
    return pl.BlockSpec((rows, DH), lambda h: (0, h))


def _stacked(rows, index):
    return pl.BlockSpec((None, rows, DH), lambda h: (index, 0, h))


def _per_head(rows, width):
    return pl.BlockSpec((None, rows, width), lambda h: (h, 0, 0))


def _whole(rows, width):
    return pl.BlockSpec((rows, width), lambda h: (0, 0))


def _params():
    return pltpu.CompilerParams(dimension_semantics=("arbitrary",))


def _full3(rows, width):
    return pl.BlockSpec((2, rows, width), lambda h: (0, 0, 0))


def shards(queries, key_states, value_states, out_grad):
    n0, width = queries.shape
    heads = width // DH
    n1 = n0 // 2
    n2 = n0 // 4
    q0, k0, v0, g0 = queries, key_states, value_states, out_grad
    s1, q1, s2, q2 = pl.pallas_call(
        _halve_kernel,
        grid=(1,),
        in_specs=[_whole(n0, width), _whole(n0, width), _whole(n0, width)],
        out_specs=[_full3(n1, width), _whole(n1, width), _full3(n2, width), _whole(n2, width)],
        out_shape=[
            jax.ShapeDtypeStruct((2, n1, width), BF16),
            jax.ShapeDtypeStruct((n1, width), BF16),
            jax.ShapeDtypeStruct((2, n2, width), BF16),
            jax.ShapeDtypeStruct((n2, width), BF16),
        ],
        scratch_shapes=[pltpu.VMEM((n0, DH), F32), pltpu.VMEM((n1, DH), F32)],
        compiler_params=_params(),
    )(q0, k0, v0)
    r1 = from_partner(s1, 1)
    r2a = from_partner(s2, 2)
    r2b = from_partner(s2, 3)

    a0, ms0 = pl.pallas_call(
        _fwd0_kernel,
        grid=(heads,),
        in_specs=[_cols(n0), _cols(n0), _cols(n0)],
        out_specs=[_cols(n0), _per_head(n0, DH)],
        out_shape=[
            jax.ShapeDtypeStruct((n0, width), F32),
            jax.ShapeDtypeStruct((heads, n0, DH), F32),
        ],
        compiler_params=_params(),
    )(q0, k0, v0)

    att, w, sums = pl.pallas_call(
        _fwd12_kernel,
        grid=(heads,),
        in_specs=[
            _cols(n0), _per_head(n0, DH), _cols(n0),
            _cols(n1), _stacked(n1, 0), _stacked(n1, 1),
            _cols(n2), _stacked(n2, 0), _stacked(n2, 1), _stacked(n2, 0), _stacked(n2, 1),
        ],
        out_specs=[_cols(n0), _per_head(n0, DH), _whole(n0, DH)],
        out_shape=[
            jax.ShapeDtypeStruct((n0, width), BF16),
            jax.ShapeDtypeStruct((heads, n0, DH), F32),
            jax.ShapeDtypeStruct((n0, DH), F32),
        ],
        scratch_shapes=[pltpu.VMEM((n, DH), F32) for n in (n1, n1, n1, n2, n2, n2, n0, n0)],
        compiler_params=_params(),
    )(a0, ms0, g0, q1, r1, r1, q2, r2a, r2a, r2b, r2b)

    assert width * lax.axis_size("head") == 2 * 4 * DH
    other = lax.ppermute(sums, "head", [(0, 1), (1, 0)])

    norm, b1, b2 = pl.pallas_call(
        _bwd1_kernel,
        grid=(heads,),
        in_specs=[_cols(n0), _cols(n0), _per_head(n0, DH), _whole(n0, DH), _whole(n0, DH), _cols(n1), _cols(n2)],
        out_specs=[_cols(n0), _cols(2 * n1 + 16), _cols(2 * n2 + 16)],
        out_shape=[
            jax.ShapeDtypeStruct((n0, width), BF16),
            jax.ShapeDtypeStruct((2 * n1 + 16, width), BF16),
            jax.ShapeDtypeStruct((2 * n2 + 16, width), BF16),
        ],
        scratch_shapes=[pltpu.VMEM((n0, DH), F32), pltpu.VMEM((n0, DH), F32)],
        compiler_params=_params(),
    )(g0, att, w, sums, other, q1, q2)
    b1p = from_partner(b1, 1)
    b2a = from_partner(b2, 2)
    b2b = from_partner(b2, 3)

    gq, dk0, dv0 = pl.pallas_call(
        _bwd2_kernel,
        grid=(heads,),
        in_specs=[
            _cols(n0), _cols(n0), _cols(n0), _cols(n0), _cols(n0), _per_head(n0, DH),
            _whole(n0, DH), _whole(n0, DH),
            _cols(n1), _stacked(n1, 0), _stacked(n1, 1),
            _cols(n2), _stacked(n2, 0), _stacked(n2, 1), _stacked(n2, 0), _stacked(n2, 1),
        ],
        out_specs=[_cols(n0), _cols(n0), _cols(n0)],
        out_shape=[
            jax.ShapeDtypeStruct((n0, width), BF16),
            jax.ShapeDtypeStruct((n0, width), F32),
            jax.ShapeDtypeStruct((n0, width), F32),
        ],
        scratch_shapes=[pltpu.VMEM((n, DH), F32) for n in (n0, n0, n0, n1, n2, n0)],
        compiler_params=_params(),
    )(q0, k0, v0, g0, att, w, sums, other, q1, r1, r1, q2, r2a, r2a, r2b, r2b)

    gk, gv = pl.pallas_call(
        _own_kernel,
        grid=(heads,),
        in_specs=[
            _stacked(n1, 0), _stacked(n1, 1), _stacked(n1, 0), _cols(2 * n1 + 16),
            _stacked(n2, 0), _stacked(n2, 1), _cols(2 * n2 + 16), _cols(2 * n2 + 16),
            _cols(n0), _cols(n0),
        ],
        out_specs=[_cols(n0), _cols(n0)],
        out_shape=[
            jax.ShapeDtypeStruct((n0, width), BF16),
            jax.ShapeDtypeStruct((n0, width), BF16),
        ],
        scratch_shapes=[pltpu.VMEM((n, DH), F32) for n in (n1, n1, n1, n2, n2, n0, n0)],
        compiler_params=_params(),
    )(s1, s1, r1, b1p, s2, s2, b2a, b2b, dk0, dv0)
    return (norm, gq, gk, gv)


def solution(mesh):
    return jax.shard_map(
        shards,
        mesh=mesh,
        in_specs=(P("seq", "head"), P("seq", "head"), P("seq", "head"), P("seq", "head")),
        out_specs=(P("seq", "head"), P("seq", "head"), P("seq", "head"), P("seq", "head")),
        check_vma=False,
    )
```

```python
import jax
import jax.numpy as jnp
from jax import lax
from jax.experimental import pallas as pl
from jax.experimental.pallas import tpu as pltpu
from jax.sharding import PartitionSpec as P


DH = 128
EPSILON = 1e-06
SCALE = DH ** (-0.5)
F32 = jnp.float32
BF16 = jnp.bfloat16


def from_partner(value, mask):
    pairs = [(source, source ^ mask) for source in range(lax.axis_size("seq"))]
    return lax.ppermute(value, "seq", pairs)


def _nt(a, b):
    return lax.dot_general(a, b, (((1,), (1,)), ((), ())), preferred_element_type=F32)


def _nn(a, b):
    return lax.dot_general(a, b, (((1,), (0,)), ((), ())), preferred_element_type=F32)


def _tn(a, b):
    return lax.dot_general(a, b, (((0,), (0,)), ((), ())), preferred_element_type=F32)


def _lanes(shape):
    return lax.broadcasted_iota(jnp.int32, shape, len(shape) - 1)


def _halve_kernel(q0, k0, v0, s1_ref, q1_ref, s2_ref, q2_ref, wide, half):
    n1 = half.shape[0]
    n2 = n1 // 2
    for h in range(q0.shape[1] // DH):
        cols = slice(h * DH, (h + 1) * DH)
        for i, src in enumerate((k0, v0, q0)):
            wide[...] = src[:, cols].astype(F32)
            h1 = ((wide[pl.ds(0, n1, stride=2), :] + wide[pl.ds(1, n1, stride=2), :]) * 0.5).astype(BF16)
            half[...] = h1.astype(F32)
            h2 = ((half[pl.ds(0, n2, stride=2), :] + half[pl.ds(1, n2, stride=2), :]) * 0.5).astype(BF16)
            if i < 2:
                s1_ref[i, :, cols] = h1
                s2_ref[i, :, cols] = h2
            else:
                q1_ref[:, cols] = h1
                q2_ref[:, cols] = h2


def _fwd0_kernel(q0, k0, v0, a0_ref, ms_ref):
    s = _nt(q0[...], k0[...]) * SCALE
    m = s.max(-1, keepdims=True)
    e = jnp.exp(s - m)
    a0_ref[...] = _nn(e.astype(BF16), v0[...])
    lane = _lanes(ms_ref.shape)
    ms_ref[...] = jnp.where(lane == 0, m, jnp.where(lane == 1, e.sum(-1, keepdims=True), 0.0))


def _fwd12_kernel(a0, ms0, g0, q1, k1p, v1p, q2, k2a, v2a, k2b, v2b,
                  att_ref, w_ref, sums_ref,
                  a1s, m1s, s1s, a2s, m2s, s2s, atts, ws):
    h = pl.program_id(0)
    n0 = atts.shape[0]
    n2 = a2s.shape[0]

    def put(a_ref, m_ref, s_ref, a, m, s):
        a_ref[...] = a
        m_ref[...] = jnp.broadcast_to(m, a.shape)
        s_ref[...] = jnp.broadcast_to(s, a.shape)

    s = _nt(q1[...], k1p[...]) * SCALE
    m = s.max(-1, keepdims=True)
    e = jnp.exp(s - m)
    put(a1s, m1s, s1s, _nn(e.astype(BF16), v1p[...]), m, e.sum(-1, keepdims=True))

    qv = q2[...]
    sa = _nt(qv, k2a[...]) * SCALE
    sb = _nt(qv, k2b[...]) * SCALE
    m = jnp.maximum(sa.max(-1, keepdims=True), sb.max(-1, keepdims=True))
    ea = jnp.exp(sa - m)
    eb = jnp.exp(sb - m)
    a = _nn(ea.astype(BF16), v2a[...]) + _nn(eb.astype(BF16), v2b[...])
    put(a2s, m2s, s2s, a, m, ea.sum(-1, keepdims=True) + eb.sum(-1, keepdims=True))

    lane = _lanes((n2, DH))
    for j in range(4):
        r0 = pl.ds(j, n2, stride=4)
        r1 = pl.ds(j >> 1, n2, stride=2)
        ms = ms0[r0, :]
        mm0 = ms[:, 0:1]
        mm1 = m1s[r1, :]
        mm2 = m2s[...]
        top = jnp.maximum(jnp.maximum(mm0, mm1), mm2)
        f0 = jnp.exp(mm0 - top)
        f1 = 2.0 * jnp.exp(mm1 - top)
        f2 = 4.0 * jnp.exp(mm2 - top)
        den = f0 * ms[:, 1:2] + f1 * s1s[r1, :] + f2 * s2s[...]
        num = f0 * a0[r0, :] + f1 * a1s[r1, :] + f2 * a2s[...]
        atts[r0, :] = (num / den).astype(BF16).astype(F32)
        ws[r0, :] = jnp.where(
            lane == 0, f0 / den, jnp.where(lane == 1, f1 / den, jnp.where(lane == 2, f2 / den, 0.0))
        )
    attv = atts[...]
    att_ref[...] = attv.astype(BF16)
    w_ref[...] = ws[...]
    gf = g0[...].astype(F32)
    sq = (attv * attv).sum(-1, keepdims=True)
    dt = (gf * attv).sum(-1, keepdims=True)
    lane0 = _lanes((n0, DH))
    part = jnp.where(lane0 == 0, sq, jnp.where(lane0 == 1, dt, 0.0))

    @pl.when(h == 0)
    def _():
        sums_ref[...] = part

    @pl.when(h > 0)
    def _():
        sums_ref[...] += part


def _level_grads(g0, att, w, mine, theirs, t_s, u_s):
    n0 = t_s.shape[0]
    n1 = n0 // 2
    n2 = n0 // 4
    full_width = 2 * 4 * DH
    totals = mine[:, 0:2] + theirs[:, 0:2]
    inv = lax.rsqrt(totals[:, 0:1] / full_width + EPSILON)
    coef = inv * inv * inv * totals[:, 1:2] / full_width
    attv = att[...].astype(F32)
    gf = g0[...].astype(F32)
    ga = inv * gf - coef * attv
    rt = (ga * attv).sum(-1, keepdims=True)
    wv = w[...]
    w0 = wv[:, 0:1]
    w1 = wv[:, 1:2]
    w2 = wv[:, 2:3]
    gl0 = (w0 * ga).astype(BF16)
    dl0 = w0 * rt
    t_s[...] = w1 * ga
    u_s[...] = jnp.broadcast_to(w1 * rt, (n0, DH))
    e_rows = pl.ds(0, n1, stride=2)
    o_rows = pl.ds(1, n1, stride=2)
    gl1 = (t_s[e_rows, :] + t_s[o_rows, :]).astype(BF16)
    dl1 = u_s[e_rows, :] + u_s[o_rows, :]
    t_s[...] = w2 * ga
    u_s[...] = jnp.broadcast_to(w2 * rt, (n0, DH))
    rows = [pl.ds(j, n2, stride=4) for j in range(4)]
    gl2 = (((t_s[rows[0], :] + t_s[rows[1], :]) + t_s[rows[2], :]) + t_s[rows[3], :]).astype(BF16)
    dl2 = ((u_s[rows[0], :] + u_s[rows[1], :]) + u_s[rows[2], :]) + u_s[rows[3], :]
    return inv, attv, gl0, dl0, gl1, dl1, gl2, dl2


def _split3(x):
    hi = x.astype(BF16).astype(F32)
    rest = x - hi
    mid = rest.astype(BF16).astype(F32)
    return hi, mid, rest - mid


def _coded(pieces):
    sub = lax.broadcasted_iota(jnp.int32, (16, DH), 0)
    out = jnp.zeros((16, DH), F32)
    for i, piece in enumerate(pieces):
        out = jnp.where(sub == i, piece, out)
    return out.astype(BF16)


def _bwd1_kernel(g0, att, w, mine, theirs, q1, q2, norm_ref, b1_ref, b2_ref, t_s, u_s):
    inv, attv, _, _, gl1, dl1, gl2, dl2 = _level_grads(g0, att, w, mine, theirs, t_s, u_s)
    n1 = gl1.shape[0]
    n2 = gl2.shape[0]
    norm_ref[...] = (attv * inv).astype(BF16)
    b1_ref[0:n1, :] = gl1
    b2_ref[0:n2, :] = gl2
    t1 = dl1.T
    a_parts = _split3(t1[0:1, 0:DH])
    b_parts = _split3(t1[0:1, DH:2 * DH])
    b1_ref[n1:n1 + 16, :] = _coded([a_parts[0], b_parts[0], a_parts[1], b_parts[1], a_parts[2], b_parts[2]])
    b2_ref[n2:n2 + 16, :] = _coded(list(_split3(dl2.T[0:1, :])))
    b1_ref[n1 + 16:, :] = q1[...]
    b2_ref[n2 + 16:, :] = q2[...]


def _bwd2_kernel(q0, k0, v0, g0, att, w, mine, theirs, q1, k1p, v1p, q2, k2a, v2a, k2b, v2b,
                 gq_ref, dk0_ref, dv0_ref,
                 t_s, u_s, dq0s, dq1s, dq2s, outs):
    n2 = dq2s.shape[0]
    _, _, gl0, dl0, gl1, dl1, gl2, dl2 = _level_grads(g0, att, w, mine, theirs, t_s, u_s)
    q0v = q0[...]
    k0v = k0[...]
    v0v = v0[...]
    s = _nt(q0v, k0v) * SCALE
    m = s.max(-1, keepdims=True)
    e = jnp.exp(s - m)
    p = e.astype(BF16)
    ds = (e * (_nt(gl0, v0v) - dl0)).astype(BF16)
    dq0s[...] = _nn(ds, k0v) * SCALE
    dk0_ref[...] = _tn(ds, q0v) * SCALE
    dv0_ref[...] = _tn(p, gl0)

    kv = k1p[...]
    s = _nt(q1[...], kv) * SCALE
    m = s.max(-1, keepdims=True)
    e = jnp.exp(s - m)
    ds = (e * (_nt(gl1, v1p[...]) - dl1[:, 0:1])).astype(BF16)
    dq1s[...] = _nn(ds, kv) * SCALE

    qv = q2[...]
    ka = k2a[...]
    kb = k2b[...]
    sa = _nt(qv, ka) * SCALE
    sb = _nt(qv, kb) * SCALE
    m = jnp.maximum(sa.max(-1, keepdims=True), sb.max(-1, keepdims=True))
    ea = jnp.exp(sa - m)
    eb = jnp.exp(sb - m)
    d2c = dl2[:, 0:1]
    dsa = (ea * (_nt(gl2, v2a[...]) - d2c)).astype(BF16)
    dsb = (eb * (_nt(gl2, v2b[...]) - d2c)).astype(BF16)
    dq2s[...] = (_nn(dsa, ka) + _nn(dsb, kb)) * SCALE

    for j in range(4):
        r0 = pl.ds(j, n2, stride=4)
        r1 = pl.ds(j >> 1, n2, stride=2)
        outs[r0, :] = dq0s[r0, :] + dq1s[r1, :] * 0.5 + dq2s[...] * 0.25
    gq_ref[...] = outs[...].astype(BF16)


def _own_kernel(k1o, v1o, k1p, b1p, k2o, v2o, b2a, b2b, dk0, dv0,
                gk_ref, gv_ref, wide, dk1s, dv1s, dk2s, dv2s, outk, outv):
    n1 = dk1s.shape[0]
    n2 = dk2s.shape[0]
    qv = b1p[n1 + 16:, :]
    gv = b1p[0:n1, :]
    x = b1p[n1:n1 + 16, :].astype(F32)
    d_row = jnp.concatenate([(x[0:1] + x[2:3]) + x[4:5], (x[1:2] + x[3:4]) + x[5:6]], axis=1)
    st = _nt(k1o[...], qv) * SCALE
    m = st.max(0, keepdims=True)
    e = jnp.exp(st - m)
    p = e.astype(BF16)
    ds = (e * (_nt(v1o[...], gv) - d_row)).astype(BF16)
    dk1s[...] = _nn(ds, qv) * SCALE
    dv1s[...] = _nn(p, gv)

    wide[...] = k1p[...].astype(F32)
    ks = ((wide[pl.ds(0, n2, stride=2), :] + wide[pl.ds(1, n2, stride=2), :]) * 0.5).astype(BF16)
    ko = k2o[...]
    vo = v2o[...]
    dks = []
    dvs = []
    for b_ref in (b2a, b2b):
        qv = b_ref[n2 + 16:, :]
        gv = b_ref[0:n2, :]
        x = b_ref[n2:n2 + 16, :].astype(F32)
        d_row = (x[0:1] + x[1:2]) + x[2:3]
        so = _nt(ko, qv) * SCALE
        ss = _nt(ks, qv) * SCALE
        m = jnp.maximum(so.max(0, keepdims=True), ss.max(0, keepdims=True))
        e = jnp.exp(so - m)
        p = e.astype(BF16)
        ds = (e * (_nt(vo, gv) - d_row)).astype(BF16)
        dks.append(_nn(ds, qv))
        dvs.append(_nn(p, gv))
    dk2s[...] = (dks[0] + dks[1]) * SCALE
    dv2s[...] = dvs[0] + dvs[1]

    for j in range(4):
        r0 = pl.ds(j, n2, stride=4)
        r1 = pl.ds(j >> 1, n2, stride=2)
        outk[r0, :] = dk0[r0, :] + dk1s[r1, :] * 0.5 + dk2s[...] * 0.25
        outv[r0, :] = dv0[r0, :] + dv1s[r1, :] * 0.5 + dv2s[...] * 0.25
    gk_ref[...] = outk[...].astype(BF16)
    gv_ref[...] = outv[...].astype(BF16)


def _cols(rows):
    return pl.BlockSpec((rows, DH), lambda h: (0, h))


def _stacked(rows, index):
    return pl.BlockSpec((None, rows, DH), lambda h: (index, 0, h))


def _per_head(rows, width):
    return pl.BlockSpec((None, rows, width), lambda h: (h, 0, 0))


def _whole(rows, width):
    return pl.BlockSpec((rows, width), lambda h: (0, 0))


def _params():
    return pltpu.CompilerParams(dimension_semantics=("arbitrary",))


def _full3(rows, width):
    return pl.BlockSpec((2, rows, width), lambda h: (0, 0, 0))


def shards(queries, key_states, value_states, out_grad):
    n0, width = queries.shape
    heads = width // DH
    n1 = n0 // 2
    n2 = n0 // 4
    q0, k0, v0, g0 = queries, key_states, value_states, out_grad
    s1, q1, s2, q2 = pl.pallas_call(
        _halve_kernel,
        grid=(1,),
        in_specs=[_whole(n0, width), _whole(n0, width), _whole(n0, width)],
        out_specs=[_full3(n1, width), _whole(n1, width), _full3(n2, width), _whole(n2, width)],
        out_shape=[
            jax.ShapeDtypeStruct((2, n1, width), BF16),
            jax.ShapeDtypeStruct((n1, width), BF16),
            jax.ShapeDtypeStruct((2, n2, width), BF16),
            jax.ShapeDtypeStruct((n2, width), BF16),
        ],
        scratch_shapes=[pltpu.VMEM((n0, DH), F32), pltpu.VMEM((n1, DH), F32)],
        compiler_params=_params(),
    )(q0, k0, v0)
    r1 = from_partner(s1, 1)
    r2a = from_partner(s2, 2)
    r2b = from_partner(s2, 3)

    a0, ms0 = _fwd0_call(heads, n0, width, q0, k0, v0)
    return _rest(heads, n0, n1, n2, width, q0, k0, v0, g0, s1, q1, s2, q2, r1, r2a, r2b, a0, ms0)


def _fwd0_call(heads, n0, width, q0, k0, v0):
    return pl.pallas_call(
        _fwd0_kernel,
        grid=(heads,),
        in_specs=[_cols(n0), _cols(n0), _cols(n0)],
        out_specs=[_cols(n0), _per_head(n0, DH)],
        out_shape=[
            jax.ShapeDtypeStruct((n0, width), F32),
            jax.ShapeDtypeStruct((heads, n0, DH), F32),
        ],
        compiler_params=_params(),
    )(q0, k0, v0)


def _rest(heads, n0, n1, n2, width, q0, k0, v0, g0, s1, q1, s2, q2, r1, r2a, r2b, a0, ms0):
    att, w, sums = pl.pallas_call(
        _fwd12_kernel,
        grid=(heads,),
        in_specs=[
            _cols(n0), _per_head(n0, DH), _cols(n0),
            _cols(n1), _stacked(n1, 0), _stacked(n1, 1),
            _cols(n2), _stacked(n2, 0), _stacked(n2, 1), _stacked(n2, 0), _stacked(n2, 1),
        ],
        out_specs=[_cols(n0), _per_head(n0, DH), _whole(n0, DH)],
        out_shape=[
            jax.ShapeDtypeStruct((n0, width), BF16),
            jax.ShapeDtypeStruct((heads, n0, DH), F32),
            jax.ShapeDtypeStruct((n0, DH), F32),
        ],
        scratch_shapes=[pltpu.VMEM((n, DH), F32) for n in (n1, n1, n1, n2, n2, n2, n0, n0)],
        compiler_params=_params(),
    )(a0, ms0, g0, q1, r1, r1, q2, r2a, r2a, r2b, r2b)

    assert width * lax.axis_size("head") == 2 * 4 * DH
    other = lax.ppermute(sums, "head", [(0, 1), (1, 0)])

    norm, b1, b2 = pl.pallas_call(
        _bwd1_kernel,
        grid=(heads,),
        in_specs=[_cols(n0), _cols(n0), _per_head(n0, DH), _whole(n0, DH), _whole(n0, DH), _cols(n1), _cols(n2)],
        out_specs=[_cols(n0), _cols(2 * n1 + 16), _cols(2 * n2 + 16)],
        out_shape=[
            jax.ShapeDtypeStruct((n0, width), BF16),
            jax.ShapeDtypeStruct((2 * n1 + 16, width), BF16),
            jax.ShapeDtypeStruct((2 * n2 + 16, width), BF16),
        ],
        scratch_shapes=[pltpu.VMEM((n0, DH), F32), pltpu.VMEM((n0, DH), F32)],
        compiler_params=_params(),
    )(g0, att, w, sums, other, q1, q2)
    b1p = from_partner(b1, 1)
    b2a = from_partner(b2, 2)
    b2b = from_partner(b2, 3)

    gq, dk0, dv0 = pl.pallas_call(
        _bwd2_kernel,
        grid=(heads,),
        in_specs=[
            _cols(n0), _cols(n0), _cols(n0), _cols(n0), _cols(n0), _per_head(n0, DH),
            _whole(n0, DH), _whole(n0, DH),
            _cols(n1), _stacked(n1, 0), _stacked(n1, 1),
            _cols(n2), _stacked(n2, 0), _stacked(n2, 1), _stacked(n2, 0), _stacked(n2, 1),
        ],
        out_specs=[_cols(n0), _cols(n0), _cols(n0)],
        out_shape=[
            jax.ShapeDtypeStruct((n0, width), BF16),
            jax.ShapeDtypeStruct((n0, width), F32),
            jax.ShapeDtypeStruct((n0, width), F32),
        ],
        scratch_shapes=[pltpu.VMEM((n, DH), F32) for n in (n0, n0, n0, n1, n2, n0)],
        compiler_params=_params(),
    )(q0, k0, v0, g0, att, w, sums, other, q1, r1, r1, q2, r2a, r2a, r2b, r2b)

    gk, gv = pl.pallas_call(
        _own_kernel,
        grid=(heads,),
        in_specs=[
            _stacked(n1, 0), _stacked(n1, 1), _stacked(n1, 0), _cols(2 * n1 + 16),
            _stacked(n2, 0), _stacked(n2, 1), _cols(2 * n2 + 16), _cols(2 * n2 + 16),
            _cols(n0), _cols(n0),
        ],
        out_specs=[_cols(n0), _cols(n0)],
        out_shape=[
            jax.ShapeDtypeStruct((n0, width), BF16),
            jax.ShapeDtypeStruct((n0, width), BF16),
        ],
        scratch_shapes=[pltpu.VMEM((n, DH), F32) for n in (n1, n1, n1, n2, n2, n0, n0)],
        compiler_params=_params(),
    )(s1, s1, r1, b1p, s2, s2, b2a, b2b, dk0, dv0)
    return (norm, gq, gk, gv)


def solution(mesh):
    return jax.shard_map(
        shards,
        mesh=mesh,
        in_specs=(P("seq", "head"), P("seq", "head"), P("seq", "head"), P("seq", "head")),
        out_specs=(P("seq", "head"), P("seq", "head"), P("seq", "head"), P("seq", "head")),
        check_vma=False,
    )
```

```python
import jax
import jax.numpy as jnp
from jax import lax
from jax.experimental import pallas as pl
from jax.experimental.pallas import tpu as pltpu
from jax.sharding import PartitionSpec as P

DH = 128
LEAF = 256
LEVELS = 3
EPSILON = 1e-06
SCALE = DH ** (-0.5)
F32 = jnp.float32
BF16 = jnp.bfloat16


def from_partner(value, mask):
    pairs = [(source, source ^ mask) for source in range(lax.axis_size("seq"))]
    return lax.ppermute(value, "seq", pairs)


def halving(source):
    widened = source.astype(F32)
    paired = widened.reshape(widened.shape[:-2] + (widened.shape[-2] // 2, 2, widened.shape[-1]))
    return ((paired[..., 0, :] + paired[..., 1, :]) * 0.5).astype(BF16)


def _nt(a, b):
    return lax.dot_general(a, b, (((1,), (1,)), ((), ())), preferred_element_type=F32)


def _nn(a, b):
    return lax.dot_general(a, b, (((1,), (0,)), ((), ())), preferred_element_type=F32)


def _tn(a, b):
    return lax.dot_general(a, b, (((0,), (0,)), ((), ())), preferred_element_type=F32)


def _lanes(shape):
    return lax.broadcasted_iota(jnp.int32, shape, len(shape) - 1)


def _halve_kernel(q0, k0, v0, s1_ref, q1_ref, s2_ref, q2_ref, wide, half):
    n1 = half.shape[0]
    n2 = n1 // 2
    for h in range(q0.shape[1] // DH):
        cols = slice(h * DH, (h + 1) * DH)
        for i, src in enumerate((k0, v0, q0)):
            wide[...] = src[:, cols].astype(F32)
            h1 = ((wide[pl.ds(0, n1, stride=2), :] + wide[pl.ds(1, n1, stride=2), :]) * 0.5).astype(BF16)
            half[...] = h1.astype(F32)
            h2 = ((half[pl.ds(0, n2, stride=2), :] + half[pl.ds(1, n2, stride=2), :]) * 0.5).astype(BF16)
            if i < 2:
                s1_ref[i, :, cols] = h1
                s2_ref[i, :, cols] = h2
            else:
                q1_ref[:, cols] = h1
                q2_ref[:, cols] = h2


def _fwd0_kernel(q0, k0, v0, a0_ref, ms_ref):
    s = _nt(q0[...], k0[...]) * SCALE
    m = s.max(-1, keepdims=True)
    e = jnp.exp(s - m)
    a0_ref[...] = _nn(e.astype(BF16), v0[...])
    lane = _lanes(ms_ref.shape)
    ms_ref[...] = jnp.where(lane == 0, m, jnp.where(lane == 1, e.sum(-1, keepdims=True), 0.0))


def _fwd12_kernel(a0, ms0, g0, q1, k1p, v1p, q2, k2a, v2a, k2b, v2b,
                  att_ref, w_ref, sums_ref,
                  a1s, m1s, s1s, a2s, m2s, s2s, atts, ws):
    h = pl.program_id(0)
    n0 = atts.shape[0]
    n2 = a2s.shape[0]

    def put(a_ref, m_ref, s_ref, a, m, s):
        a_ref[...] = a
        m_ref[...] = jnp.broadcast_to(m, a.shape)
        s_ref[...] = jnp.broadcast_to(s, a.shape)

    s = _nt(q1[...], k1p[...]) * SCALE
    m = s.max(-1, keepdims=True)
    e = jnp.exp(s - m)
    put(a1s, m1s, s1s, _nn(e.astype(BF16), v1p[...]), m, e.sum(-1, keepdims=True))

    qv = q2[...]
    sa = _nt(qv, k2a[...]) * SCALE
    sb = _nt(qv, k2b[...]) * SCALE
    m = jnp.maximum(sa.max(-1, keepdims=True), sb.max(-1, keepdims=True))
    ea = jnp.exp(sa - m)
    eb = jnp.exp(sb - m)
    a = _nn(ea.astype(BF16), v2a[...]) + _nn(eb.astype(BF16), v2b[...])
    put(a2s, m2s, s2s, a, m, ea.sum(-1, keepdims=True) + eb.sum(-1, keepdims=True))

    lane = _lanes((n2, DH))
    for j in range(4):
        r0 = pl.ds(j, n2, stride=4)
        r1 = pl.ds(j >> 1, n2, stride=2)
        ms = ms0[r0, :]
        mm0 = ms[:, 0:1]
        mm1 = m1s[r1, :]
        mm2 = m2s[...]
        top = jnp.maximum(jnp.maximum(mm0, mm1), mm2)
        f0 = jnp.exp(mm0 - top)
        f1 = 2.0 * jnp.exp(mm1 - top)
        f2 = 4.0 * jnp.exp(mm2 - top)
        den = f0 * ms[:, 1:2] + f1 * s1s[r1, :] + f2 * s2s[...]
        num = f0 * a0[r0, :] + f1 * a1s[r1, :] + f2 * a2s[...]
        atts[r0, :] = (num / den).astype(BF16).astype(F32)
        rd = 1.0 / den
        ws[r0, :] = jnp.where(
            lane == 0, f0 * rd, jnp.where(lane == 1, f1 * rd, jnp.where(lane == 2, f2 * rd, 0.0))
        )
    attv = atts[...]
    att_ref[...] = attv.astype(BF16)
    w_ref[...] = ws[...]
    gf = g0[...].astype(F32)
    sq = (attv * attv).sum(-1, keepdims=True)
    dt = (gf * attv).sum(-1, keepdims=True)
    lane0 = _lanes((n0, DH))
    part = jnp.where(lane0 == 0, sq, jnp.where(lane0 == 1, dt, 0.0))

    @pl.when(h == 0)
    def _():
        sums_ref[...] = part

    @pl.when(h > 0)
    def _():
        sums_ref[...] += part


def _level_grads(g0, att, w, mine, theirs, t_s, u_s):
    n0 = t_s.shape[0]
    n1 = n0 // 2
    n2 = n0 // 4
    full_width = 2 * 4 * DH
    totals = mine[:, 0:2] + theirs[:, 0:2]
    inv = lax.rsqrt(totals[:, 0:1] / full_width + EPSILON)
    coef = inv * inv * inv * totals[:, 1:2] / full_width
    attv = att[...].astype(F32)
    gf = g0[...].astype(F32)
    ga = inv * gf - coef * attv
    rt = (ga * attv).sum(-1, keepdims=True)
    wv = w[...]
    w0 = wv[:, 0:1]
    w1 = wv[:, 1:2]
    w2 = wv[:, 2:3]
    gl0 = (w0 * ga).astype(BF16)
    dl0 = w0 * rt
    t_s[...] = w1 * ga
    u_s[...] = jnp.broadcast_to(w1 * rt, (n0, DH))
    e_rows = pl.ds(0, n1, stride=2)
    o_rows = pl.ds(1, n1, stride=2)
    gl1 = (t_s[e_rows, :] + t_s[o_rows, :]).astype(BF16)
    dl1 = u_s[e_rows, :] + u_s[o_rows, :]
    t_s[...] = w2 * ga
    u_s[...] = jnp.broadcast_to(w2 * rt, (n0, DH))
    rows = [pl.ds(j, n2, stride=4) for j in range(4)]
    gl2 = (((t_s[rows[0], :] + t_s[rows[1], :]) + t_s[rows[2], :]) + t_s[rows[3], :]).astype(BF16)
    dl2 = ((u_s[rows[0], :] + u_s[rows[1], :]) + u_s[rows[2], :]) + u_s[rows[3], :]
    return inv, attv, gl0, dl0, gl1, dl1, gl2, dl2


def _split3(x):
    hi = x.astype(BF16).astype(F32)
    rest = x - hi
    mid = rest.astype(BF16).astype(F32)
    return hi, mid, rest - mid


def _coded(pieces):
    sub = lax.broadcasted_iota(jnp.int32, (16, DH), 0)
    out = jnp.zeros((16, DH), F32)
    for i, piece in enumerate(pieces):
        out = jnp.where(sub == i, piece, out)
    return out.astype(BF16)


def _bwd1_kernel(g0, att, w, mine, theirs, q1, q2, norm_ref, b1_ref, b2_ref, t_s, u_s):
    inv, attv, _, _, gl1, dl1, gl2, dl2 = _level_grads(g0, att, w, mine, theirs, t_s, u_s)
    n1 = gl1.shape[0]
    n2 = gl2.shape[0]
    norm_ref[...] = (attv * inv).astype(BF16)
    b1_ref[0:n1, :] = gl1
    b2_ref[0:n2, :] = gl2
    t1 = dl1.T
    a_parts = _split3(t1[0:1, 0:DH])
    b_parts = _split3(t1[0:1, DH:2 * DH])
    b1_ref[n1:n1 + 16, :] = _coded([a_parts[0], b_parts[0], a_parts[1], b_parts[1], a_parts[2], b_parts[2]])
    b2_ref[n2:n2 + 16, :] = _coded(list(_split3(dl2.T[0:1, :])))
    b1_ref[n1 + 16:, :] = q1[...]
    b2_ref[n2 + 16:, :] = q2[...]


def _bwd2_kernel(q0, k0, v0, g0, att, w, mine, theirs, q1, k1p, v1p, q2, k2a, v2a, k2b, v2b,
                 gq_ref, dk0_ref, dv0_ref,
                 t_s, u_s, dq0s, dq1s, dq2s, outs):
    n2 = dq2s.shape[0]
    _, _, gl0, dl0, gl1, dl1, gl2, dl2 = _level_grads(g0, att, w, mine, theirs, t_s, u_s)
    q0v = q0[...]
    k0v = k0[...]
    v0v = v0[...]
    s = _nt(q0v, k0v) * SCALE
    m = s.max(-1, keepdims=True)
    e = jnp.exp(s - m)
    p = e.astype(BF16)
    ds = (e * (_nt(gl0, v0v) - dl0)).astype(BF16)
    dq0s[...] = _nn(ds, k0v) * SCALE
    dk0_ref[...] = _tn(ds, q0v) * SCALE
    dv0_ref[...] = _tn(p, gl0)

    kv = k1p[...]
    s = _nt(q1[...], kv) * SCALE
    m = s.max(-1, keepdims=True)
    e = jnp.exp(s - m)
    ds = (e * (_nt(gl1, v1p[...]) - dl1[:, 0:1])).astype(BF16)
    dq1s[...] = _nn(ds, kv) * SCALE

    qv = q2[...]
    ka = k2a[...]
    kb = k2b[...]
    sa = _nt(qv, ka) * SCALE
    sb = _nt(qv, kb) * SCALE
    m = jnp.maximum(sa.max(-1, keepdims=True), sb.max(-1, keepdims=True))
    ea = jnp.exp(sa - m)
    eb = jnp.exp(sb - m)
    d2c = dl2[:, 0:1]
    dsa = (ea * (_nt(gl2, v2a[...]) - d2c)).astype(BF16)
    dsb = (eb * (_nt(gl2, v2b[...]) - d2c)).astype(BF16)
    dq2s[...] = (_nn(dsa, ka) + _nn(dsb, kb)) * SCALE

    for j in range(4):
        r0 = pl.ds(j, n2, stride=4)
        r1 = pl.ds(j >> 1, n2, stride=2)
        outs[r0, :] = dq0s[r0, :] + dq1s[r1, :] * 0.5 + dq2s[...] * 0.25
    gq_ref[...] = outs[...].astype(BF16)


def _own_kernel(k1o, v1o, k1p, b1p, k2o, v2o, b2a, b2b, dk0, dv0,
                gk_ref, gv_ref, wide, dk1s, dv1s, dk2s, dv2s, outk, outv):
    n1 = dk1s.shape[0]
    n2 = dk2s.shape[0]
    qv = b1p[n1 + 16:, :]
    gv = b1p[0:n1, :]
    x = b1p[n1:n1 + 16, :].astype(F32)
    d_row = jnp.concatenate([(x[0:1] + x[2:3]) + x[4:5], (x[1:2] + x[3:4]) + x[5:6]], axis=1)
    st = _nt(k1o[...], qv) * SCALE
    m = st.max(0, keepdims=True)
    e = jnp.exp(st - m)
    p = e.astype(BF16)
    ds = (e * (_nt(v1o[...], gv) - d_row)).astype(BF16)
    dk1s[...] = _nn(ds, qv) * SCALE
    dv1s[...] = _nn(p, gv)

    wide[...] = k1p[...].astype(F32)
    ks = ((wide[pl.ds(0, n2, stride=2), :] + wide[pl.ds(1, n2, stride=2), :]) * 0.5).astype(BF16)
    ko = k2o[...]
    vo = v2o[...]
    dks = []
    dvs = []
    for b_ref in (b2a, b2b):
        qv = b_ref[n2 + 16:, :]
        gv = b_ref[0:n2, :]
        x = b_ref[n2:n2 + 16, :].astype(F32)
        d_row = (x[0:1] + x[1:2]) + x[2:3]
        so = _nt(ko, qv) * SCALE
        ss = _nt(ks, qv) * SCALE
        m = jnp.maximum(so.max(0, keepdims=True), ss.max(0, keepdims=True))
        e = jnp.exp(so - m)
        p = e.astype(BF16)
        ds = (e * (_nt(vo, gv) - d_row)).astype(BF16)
        dks.append(_nn(ds, qv))
        dvs.append(_nn(p, gv))
    dk2s[...] = (dks[0] + dks[1]) * SCALE
    dv2s[...] = dvs[0] + dvs[1]

    for j in range(4):
        r0 = pl.ds(j, n2, stride=4)
        r1 = pl.ds(j >> 1, n2, stride=2)
        outk[r0, :] = dk0[r0, :] + dk1s[r1, :] * 0.5 + dk2s[...] * 0.25
        outv[r0, :] = dv0[r0, :] + dv1s[r1, :] * 0.5 + dv2s[...] * 0.25
    gk_ref[...] = outk[...].astype(BF16)
    gv_ref[...] = outv[...].astype(BF16)


def _cols(rows):
    return pl.BlockSpec((rows, DH), lambda h: (0, h))


def _stacked(rows, index):
    return pl.BlockSpec((None, rows, DH), lambda h: (index, 0, h))


def _per_head(rows, width):
    return pl.BlockSpec((None, rows, width), lambda h: (h, 0, 0))


def _whole(rows, width):
    return pl.BlockSpec((rows, width), lambda h: (0, 0))


def _params():
    return pltpu.CompilerParams(dimension_semantics=("arbitrary",))


def _full3(rows, width):
    return pl.BlockSpec((2, rows, width), lambda h: (0, 0, 0))


def _two(rows):
    return pl.BlockSpec((2, rows, DH), lambda h: (0, 0, h))


def shards(queries, key_states, value_states, out_grad):
    n0, width = queries.shape
    heads = width // DH
    n1 = n0 // 2
    n2 = n0 // 4
    q0, k0, v0, g0 = queries, key_states, value_states, out_grad
    s1, q1, s2, q2 = pl.pallas_call(
        _halve_kernel,
        grid=(1,),
        in_specs=[_whole(n0, width), _whole(n0, width), _whole(n0, width)],
        out_specs=[_full3(n1, width), _whole(n1, width), _full3(n2, width), _whole(n2, width)],
        out_shape=[
            jax.ShapeDtypeStruct((2, n1, width), BF16),
            jax.ShapeDtypeStruct((n1, width), BF16),
            jax.ShapeDtypeStruct((2, n2, width), BF16),
            jax.ShapeDtypeStruct((n2, width), BF16),
        ],
        scratch_shapes=[pltpu.VMEM((n0, DH), F32), pltpu.VMEM((n1, DH), F32)],
        compiler_params=_params(),
    )(q0, k0, v0)
    r1 = from_partner(s1, 1)
    r2a = from_partner(s2, 2)
    r2b = from_partner(s2, 3)

    a0, ms0 = pl.pallas_call(
        _fwd0_kernel,
        grid=(heads,),
        in_specs=[_cols(n0), _cols(n0), _cols(n0)],
        out_specs=[_cols(n0), _per_head(n0, DH)],
        out_shape=[
            jax.ShapeDtypeStruct((n0, width), F32),
            jax.ShapeDtypeStruct((heads, n0, DH), F32),
        ],
        compiler_params=_params(),
    )(q0, k0, v0)

    att, w, sums = pl.pallas_call(
        _fwd12_kernel,
        grid=(heads,),
        in_specs=[
            _cols(n0), _per_head(n0, DH), _cols(n0),
            _cols(n1), _stacked(n1, 0), _stacked(n1, 1),
            _cols(n2), _stacked(n2, 0), _stacked(n2, 1), _stacked(n2, 0), _stacked(n2, 1),
        ],
        out_specs=[_cols(n0), _per_head(n0, DH), _whole(n0, DH)],
        out_shape=[
            jax.ShapeDtypeStruct((n0, width), BF16),
            jax.ShapeDtypeStruct((heads, n0, DH), F32),
            jax.ShapeDtypeStruct((n0, DH), F32),
        ],
        scratch_shapes=[pltpu.VMEM((n, DH), F32) for n in (n1, n1, n1, n2, n2, n2, n0, n0)],
        compiler_params=_params(),
    )(a0, ms0, g0, q1, r1, r1, q2, r2a, r2a, r2b, r2b)

    assert width * lax.axis_size("head") == 2 * 4 * DH
    other = lax.ppermute(sums, "head", [(0, 1), (1, 0)])

    norm, b1, b2 = pl.pallas_call(
        _bwd1_kernel,
        grid=(heads,),
        in_specs=[_cols(n0), _cols(n0), _per_head(n0, DH), _whole(n0, DH), _whole(n0, DH), _cols(n1), _cols(n2)],
        out_specs=[_cols(n0), _cols(2 * n1 + 16), _cols(2 * n2 + 16)],
        out_shape=[
            jax.ShapeDtypeStruct((n0, width), BF16),
            jax.ShapeDtypeStruct((2 * n1 + 16, width), BF16),
            jax.ShapeDtypeStruct((2 * n2 + 16, width), BF16),
        ],
        scratch_shapes=[pltpu.VMEM((n0, DH), F32), pltpu.VMEM((n0, DH), F32)],
        compiler_params=_params(),
    )(g0, att, w, sums, other, q1, q2)
    b1p = from_partner(b1, 1)
    b2a = from_partner(b2, 2)
    b2b = from_partner(b2, 3)

    gq, dk0, dv0 = pl.pallas_call(
        _bwd2_kernel,
        grid=(heads,),
        in_specs=[
            _cols(n0), _cols(n0), _cols(n0), _cols(n0), _cols(n0), _per_head(n0, DH),
            _whole(n0, DH), _whole(n0, DH),
            _cols(n1), _stacked(n1, 0), _stacked(n1, 1),
            _cols(n2), _stacked(n2, 0), _stacked(n2, 1), _stacked(n2, 0), _stacked(n2, 1),
        ],
        out_specs=[_cols(n0), _cols(n0), _cols(n0)],
        out_shape=[
            jax.ShapeDtypeStruct((n0, width), BF16),
            jax.ShapeDtypeStruct((n0, width), F32),
            jax.ShapeDtypeStruct((n0, width), F32),
        ],
        scratch_shapes=[pltpu.VMEM((n, DH), F32) for n in (n0, n0, n0, n1, n2, n0)],
        compiler_params=_params(),
    )(q0, k0, v0, g0, att, w, sums, other, q1, r1, r1, q2, r2a, r2a, r2b, r2b)

    gk, gv = pl.pallas_call(
        _own_kernel,
        grid=(heads,),
        in_specs=[
            _stacked(n1, 0), _stacked(n1, 1), _stacked(n1, 0), _cols(2 * n1 + 16),
            _stacked(n2, 0), _stacked(n2, 1), _cols(2 * n2 + 16), _cols(2 * n2 + 16),
            _cols(n0), _cols(n0),
        ],
        out_specs=[_cols(n0), _cols(n0)],
        out_shape=[
            jax.ShapeDtypeStruct((n0, width), BF16),
            jax.ShapeDtypeStruct((n0, width), BF16),
        ],
        scratch_shapes=[pltpu.VMEM((n, DH), F32) for n in (n1, n1, n1, n2, n2, n0, n0)],
        compiler_params=_params(),
    )(s1, s1, r1, b1p, s2, s2, b2a, b2b, dk0, dv0)
    return (norm, gq, gk, gv)


def solution(mesh):
    return jax.shard_map(
        shards,
        mesh=mesh,
        in_specs=(P("seq", "head"), P("seq", "head"), P("seq", "head"), P("seq", "head")),
        out_specs=(P("seq", "head"), P("seq", "head"), P("seq", "head"), P("seq", "head")),
        check_vma=False,
    )
```
